256 devices in a mesh: sec: 2 (over x_hi), gy: 16 (over y, x_lo, core), gz: 8 (over z).
Axes of the slice: x: 4 (x_hi: 2, x_lo: 2; x = x_hi * 2 + x_lo), y: 4, z: 8, core: 2. Of those that a mesh axis runs over, the one named last changes fastest.
Arguments:
- populations: float32 [56, 4, 128, 1024], P('sec', None, 'gy', 'gz'), may hold values from 0 to 1, as said below
- solid_mask: int32 [4, 128, 1024], P(None, 'gy', 'gz'), may hold values 0 or 1
- flow_rates: float32 [15], replicated, may hold values from 0.5 to 1.8
- species_rates: float32 [4], replicated, may hold values from 0.5 to 1.8
- cotangents: float32 [56, 4, 128, 1024], P('sec', None, 'gy', 'gz'), may hold values from -6 to 6
Outputs:
- next_pop: float32 [56, 4, 128, 1024], P('sec', None, 'gy', 'gz')
- pop_grad: float32 [56, 4, 128, 1024], P('sec', None, 'gy', 'gz')
- rate_grad: float32 [19], replicated
The draws below stay inside these ranges and needn't reach their ends.
Inputs may be any that keep to these rules, and one draw needn't show every extreme that they name: `populations`: entries are positive.
All inputs are finite; a program needn't handle non-finite values. No bound on the sum of `solid_mask` on one device may be relied on, other than what follows from the above.
Results may differ from the reference program's by a relative error of at most 0.0003.
Values sent between devices are 32-bit elements; how exact they have to be, the bound alone decides.
No kernel may reach another device: no remote copies, remote signals or barrier semaphores. Data moves between devices by JAX's collectives and lax.ppermute only.
A program may use at most 64 MiB of HBM per device.

```python
import jax
import jax.numpy as jnp
import numpy as np
from jax import lax

SPECIES = 4
CH = 28
NX = 4
NY = 128
NZ = 1024


def draw_populations(key, part):
    flow_weights = np.array([1.0 / 3.0] + [1.0 / 18.0] * 6 + [1.0 / 36.0] * 12 + [1.0 / 36.0] * (CH - 19))
    small = np.array([0.25] + [0.125] * 6)
    levels = 0.5 * (1.0 + np.arange(SPECIES))
    species_weights = (levels[:, None] * small[None, :]).reshape(-1)
    table = jnp.asarray(np.concatenate([flow_weights, species_weights]), jnp.float32).reshape(2 * CH, 1, 1, 1)
    noise = jax.random.uniform(key, (2 * CH, NX, NY, NZ), jnp.float32, -1.0, 1.0)
    return table * (1.0 + 0.3 * noise)


def place_ends(values, stream_key, least, high):
    spot = [jax.random.randint(jax.random.fold_in(stream_key, axis), (), 0, length) for axis, length in enumerate(values.shape)]
    main_axis = values.shape.index(max(values.shape))
    beside = spot[:main_axis] + [(spot[main_axis] + 1) % values.shape[main_axis]] + spot[main_axis + 1:]
    return values.at[tuple(spot)].set(least).at[tuple(beside)].set(high)


def shard_levels(key, extent, cuts, least, top_value):
    factor_of = 1.0
    for dim, blocks in cuts:
        heights = jax.random.uniform(jax.random.fold_in(jax.random.fold_in(key, 6), dim), (blocks,), jnp.float32, least / len(cuts), top_value / len(cuts))
        factor_of = factor_of * jnp.repeat(jnp.exp(heights), extent[dim] // blocks).reshape((-1,) + (1,) * (len(extent) - 1 - dim))
    return factor_of


def bell_draw(stream_key, dims, spread, bound, shards=(), kind=jnp.bfloat16):
    values = jax.random.normal(stream_key, dims, jnp.float32) * spread
    if len(shards) > 0:
        values = shard_levels(stream_key, dims, shards, -0.22, 0.18) * values
    return jnp.clip(values, min=-bound, max=bound).astype(kind)


def setup_inputs(seed: int = 0) -> dict:
    arg_keys = jax.random.split(jax.random.key(seed), 6)
    return {
        "populations": draw_populations(jax.random.fold_in(arg_keys[5], 71), 0),
        "solid_mask": place_ends((jax.random.randint(arg_keys[1], (NX, NY, NZ), 0, 5) < 1).astype(jnp.int32), jax.random.fold_in(arg_keys[1], 1), 0, 1),
        "flow_rates": jnp.clip(jax.random.uniform(arg_keys[2], (15,), jnp.float32, 0.5, 1.8), 0.5, 1.8),
        "species_rates": jnp.clip(jax.random.uniform(arg_keys[3], (SPECIES,), jnp.float32, 0.5, 1.8), 0.5, 1.8),
        "cotangents": bell_draw(arg_keys[4], (2 * CH, NX, NY, NZ), 1.0, 6.0, ((0, 2), (2, 16), (3, 8)), jnp.float32),
    }


def orthonormal_columns(basis):
    result = []
    for column in range(basis.shape[1]):
        vector = basis[:, column] * 1.0
        for repeat in range(2):
            for earlier in result:
                vector = vector - np.sum(earlier * vector) * earlier
        vector = vector / np.sqrt(np.sum(vector * vector))
        result.append(vector)
    return np.stack(result, 1)

def lattice_tables():
    axis_moves = [(1, 0, 0), (-1, 0, 0), (0, 1, 0), (0, -1, 0), (0, 0, 1), (0, 0, -1)]
    edge_moves = []
    for first, second in ((0, 1), (0, 2), (1, 2)):
        for sign_first in (1, -1):
            for sign_second in (1, -1):
                move = [0, 0, 0]
                move[first] = sign_first
                move[second] = sign_second
                edge_moves.append(tuple(move))
    velocity = np.array([(0, 0, 0)] + axis_moves + edge_moves) * 1.0
    weights = np.array([1.0 / 3.0] + [1.0 / 18.0] * 6 + [1.0 / 36.0] * 12)
    opposite = np.array([int(np.argmin(np.abs(velocity + velocity[channel]).sum(1))) for channel in range(19)])
    along_x = velocity[:, 0]
    along_y = velocity[:, 1]
    along_z = velocity[:, 2]
    basis = np.stack([np.ones(19), along_x, along_y, along_z, along_x ** 2, along_y ** 2, along_z ** 2, along_x * along_y, along_y * along_z, along_x * along_z, along_x * along_y ** 2, along_x * along_z ** 2, along_y * along_x ** 2, along_y * along_z ** 2, along_z * along_x ** 2, along_z * along_y ** 2, along_x ** 2 * along_y ** 2, along_x ** 2 * along_z ** 2, along_y ** 2 * along_z ** 2], 1)
    ortho = orthonormal_columns(basis)
    return (velocity, weights, opposite, ortho)

def expand(table, trailing):
    return jnp.asarray(table, jnp.float32).reshape(table.shape + (1,) * trailing)

def collide(flow, species, is_fluid, flow_rates, species_rates):
    velocity, weights, opposite, ortho = lattice_tables()
    trailing = flow.ndim - 1
    highest = lax.Precision.HIGHEST
    rates = jnp.concatenate([jnp.zeros((4,), flow_rates.dtype), flow_rates])
    ortho_table = jnp.asarray(ortho, jnp.float32)
    collision = jnp.dot(ortho_table * rates[None, :], ortho_table.T, precision=highest)
    velocity_table = jnp.asarray(velocity, jnp.float32)
    density = lax.optimization_barrier(jnp.sum(flow, 0))
    momentum = jnp.tensordot(velocity_table.T, flow, 1, precision=highest)
    motion = momentum / density
    projected = jnp.tensordot(velocity_table, motion, 1, precision=highest)
    squared = lax.optimization_barrier(jnp.sum(motion * motion, 0))
    equilibrium = expand(weights, trailing) * density * (1.0 + 3.0 * projected + 4.5 * projected * projected - 1.5 * squared)
    relaxed = flow - jnp.tensordot(collision, flow - equilibrium, 1, precision=highest)
    flow_out = jnp.where(is_fluid, relaxed, flow[opposite])
    grouped = species.reshape((species.shape[0] // 7, 7) + species.shape[1:])
    concentration = lax.optimization_barrier(jnp.sum(grouped, 1))
    small_weights = np.array([0.25] + [0.125] * 6)
    species_eq = expand(small_weights, trailing)[None] * concentration[:, None] * (1.0 + 4.0 * projected[:7])[None]
    rate_shape = species_rates.reshape((-1, 1) + (1,) * trailing)
    relaxed_species = grouped - rate_shape * (grouped - species_eq)
    species_out = jnp.where(is_fluid, relaxed_species, grouped[:, opposite[:7]]).reshape(species.shape)
    return (flow_out, species_out)

def shift_all(field, velocity):
    pieces = []
    for channel in range(field.shape[0]):
        moves = tuple((int(value) for value in velocity[channel]))
        pieces.append(jnp.roll(field[channel], moves, axis=(0, 1, 2)))
    return jnp.stack(pieces)

def reference(populations, solid_mask, flow_rates, species_rates, cotangents):
    velocity, weights, opposite, ortho = lattice_tables()
    section = populations.shape[0] // 2
    flow_pop = populations[:19]
    species_pop = populations[section:]
    cot_flow = cotangents[:19]
    cot_species = cotangents[section:]
    count_flow = 19
    combined_velocity = np.concatenate([velocity, np.tile(velocity[:7], (species_pop.shape[0] // 7, 1))])
    returned = shift_all(jnp.concatenate([cot_flow, cot_species]), -combined_velocity)

    def per_plane(items):
        flow, species, plane_mask, back_flow, back_species = items
        outputs, pullback = jax.vjp(lambda a, b, c, d: collide(a, b, plane_mask == 0, c, d), flow, species, flow_rates, species_rates)
        grads = pullback((back_flow, back_species))
        return outputs + grads
    planes = (jnp.moveaxis(flow_pop, 1, 0), jnp.moveaxis(species_pop, 1, 0), solid_mask, jnp.moveaxis(returned[:count_flow], 1, 0), jnp.moveaxis(returned[count_flow:], 1, 0))
    post_flow, post_species, grad_flow, grad_species, plane_flow_rates, plane_species_rates = lax.map(per_plane, planes)
    post = jnp.concatenate([jnp.moveaxis(post_flow, 0, 1), jnp.moveaxis(post_species, 0, 1)])
    moved = shift_all(post, combined_velocity)
    rate_grad = jnp.concatenate([lax.optimization_barrier(jnp.sum(plane_flow_rates, 0)), lax.optimization_barrier(jnp.sum(plane_species_rates, 0))])
    filler = jnp.zeros((section - 19,) + populations.shape[1:], jnp.float32)
    next_pop = jnp.concatenate([moved[:count_flow], filler, moved[count_flow:]])
    pop_grad = jnp.concatenate([jnp.moveaxis(grad_flow, 0, 1), filler, jnp.moveaxis(grad_species, 0, 1)])
    return (next_pop, pop_grad, rate_grad)
```

```python
import jax
import jax.numpy as jnp
import numpy as np
from jax import lax
from jax.sharding import PartitionSpec as P


def orthonormal_columns(basis):
    result = []
    for column in range(basis.shape[1]):
        vector = basis[:, column] * 1.0
        for repeat in range(2):
            for earlier in result:
                vector = vector - np.sum(earlier * vector) * earlier
        vector = vector / np.sqrt(np.sum(vector * vector))
        result.append(vector)
    return np.stack(result, 1)


def lattice_tables():
    axis_moves = [(1, 0, 0), (-1, 0, 0), (0, 1, 0), (0, -1, 0), (0, 0, 1), (0, 0, -1)]
    edge_moves = []
    for first, second in ((0, 1), (0, 2), (1, 2)):
        for sign_first in (1, -1):
            for sign_second in (1, -1):
                move = [0, 0, 0]
                move[first] = sign_first
                move[second] = sign_second
                edge_moves.append(tuple(move))
    velocity = np.array([(0, 0, 0)] + axis_moves + edge_moves) * 1.0
    weights = np.array([1.0 / 3.0] + [1.0 / 18.0] * 6 + [1.0 / 36.0] * 12)
    opposite = np.array(
        [int(np.argmin(np.abs(velocity + velocity[channel]).sum(1))) for channel in range(19)]
    )
    along_x = velocity[:, 0]
    along_y = velocity[:, 1]
    along_z = velocity[:, 2]
    basis = np.stack(
        [
            np.ones(19),
            along_x,
            along_y,
            along_z,
            along_x**2,
            along_y**2,
            along_z**2,
            along_x * along_y,
            along_y * along_z,
            along_x * along_z,
            along_x * along_y**2,
            along_x * along_z**2,
            along_y * along_x**2,
            along_y * along_z**2,
            along_z * along_x**2,
            along_z * along_y**2,
            along_x**2 * along_y**2,
            along_x**2 * along_z**2,
            along_y**2 * along_z**2,
        ],
        1,
    )
    ortho = orthonormal_columns(basis)
    return (velocity, weights, opposite, ortho)


def column(values):
    return jnp.asarray(np.asarray(values, np.float32).reshape(-1, 1, 1, 1))


def ring(axis, step):
    count = lax.axis_size(axis)
    return [(i, (i + step) % count) for i in range(count)]


def shift_rows(field, moves):
    move_x, move_y, move_z = moves
    size_y, size_z = field.shape[2], field.shape[3]
    low = lax.ppermute(field[:, :, size_y - 1 :, :], "gy", ring("gy", 1))
    high = lax.ppermute(field[:, :, :1, :], "gy", ring("gy", -1))
    from_low = jnp.concatenate([low, field[:, :, : size_y - 1, :]], axis=2)
    from_high = jnp.concatenate([field[:, :, 1:, :], high], axis=2)
    field = jnp.where(move_y > 0, from_low, jnp.where(move_y < 0, from_high, field))
    low = lax.ppermute(field[:, :, :, size_z - 1 :], "gz", ring("gz", 1))
    high = lax.ppermute(field[:, :, :, :1], "gz", ring("gz", -1))
    from_low = jnp.concatenate([low, field[:, :, :, : size_z - 1]], axis=3)
    from_high = jnp.concatenate([field[:, :, :, 1:], high], axis=3)
    field = jnp.where(move_z > 0, from_low, jnp.where(move_z < 0, from_high, field))
    from_low = jnp.roll(field, 1, axis=1)
    from_high = jnp.roll(field, -1, axis=1)
    return jnp.where(move_x > 0, from_low, jnp.where(move_x < 0, from_high, field))


def butterfly_sum(values):
    for axis in ("gy", "gz", "sec"):
        count = lax.axis_size(axis)
        step = 1
        while step < count:
            values = values + lax.ppermute(
                values, axis, [(i, i ^ step) for i in range(count)]
            )
            step *= 2
    return values


def per_device(populations, solid_mask, flow_rates, species_rates, cotangents):
    velocity, weights, opposite, ortho = lattice_tables()
    highest = lax.Precision.HIGHEST
    rows = populations.shape[0]
    groups = rows // 7
    is_flow = lax.axis_index("sec") == 0
    fluid = (solid_mask == 0)[None]

    flow_moves = np.concatenate([velocity, np.zeros((rows - 19, 3))])
    species_moves = np.tile(velocity[:7], (groups, 1))
    moves = [
        jnp.where(is_flow, column(flow_moves[:, d]), column(species_moves[:, d])) for d in range(3)
    ]
    returned = shift_rows(cotangents, [-m for m in moves])

    flow = populations[:19]
    vx, vy, vz = (column(velocity[:, d]) for d in range(3))
    density = jnp.sum(flow, 0)
    own_motion = jnp.stack(
        [jnp.sum(flow * vx, 0), jnp.sum(flow * vy, 0), jnp.sum(flow * vz, 0)]
    ) / density[None]
    sent_motion = lax.ppermute(own_motion, "sec", [(0, 1)])
    motion = jnp.where(is_flow, own_motion, sent_motion)

    small_weights = column([0.25] + [0.125] * 6)
    grouped = populations.reshape((groups, 7) + populations.shape[1:])
    back_species = returned.reshape(grouped.shape)
    species_r = species_rates.reshape((groups, 1, 1, 1, 1))
    concentration = jnp.sum(grouped, 1)
    sx, sy, sz = (column(velocity[:7, d])[None] for d in range(3))
    weighted_back = back_species * small_weights[None]
    species_motion_grad = 4.0 * jnp.sum(
        species_r * concentration[:, None] * jnp.stack(
            [jnp.sum(weighted_back * sx, 1), jnp.sum(weighted_back * sy, 1), jnp.sum(weighted_back * sz, 1)], 1
        ),
        0,
    )
    species_motion_grad = jnp.where(fluid, species_motion_grad, 0.0)
    sent_grad = lax.ppermute(species_motion_grad, "sec", [(1, 0)])

    projected_small = motion[0][None] * sx[0] + motion[1][None] * sy[0] + motion[2][None] * sz[0]
    factor = small_weights * (1.0 + 4.0 * projected_small)
    species_eq = factor[None] * concentration[:, None]
    species_gap = grouped - species_eq
    species_relaxed = grouped - species_r * species_gap
    species_bounce = grouped[:, opposite[:7]]
    species_post = jnp.where(fluid[None], species_relaxed, species_bounce).reshape(populations.shape)
    species_t = jnp.sum(back_species * factor[None], 1)
    species_grad_fluid = (1.0 - species_r) * back_species + species_r * species_t[:, None]
    species_grad = jnp.where(
        fluid[None], species_grad_fluid, back_species[:, opposite[:7]]
    ).reshape(populations.shape)
    species_rate_grad = -jnp.sum(
        jnp.where(fluid[None], back_species * species_gap, 0.0), axis=(1, 2, 3, 4)
    )

    q_table = jnp.asarray(ortho, jnp.float32)
    relax = jnp.concatenate([jnp.zeros((4,), flow_rates.dtype), flow_rates]).reshape(19, 1, 1, 1)
    w = column(weights)
    projected = vx * motion[0][None] + vy * motion[1][None] + vz * motion[2][None]
    squared = jnp.sum(motion * motion, 0)
    poly = w * (1.0 + 3.0 * projected + 4.5 * projected * projected - 1.5 * squared[None])
    equilibrium = density[None] * poly
    moments = jnp.einsum("ji,jxyz->ixyz", q_table, flow - equilibrium, precision=highest)
    flow_relaxed = flow - jnp.einsum("ij,jxyz->ixyz", q_table, relax * moments, precision=highest)
    flow_post = jnp.where(fluid, flow_relaxed, flow[opposite])

    back_flow = returned[:19]
    back_moments = jnp.einsum("ji,jxyz->ixyz", q_table, back_flow, precision=highest)
    through_eq = jnp.einsum("ij,jxyz->ixyz", q_table, relax * back_moments, precision=highest)
    flow_rate_grad = -jnp.sum(
        jnp.where(fluid, back_moments * moments, 0.0)[4:], axis=(1, 2, 3)
    )
    density_grad = jnp.sum(through_eq * poly, 0)
    hw = through_eq * w
    hw_sum = jnp.sum(hw, 0)
    hwp = hw * (3.0 + 9.0 * projected)
    motion_grad = density[None] * (
        jnp.stack([jnp.sum(hwp * vx, 0), jnp.sum(hwp * vy, 0), jnp.sum(hwp * vz, 0)])
        - 3.0 * motion * hw_sum[None]
    )
    motion_grad = jnp.where(fluid, motion_grad + sent_grad, 0.0)
    along = vx * motion_grad[0][None] + vy * motion_grad[1][None] + vz * motion_grad[2][None]
    extra = (along - jnp.sum(motion * motion_grad, 0)[None]) / density[None]
    flow_grad = jnp.where(
        fluid, back_flow - through_eq + density_grad[None] + extra, back_flow[opposite]
    )

    filler = jnp.zeros((rows - 19,) + populations.shape[1:], jnp.float32)
    post = jnp.where(is_flow, jnp.concatenate([flow_post, filler]), species_post)
    grad_rows = jnp.where(is_flow, jnp.concatenate([flow_grad, filler]), species_grad)
    local_rates = jnp.where(
        is_flow,
        jnp.concatenate([flow_rate_grad, jnp.zeros((groups,), jnp.float32)]),
        jnp.concatenate([jnp.zeros((15,), jnp.float32), species_rate_grad]),
    )
    rate_grad = butterfly_sum(local_rates)
    moved = shift_rows(post, moves)
    moved = jnp.where(is_flow, jnp.concatenate([moved[:19], filler]), moved)
    return (moved, grad_rows, rate_grad)


def solution(mesh):
    placed = (P("sec", None, "gy", "gz"), P(None, "gy", "gz"), P(), P(), P("sec", None, "gy", "gz"))
    return jax.shard_map(
        per_device,
        mesh=mesh,
        in_specs=placed,
        out_specs=(P("sec", None, "gy", "gz"), P("sec", None, "gy", "gz"), P()),
        check_vma=False,
    )
```

```python
import jax
import jax.numpy as jnp
import numpy as np
from jax import lax
from jax.sharding import PartitionSpec as P


def orthonormal_columns(basis):
    result = []
    for column in range(basis.shape[1]):
        vector = basis[:, column] * 1.0
        for repeat in range(2):
            for earlier in result:
                vector = vector - np.sum(earlier * vector) * earlier
        vector = vector / np.sqrt(np.sum(vector * vector))
        result.append(vector)
    return np.stack(result, 1)


def lattice_tables():
    axis_moves = [(1, 0, 0), (-1, 0, 0), (0, 1, 0), (0, -1, 0), (0, 0, 1), (0, 0, -1)]
    edge_moves = []
    for first, second in ((0, 1), (0, 2), (1, 2)):
        for sign_first in (1, -1):
            for sign_second in (1, -1):
                move = [0, 0, 0]
                move[first] = sign_first
                move[second] = sign_second
                edge_moves.append(tuple(move))
    velocity = np.array([(0, 0, 0)] + axis_moves + edge_moves) * 1.0
    weights = np.array([1.0 / 3.0] + [1.0 / 18.0] * 6 + [1.0 / 36.0] * 12)
    opposite = np.array(
        [int(np.argmin(np.abs(velocity + velocity[channel]).sum(1))) for channel in range(19)]
    )
    along_x = velocity[:, 0]
    along_y = velocity[:, 1]
    along_z = velocity[:, 2]
    basis = np.stack(
        [
            np.ones(19),
            along_x,
            along_y,
            along_z,
            along_x**2,
            along_y**2,
            along_z**2,
            along_x * along_y,
            along_y * along_z,
            along_x * along_z,
            along_x * along_y**2,
            along_x * along_z**2,
            along_y * along_x**2,
            along_y * along_z**2,
            along_z * along_x**2,
            along_z * along_y**2,
            along_x**2 * along_y**2,
            along_x**2 * along_z**2,
            along_y**2 * along_z**2,
        ],
        1,
    )
    ortho = orthonormal_columns(basis)
    return (velocity, weights, opposite, ortho)


def column(values):
    return jnp.asarray(np.asarray(values, np.float32).reshape(-1, 1, 1, 1))


def ring(axis, step):
    count = lax.axis_size(axis)
    return [(i, (i + step) % count) for i in range(count)]


def shift_rows(field, moves):
    move_x, move_y, move_z = moves
    size_y, size_z = field.shape[2], field.shape[3]
    low = lax.ppermute(field[:, :, size_y - 1 :, :], "gy", ring("gy", 1))
    high = lax.ppermute(field[:, :, :1, :], "gy", ring("gy", -1))
    from_low = jnp.concatenate([low, field[:, :, : size_y - 1, :]], axis=2)
    from_high = jnp.concatenate([field[:, :, 1:, :], high], axis=2)
    field = jnp.where(move_y > 0, from_low, jnp.where(move_y < 0, from_high, field))
    low = lax.ppermute(field[:, :, :, size_z - 1 :], "gz", ring("gz", 1))
    high = lax.ppermute(field[:, :, :, :1], "gz", ring("gz", -1))
    from_low = jnp.concatenate([low, field[:, :, :, : size_z - 1]], axis=3)
    from_high = jnp.concatenate([field[:, :, :, 1:], high], axis=3)
    field = jnp.where(move_z > 0, from_low, jnp.where(move_z < 0, from_high, field))
    from_low = jnp.roll(field, 1, axis=1)
    from_high = jnp.roll(field, -1, axis=1)
    return jnp.where(move_x > 0, from_low, jnp.where(move_x < 0, from_high, field))


def butterfly_sum(values, axes):
    for axis in axes:
        count = lax.axis_size(axis)
        step = 1
        while step < count:
            values = values + lax.ppermute(
                values, axis, [(i, i ^ step) for i in range(count)]
            )
            step *= 2
    return values


def per_device(populations, solid_mask, flow_rates, species_rates, cotangents):
    velocity, weights, opposite, ortho = lattice_tables()
    highest = lax.Precision.HIGHEST
    rows = populations.shape[0]
    groups = rows // 7
    is_flow = lax.axis_index("sec") == 0
    fluid = (solid_mask == 0)[None]

    flow = populations[:19]
    vx, vy, vz = (column(velocity[:, d]) for d in range(3))
    density = jnp.sum(flow, 0)
    own_motion = jnp.stack(
        [jnp.sum(flow * vx, 0), jnp.sum(flow * vy, 0), jnp.sum(flow * vz, 0)]
    ) / density[None]
    sent_motion = lax.ppermute(own_motion, "sec", [(0, 1)])
    motion = jnp.where(is_flow, own_motion, sent_motion)

    small_weights = column([0.25] + [0.125] * 6)
    grouped = populations.reshape((groups, 7) + populations.shape[1:])
    species_r = species_rates.reshape((groups, 1, 1, 1, 1))
    concentration = jnp.sum(grouped, 1)
    sx, sy, sz = (column(velocity[:7, d])[None] for d in range(3))
    projected_small = motion[0][None] * sx[0] + motion[1][None] * sy[0] + motion[2][None] * sz[0]
    factor = small_weights * (1.0 + 4.0 * projected_small)
    species_eq = factor[None] * concentration[:, None]
    species_gap = grouped - species_eq
    species_relaxed = grouped - species_r * species_gap
    species_bounce = grouped[:, opposite[:7]]
    species_post = jnp.where(fluid[None], species_relaxed, species_bounce).reshape(populations.shape)

    q_table = jnp.asarray(ortho, jnp.float32)
    relax = jnp.concatenate([jnp.zeros((4,), flow_rates.dtype), flow_rates]).reshape(19, 1, 1, 1)
    w = column(weights)
    projected = vx * motion[0][None] + vy * motion[1][None] + vz * motion[2][None]
    squared = jnp.sum(motion * motion, 0)
    poly = w * (1.0 + 3.0 * projected + 4.5 * projected * projected - 1.5 * squared[None])
    equilibrium = density[None] * poly
    moments = jnp.einsum("ji,jxyz->ixyz", q_table, flow - equilibrium, precision=highest)
    flow_relaxed = flow - jnp.einsum("ij,jxyz->ixyz", q_table, relax * moments, precision=highest)
    flow_post = jnp.where(fluid, flow_relaxed, flow[opposite])
    filler = jnp.zeros((rows - 19,) + populations.shape[1:], jnp.float32)
    post = jnp.where(is_flow, jnp.concatenate([flow_post, filler]), species_post)

    flow_moves = np.concatenate([velocity, np.zeros((rows - 19, 3))])
    species_moves = np.tile(velocity[:7], (groups, 1))
    both_moves = []
    for d in range(3):
        table = jnp.where(is_flow, column(flow_moves[:, d]), column(species_moves[:, d]))
        both_moves.append(jnp.concatenate([table, -table]))
    both = shift_rows(jnp.concatenate([post, cotangents]), both_moves)
    moved = both[:rows]
    returned = both[rows:]
    moved = jnp.where(is_flow, jnp.concatenate([moved[:19], filler]), moved)

    back_species = returned.reshape(grouped.shape)
    weighted_back = back_species * small_weights[None]
    species_motion_grad = 4.0 * jnp.sum(
        species_r * concentration[:, None] * jnp.stack(
            [jnp.sum(weighted_back * sx, 1), jnp.sum(weighted_back * sy, 1), jnp.sum(weighted_back * sz, 1)], 1
        ),
        0,
    )
    species_motion_grad = jnp.where(fluid, species_motion_grad, 0.0)
    species_t = jnp.sum(back_species * factor[None], 1)
    species_grad_fluid = (1.0 - species_r) * back_species + species_r * species_t[:, None]
    species_grad = jnp.where(
        fluid[None], species_grad_fluid, back_species[:, opposite[:7]]
    ).reshape(populations.shape)
    species_rate_grad = -jnp.sum(
        jnp.where(fluid[None], back_species * species_gap, 0.0), axis=(1, 2, 3, 4)
    )

    back_flow = returned[:19]
    back_moments = jnp.einsum("ji,jxyz->ixyz", q_table, back_flow, precision=highest)
    through_eq = jnp.einsum("ij,jxyz->ixyz", q_table, relax * back_moments, precision=highest)
    flow_rate_grad = -jnp.sum(
        jnp.where(fluid, back_moments * moments, 0.0)[4:], axis=(1, 2, 3)
    )
    density_grad = jnp.sum(through_eq * poly, 0)
    hw = through_eq * w
    hw_sum = jnp.sum(hw, 0)
    hwp = hw * (3.0 + 9.0 * projected)
    motion_grad = density[None] * (
        jnp.stack([jnp.sum(hwp * vx, 0), jnp.sum(hwp * vy, 0), jnp.sum(hwp * vz, 0)])
        - 3.0 * motion * hw_sum[None]
    )

    local_rates = jnp.where(
        is_flow,
        jnp.concatenate([flow_rate_grad, jnp.zeros((groups,), jnp.float32)]),
        jnp.concatenate([jnp.zeros((15,), jnp.float32), species_rate_grad]),
    )
    partial_rates = butterfly_sum(local_rates, ("gy", "gz"))
    plane = populations.shape[1:]
    rate_plane = jnp.zeros(plane, jnp.float32).at[0, 0, : partial_rates.shape[0]].set(partial_rates)
    payload = jnp.concatenate([species_motion_grad, rate_plane[None]])
    other = lax.ppermute(payload, "sec", [(0, 1), (1, 0)])
    rate_grad = partial_rates + other[3, 0, 0, : partial_rates.shape[0]]

    motion_grad = jnp.where(fluid, motion_grad + other[:3], 0.0)
    along = vx * motion_grad[0][None] + vy * motion_grad[1][None] + vz * motion_grad[2][None]
    extra = (along - jnp.sum(motion * motion_grad, 0)[None]) / density[None]
    flow_grad = jnp.where(
        fluid, back_flow - through_eq + density_grad[None] + extra, back_flow[opposite]
    )
    grad_rows = jnp.where(is_flow, jnp.concatenate([flow_grad, filler]), species_grad)
    return (moved, grad_rows, rate_grad)


def solution(mesh):
    placed = (P("sec", None, "gy", "gz"), P(None, "gy", "gz"), P(), P(), P("sec", None, "gy", "gz"))
    return jax.shard_map(
        per_device,
        mesh=mesh,
        in_specs=placed,
        out_specs=(P("sec", None, "gy", "gz"), P("sec", None, "gy", "gz"), P()),
        check_vma=False,
    )
```

```python
import jax
import jax.numpy as jnp
import numpy as np
from jax import lax
from jax.sharding import PartitionSpec as P


def orthonormal_columns(basis):
    result = []
    for column in range(basis.shape[1]):
        vector = basis[:, column] * 1.0
        for repeat in range(2):
            for earlier in result:
                vector = vector - np.sum(earlier * vector) * earlier
        vector = vector / np.sqrt(np.sum(vector * vector))
        result.append(vector)
    return np.stack(result, 1)


def lattice_tables():
    axis_moves = [(1, 0, 0), (-1, 0, 0), (0, 1, 0), (0, -1, 0), (0, 0, 1), (0, 0, -1)]
    edge_moves = []
    for first, second in ((0, 1), (0, 2), (1, 2)):
        for sign_first in (1, -1):
            for sign_second in (1, -1):
                move = [0, 0, 0]
                move[first] = sign_first
                move[second] = sign_second
                edge_moves.append(tuple(move))
    velocity = np.array([(0, 0, 0)] + axis_moves + edge_moves) * 1.0
    weights = np.array([1.0 / 3.0] + [1.0 / 18.0] * 6 + [1.0 / 36.0] * 12)
    opposite = np.array(
        [int(np.argmin(np.abs(velocity + velocity[channel]).sum(1))) for channel in range(19)]
    )
    along_x = velocity[:, 0]
    along_y = velocity[:, 1]
    along_z = velocity[:, 2]
    basis = np.stack(
        [
            np.ones(19),
            along_x,
            along_y,
            along_z,
            along_x**2,
            along_y**2,
            along_z**2,
            along_x * along_y,
            along_y * along_z,
            along_x * along_z,
            along_x * along_y**2,
            along_x * along_z**2,
            along_y * along_x**2,
            along_y * along_z**2,
            along_z * along_x**2,
            along_z * along_y**2,
            along_x**2 * along_y**2,
            along_x**2 * along_z**2,
            along_y**2 * along_z**2,
        ],
        1,
    )
    ortho = orthonormal_columns(basis)
    return (velocity, weights, opposite, ortho)


def column(values):
    return jnp.asarray(np.asarray(values, np.float32).reshape(-1, 1, 1, 1))


def ring(axis, step):
    count = lax.axis_size(axis)
    return [(i, (i + step) % count) for i in range(count)]


def shift_rows(field, moves):
    move_x, move_y, move_z = moves
    size_y, size_z = field.shape[2], field.shape[3]
    low = lax.ppermute(field[:, :, size_y - 1 :, :], "gy", ring("gy", 1))
    high = lax.ppermute(field[:, :, :1, :], "gy", ring("gy", -1))
    from_low = jnp.concatenate([low, field[:, :, : size_y - 1, :]], axis=2)
    from_high = jnp.concatenate([field[:, :, 1:, :], high], axis=2)
    field = jnp.where(move_y > 0, from_low, jnp.where(move_y < 0, from_high, field))
    low = lax.ppermute(field[:, :, :, size_z - 1], "gz", ring("gz", 1))
    high = lax.ppermute(field[:, :, :, 0], "gz", ring("gz", -1))
    lane = lax.broadcasted_iota(jnp.int32, field.shape, 3)
    from_low = jnp.where(lane == 0, low[..., None], jnp.roll(field, 1, axis=3))
    from_high = jnp.where(lane == size_z - 1, high[..., None], jnp.roll(field, -1, axis=3))
    field = jnp.where(move_z > 0, from_low, jnp.where(move_z < 0, from_high, field))
    from_low = jnp.roll(field, 1, axis=1)
    from_high = jnp.roll(field, -1, axis=1)
    return jnp.where(move_x > 0, from_low, jnp.where(move_x < 0, from_high, field))


def reverse_pairs(rows, opposite):
    return jnp.concatenate([rows[int(o) : int(o) + 1] for o in opposite])


def butterfly_sum(values, axes, deferred):
    round_index = 0
    for axis in axes:
        count = lax.axis_size(axis)
        step = 1
        while step < count:
            values = values + lax.ppermute(
                values, axis, [(i, i ^ step) for i in range(count)]
            )
            step *= 2
            if round_index < len(deferred):
                values = deferred[round_index](values)
            round_index += 1
    return values


def per_device(populations, solid_mask, flow_rates, species_rates, cotangents):
    velocity, weights, opposite, ortho = lattice_tables()
    highest = lax.Precision.HIGHEST
    rows = populations.shape[0]
    groups = rows // 7
    is_flow = lax.axis_index("sec") == 0
    fluid = (solid_mask == 0)[None]

    flow = populations[:19]
    vx, vy, vz = (column(velocity[:, d]) for d in range(3))
    density = jnp.sum(flow, 0)
    own_motion = jnp.stack(
        [jnp.sum(flow * vx, 0), jnp.sum(flow * vy, 0), jnp.sum(flow * vz, 0)]
    ) / density[None]
    sent_motion = lax.ppermute(own_motion, "sec", [(0, 1)])
    motion = jnp.where(is_flow, own_motion, sent_motion)

    small_weights = column([0.25] + [0.125] * 6)
    grouped = populations.reshape((groups, 7) + populations.shape[1:])
    species_r = species_rates.reshape((groups, 1, 1, 1, 1))
    concentration = jnp.sum(grouped, 1)
    sx, sy, sz = (column(velocity[:7, d])[None] for d in range(3))
    projected_small = motion[0][None] * sx[0] + motion[1][None] * sy[0] + motion[2][None] * sz[0]
    factor = small_weights * (1.0 + 4.0 * projected_small)
    species_eq = factor[None] * concentration[:, None]
    species_gap = grouped - species_eq
    species_relaxed = grouped - species_r * species_gap
    species_bounce = jnp.swapaxes(reverse_pairs(jnp.swapaxes(grouped, 0, 1), opposite[:7]), 0, 1)
    species_post = jnp.where(fluid[None], species_relaxed, species_bounce).reshape(populations.shape)

    q_table = jnp.asarray(ortho, jnp.float32)
    relax = jnp.concatenate([jnp.zeros((4,), flow_rates.dtype), flow_rates]).reshape(19, 1, 1, 1)
    w = column(weights)
    projected = vx * motion[0][None] + vy * motion[1][None] + vz * motion[2][None]
    squared = jnp.sum(motion * motion, 0)
    poly = w * (1.0 + 3.0 * projected + 4.5 * projected * projected - 1.5 * squared[None])
    equilibrium = density[None] * poly
    moments = jnp.einsum("ji,jxyz->ixyz", q_table, flow - equilibrium, precision=highest)
    flow_relaxed = flow - jnp.einsum("ij,jxyz->ixyz", q_table, relax * moments, precision=highest)
    flow_post = jnp.where(fluid, flow_relaxed, reverse_pairs(flow, opposite))
    filler = jnp.zeros((rows - 19,) + populations.shape[1:], jnp.float32)
    post = jnp.where(is_flow, jnp.concatenate([flow_post, filler]), species_post)

    flow_moves = np.concatenate([velocity, np.zeros((rows - 19, 3))])
    species_moves = np.tile(velocity[:7], (groups, 1))
    both_moves = []
    for d in range(3):
        table = jnp.where(is_flow, column(flow_moves[:, d]), column(species_moves[:, d]))
        both_moves.append(jnp.concatenate([table, -table]))
    both = shift_rows(jnp.concatenate([post, cotangents]), both_moves)
    moved = both[:rows]
    returned = both[rows:]
    moved = jnp.where(is_flow, jnp.concatenate([moved[:19], filler]), moved)

    back_species = returned.reshape(grouped.shape)
    back_flow = returned[:19]
    species_rate_grad = -jnp.sum(
        jnp.where(fluid[None], back_species * species_gap, 0.0), axis=(1, 2, 3, 4)
    )
    back_moments = jnp.einsum("ji,jxyz->ixyz", q_table, back_flow, precision=highest)
    flow_rate_grad = -jnp.sum(
        jnp.where(fluid, back_moments * moments, 0.0)[4:], axis=(1, 2, 3)
    )
    local_rates = jnp.where(
        is_flow,
        jnp.concatenate([flow_rate_grad, jnp.zeros((groups,), jnp.float32)]),
        jnp.concatenate([jnp.zeros((15,), jnp.float32), species_rate_grad]),
    )

    later = {}

    def flow_adjoint(values):
        values, (back_flow_, back_moments_) = lax.optimization_barrier(
            (values, (back_flow, back_moments))
        )
        through_eq = jnp.einsum("ij,jxyz->ixyz", q_table, relax * back_moments_, precision=highest)
        density_grad = jnp.sum(through_eq * poly, 0)
        hw = through_eq * w
        hw_sum = jnp.sum(hw, 0)
        hwp = hw * (3.0 + 9.0 * projected)
        later["motion_grad"] = density[None] * (
            jnp.stack([jnp.sum(hwp * vx, 0), jnp.sum(hwp * vy, 0), jnp.sum(hwp * vz, 0)])
            - 3.0 * motion * hw_sum[None]
        )
        later["flow_base"] = back_flow_ - through_eq + density_grad[None]
        return values

    def species_adjoint(values):
        values, back = lax.optimization_barrier((values, back_species))
        weighted_back = back * small_weights[None]
        species_motion_grad = 4.0 * jnp.sum(
            species_r * concentration[:, None] * jnp.stack(
                [jnp.sum(weighted_back * sx, 1), jnp.sum(weighted_back * sy, 1), jnp.sum(weighted_back * sz, 1)], 1
            ),
            0,
        )
        later["species_motion_grad"] = jnp.where(fluid, species_motion_grad, 0.0)
        species_t = jnp.sum(back * factor[None], 1)
        species_grad_fluid = (1.0 - species_r) * back + species_r * species_t[:, None]
        bounced = jnp.swapaxes(reverse_pairs(jnp.swapaxes(back, 0, 1), opposite[:7]), 0, 1)
        later["species_grad"] = jnp.where(fluid[None], species_grad_fluid, bounced).reshape(
            populations.shape
        )
        return values

    partial_rates = butterfly_sum(local_rates, ("gy", "gz"), [flow_adjoint, species_adjoint])
    plane = populations.shape[1:]
    rate_plane = jnp.zeros(plane, jnp.float32).at[0, 0, : partial_rates.shape[0]].set(partial_rates)
    payload = jnp.concatenate([later["species_motion_grad"], rate_plane[None]])
    other = lax.ppermute(payload, "sec", [(0, 1), (1, 0)])
    rate_grad = partial_rates + other[3, 0, 0, : partial_rates.shape[0]]

    motion_grad = jnp.where(fluid, later["motion_grad"] + other[:3], 0.0)
    along = vx * motion_grad[0][None] + vy * motion_grad[1][None] + vz * motion_grad[2][None]
    extra = (along - jnp.sum(motion * motion_grad, 0)[None]) / density[None]
    flow_grad = jnp.where(
        fluid, later["flow_base"] + extra, reverse_pairs(back_flow, opposite)
    )
    grad_rows = jnp.where(is_flow, jnp.concatenate([flow_grad, filler]), later["species_grad"])
    return (moved, grad_rows, rate_grad)


def solution(mesh):
    placed = (P("sec", None, "gy", "gz"), P(None, "gy", "gz"), P(), P(), P("sec", None, "gy", "gz"))
    return jax.shard_map(
        per_device,
        mesh=mesh,
        in_specs=placed,
        out_specs=(P("sec", None, "gy", "gz"), P("sec", None, "gy", "gz"), P()),
        check_vma=False,
    )
```

```python
import jax
import jax.numpy as jnp
import numpy as np
from jax import lax
from jax.sharding import PartitionSpec as P


def orthonormal_columns(basis):
    result = []
    for column in range(basis.shape[1]):
        vector = basis[:, column] * 1.0
        for repeat in range(2):
            for earlier in result:
                vector = vector - np.sum(earlier * vector) * earlier
        vector = vector / np.sqrt(np.sum(vector * vector))
        result.append(vector)
    return np.stack(result, 1)


def lattice_tables():
    axis_moves = [(1, 0, 0), (-1, 0, 0), (0, 1, 0), (0, -1, 0), (0, 0, 1), (0, 0, -1)]
    edge_moves = []
    for first, second in ((0, 1), (0, 2), (1, 2)):
        for sign_first in (1, -1):
            for sign_second in (1, -1):
                move = [0, 0, 0]
                move[first] = sign_first
                move[second] = sign_second
                edge_moves.append(tuple(move))
    velocity = np.array([(0, 0, 0)] + axis_moves + edge_moves) * 1.0
    weights = np.array([1.0 / 3.0] + [1.0 / 18.0] * 6 + [1.0 / 36.0] * 12)
    opposite = np.array(
        [int(np.argmin(np.abs(velocity + velocity[channel]).sum(1))) for channel in range(19)]
    )
    along_x = velocity[:, 0]
    along_y = velocity[:, 1]
    along_z = velocity[:, 2]
    basis = np.stack(
        [
            np.ones(19),
            along_x,
            along_y,
            along_z,
            along_x**2,
            along_y**2,
            along_z**2,
            along_x * along_y,
            along_y * along_z,
            along_x * along_z,
            along_x * along_y**2,
            along_x * along_z**2,
            along_y * along_x**2,
            along_y * along_z**2,
            along_z * along_x**2,
            along_z * along_y**2,
            along_x**2 * along_y**2,
            along_x**2 * along_z**2,
            along_y**2 * along_z**2,
        ],
        1,
    )
    ortho = orthonormal_columns(basis)
    return (velocity, weights, opposite, ortho)


def column(values):
    return jnp.asarray(np.asarray(values, np.float32).reshape(-1, 1, 1, 1))


def ring(axis, step):
    count = lax.axis_size(axis)
    return [(i, (i + step) % count) for i in range(count)]


def shift_rows(field, moves):
    move_x, move_y, move_z = moves
    size_y, size_z = field.shape[2], field.shape[3]
    low = lax.ppermute(field[:, :, size_y - 1 :, :], "gy", ring("gy", 1))
    high = lax.ppermute(field[:, :, :1, :], "gy", ring("gy", -1))
    from_low = jnp.concatenate([low, field[:, :, : size_y - 1, :]], axis=2)
    from_high = jnp.concatenate([field[:, :, 1:, :], high], axis=2)
    field = jnp.where(move_y > 0, from_low, jnp.where(move_y < 0, from_high, field))
    low = lax.ppermute(field[:, :, :, size_z - 1], "gz", ring("gz", 1))
    high = lax.ppermute(field[:, :, :, 0], "gz", ring("gz", -1))
    lane = lax.broadcasted_iota(jnp.int32, field.shape, 3)
    from_low = jnp.where(lane == 0, low[..., None], jnp.roll(field, 1, axis=3))
    from_high = jnp.where(lane == size_z - 1, high[..., None], jnp.roll(field, -1, axis=3))
    field = jnp.where(move_z > 0, from_low, jnp.where(move_z < 0, from_high, field))
    from_low = jnp.roll(field, 1, axis=1)
    from_high = jnp.roll(field, -1, axis=1)
    return jnp.where(move_x > 0, from_low, jnp.where(move_x < 0, from_high, field))


def reverse_pairs(rows, opposite):
    return jnp.concatenate([rows[int(o) : int(o) + 1] for o in opposite])


NEAR_HALVES = {4: [3, 2, 1, 0], 8: [6, 7, 4, 5, 2, 3, 0, 1]}


def butterfly_rounds(count, inner):
    rounds = []
    step = 1
    while step < inner:
        rounds.append([i ^ step for i in range(count)])
        step *= 2
    ring_size = count // inner
    step = 1
    while step < ring_size:
        if 2 * step == ring_size and ring_size in NEAR_HALVES:
            mirror = NEAR_HALVES[ring_size]
        else:
            mirror = [j ^ step for j in range(ring_size)]
        rounds.append([mirror[i // inner] * inner + i % inner for i in range(count)])
        step *= 2
    return rounds


def butterfly_sum(values, axes, deferred):
    round_index = 0
    for axis, inner in axes:
        for targets in butterfly_rounds(lax.axis_size(axis), inner):
            values = values + lax.ppermute(values, axis, list(enumerate(targets)))
            if round_index < len(deferred):
                values = deferred[round_index](values)
            round_index += 1
    return values


def mix(table, field, scale=None):
    rows = [field[j] if scale is None else field[j] * scale[j] for j in range(table.shape[0])]
    out = []
    for k in range(table.shape[1]):
        total = None
        for j in range(table.shape[0]):
            weight = float(table[j, k])
            if abs(weight) < 1e-12:
                continue
            term = rows[j] * weight
            total = term if total is None else total + term
        out.append(total if total is not None else jnp.zeros_like(rows[0]))
    return jnp.stack(out)


def per_device(populations, solid_mask, flow_rates, species_rates, cotangents):
    velocity, weights, opposite, ortho = lattice_tables()
    rows = populations.shape[0]
    groups = rows // 7
    is_flow = lax.axis_index("sec") == 0
    fluid = (solid_mask == 0)[None]

    flow = populations[:19]
    vx, vy, vz = (column(velocity[:, d]) for d in range(3))
    density = jnp.sum(flow, 0)
    own_motion = jnp.stack(
        [jnp.sum(flow * vx, 0), jnp.sum(flow * vy, 0), jnp.sum(flow * vz, 0)]
    ) / density[None]
    sent_motion = lax.ppermute(own_motion, "sec", [(0, 1)])
    motion = jnp.where(is_flow, own_motion, sent_motion)

    small_weights = column([0.25] + [0.125] * 6)
    grouped = populations.reshape((groups, 7) + populations.shape[1:])
    species_r = species_rates.reshape((groups, 1, 1, 1, 1))
    concentration = jnp.sum(grouped, 1)
    sx, sy, sz = (column(velocity[:7, d])[None] for d in range(3))
    projected_small = motion[0][None] * sx[0] + motion[1][None] * sy[0] + motion[2][None] * sz[0]
    factor = small_weights * (1.0 + 4.0 * projected_small)
    species_eq = factor[None] * concentration[:, None]
    species_gap = grouped - species_eq
    species_relaxed = grouped - species_r * species_gap
    species_bounce = jnp.swapaxes(reverse_pairs(jnp.swapaxes(grouped, 0, 1), opposite[:7]), 0, 1)
    species_post = jnp.where(fluid[None], species_relaxed, species_bounce).reshape(populations.shape)

    relax_scalars = [0.0] * 4 + [flow_rates[k] for k in range(flow_rates.shape[0])]
    w = column(weights)
    projected = vx * motion[0][None] + vy * motion[1][None] + vz * motion[2][None]
    squared = jnp.sum(motion * motion, 0)
    poly = w * (1.0 + 3.0 * projected + 4.5 * projected * projected - 1.5 * squared[None])
    equilibrium = density[None] * poly
    moments = mix(ortho, flow - equilibrium)
    flow_relaxed = flow - mix(ortho.T, moments, relax_scalars)
    flow_post = jnp.where(fluid, flow_relaxed, reverse_pairs(flow, opposite))
    filler = jnp.zeros((rows - 19,) + populations.shape[1:], jnp.float32)
    post = jnp.where(is_flow, jnp.concatenate([flow_post, filler]), species_post)

    flow_moves = np.concatenate([velocity, np.zeros((rows - 19, 3))])
    species_moves = np.tile(velocity[:7], (groups, 1))
    both_moves = []
    for d in range(3):
        table = jnp.where(is_flow, column(flow_moves[:, d]), column(species_moves[:, d]))
        both_moves.append(jnp.concatenate([table, -table]))
    both = shift_rows(jnp.concatenate([post, cotangents]), both_moves)
    moved = both[:rows]
    returned = both[rows:]
    moved = jnp.where(is_flow, jnp.concatenate([moved[:19], filler]), moved)

    back_species = returned.reshape(grouped.shape)
    back_flow = returned[:19]
    species_rate_grad = -jnp.sum(
        jnp.where(fluid[None], back_species * species_gap, 0.0), axis=(1, 2, 3, 4)
    )
    back_moments = mix(ortho, back_flow)
    flow_rate_grad = -jnp.sum(
        jnp.where(fluid, back_moments * moments, 0.0)[4:], axis=(1, 2, 3)
    )
    local_rates = jnp.where(
        is_flow,
        jnp.concatenate([flow_rate_grad, jnp.zeros((groups,), jnp.float32)]),
        jnp.concatenate([jnp.zeros((15,), jnp.float32), species_rate_grad]),
    )

    later = {}

    def flow_adjoint(values):
        values, (back_flow_, back_moments_) = lax.optimization_barrier(
            (values, (back_flow, back_moments))
        )
        through_eq = mix(ortho.T, back_moments_, relax_scalars)
        density_grad = jnp.sum(through_eq * poly, 0)
        hw = through_eq * w
        hw_sum = jnp.sum(hw, 0)
        hwp = hw * (3.0 + 9.0 * projected)
        later["motion_grad"] = density[None] * (
            jnp.stack([jnp.sum(hwp * vx, 0), jnp.sum(hwp * vy, 0), jnp.sum(hwp * vz, 0)])
            - 3.0 * motion * hw_sum[None]
        )
        later["flow_base"] = back_flow_ - through_eq + density_grad[None]
        return values

    def species_adjoint(values):
        values, back = lax.optimization_barrier((values, back_species))
        weighted_back = back * small_weights[None]
        species_motion_grad = 4.0 * jnp.sum(
            species_r * concentration[:, None] * jnp.stack(
                [jnp.sum(weighted_back * sx, 1), jnp.sum(weighted_back * sy, 1), jnp.sum(weighted_back * sz, 1)], 1
            ),
            0,
        )
        later["species_motion_grad"] = jnp.where(fluid, species_motion_grad, 0.0)
        species_t = jnp.sum(back * factor[None], 1)
        species_grad_fluid = (1.0 - species_r) * back + species_r * species_t[:, None]
        bounced = jnp.swapaxes(reverse_pairs(jnp.swapaxes(back, 0, 1), opposite[:7]), 0, 1)
        later["species_grad"] = jnp.where(fluid[None], species_grad_fluid, bounced).reshape(
            populations.shape
        )
        return values

    partial_rates = butterfly_sum(local_rates, (("gy", 4), ("gz", 1)), [flow_adjoint, species_adjoint])
    plane = populations.shape[1:]
    rate_plane = jnp.zeros(plane, jnp.float32).at[0, 0, : partial_rates.shape[0]].set(partial_rates)
    payload = jnp.concatenate([later["species_motion_grad"], rate_plane[None]])
    other = lax.ppermute(payload, "sec", [(0, 1), (1, 0)])
    rate_grad = partial_rates + other[3, 0, 0, : partial_rates.shape[0]]

    motion_grad = jnp.where(fluid, later["motion_grad"] + other[:3], 0.0)
    along = vx * motion_grad[0][None] + vy * motion_grad[1][None] + vz * motion_grad[2][None]
    extra = (along - jnp.sum(motion * motion_grad, 0)[None]) / density[None]
    flow_grad = jnp.where(
        fluid, later["flow_base"] + extra, reverse_pairs(back_flow, opposite)
    )
    grad_rows = jnp.where(is_flow, jnp.concatenate([flow_grad, filler]), later["species_grad"])
    return (moved, grad_rows, rate_grad)


def solution(mesh):
    placed = (P("sec", None, "gy", "gz"), P(None, "gy", "gz"), P(), P(), P("sec", None, "gy", "gz"))
    return jax.shard_map(
        per_device,
        mesh=mesh,
        in_specs=placed,
        out_specs=(P("sec", None, "gy", "gz"), P("sec", None, "gy", "gz"), P()),
        check_vma=False,
    )
```

```python
import jax
import jax.numpy as jnp
import numpy as np
from jax import lax
from jax.sharding import PartitionSpec as P


def orthonormal_columns(basis):
    result = []
    for column in range(basis.shape[1]):
        vector = basis[:, column] * 1.0
        for repeat in range(2):
            for earlier in result:
                vector = vector - np.sum(earlier * vector) * earlier
        vector = vector / np.sqrt(np.sum(vector * vector))
        result.append(vector)
    return np.stack(result, 1)


def lattice_tables():
    axis_moves = [(1, 0, 0), (-1, 0, 0), (0, 1, 0), (0, -1, 0), (0, 0, 1), (0, 0, -1)]
    edge_moves = []
    for first, second in ((0, 1), (0, 2), (1, 2)):
        for sign_first in (1, -1):
            for sign_second in (1, -1):
                move = [0, 0, 0]
                move[first] = sign_first
                move[second] = sign_second
                edge_moves.append(tuple(move))
    velocity = np.array([(0, 0, 0)] + axis_moves + edge_moves) * 1.0
    weights = np.array([1.0 / 3.0] + [1.0 / 18.0] * 6 + [1.0 / 36.0] * 12)
    opposite = np.array(
        [int(np.argmin(np.abs(velocity + velocity[channel]).sum(1))) for channel in range(19)]
    )
    along_x = velocity[:, 0]
    along_y = velocity[:, 1]
    along_z = velocity[:, 2]
    basis = np.stack(
        [
            np.ones(19),
            along_x,
            along_y,
            along_z,
            along_x**2,
            along_y**2,
            along_z**2,
            along_x * along_y,
            along_y * along_z,
            along_x * along_z,
            along_x * along_y**2,
            along_x * along_z**2,
            along_y * along_x**2,
            along_y * along_z**2,
            along_z * along_x**2,
            along_z * along_y**2,
            along_x**2 * along_y**2,
            along_x**2 * along_z**2,
            along_y**2 * along_z**2,
        ],
        1,
    )
    ortho = orthonormal_columns(basis)
    return (velocity, weights, opposite, ortho)


def column(values):
    return jnp.asarray(np.asarray(values, np.float32).reshape(-1, 1, 1, 1))


def ring(axis, step):
    count = lax.axis_size(axis)
    return [(i, (i + step) % count) for i in range(count)]


def shift_rows(field, moves):
    move_x, move_y, move_z = moves
    size_y, size_z = field.shape[2], field.shape[3]
    low = lax.ppermute(field[:, :, size_y - 1 :, :], "gy", ring("gy", 1))
    high = lax.ppermute(field[:, :, :1, :], "gy", ring("gy", -1))
    from_low = jnp.concatenate([low, field[:, :, : size_y - 1, :]], axis=2)
    from_high = jnp.concatenate([field[:, :, 1:, :], high], axis=2)
    field = jnp.where(move_y > 0, from_low, jnp.where(move_y < 0, from_high, field))
    low = lax.ppermute(field[:, :, :, size_z - 1], "gz", ring("gz", 1))
    high = lax.ppermute(field[:, :, :, 0], "gz", ring("gz", -1))
    lane = lax.broadcasted_iota(jnp.int32, field.shape, 3)
    from_low = jnp.where(lane == 0, low[..., None], jnp.roll(field, 1, axis=3))
    from_high = jnp.where(lane == size_z - 1, high[..., None], jnp.roll(field, -1, axis=3))
    field = jnp.where(move_z > 0, from_low, jnp.where(move_z < 0, from_high, field))
    from_low = jnp.roll(field, 1, axis=1)
    from_high = jnp.roll(field, -1, axis=1)
    return jnp.where(move_x > 0, from_low, jnp.where(move_x < 0, from_high, field))


def reverse_pairs(rows, opposite):
    return jnp.concatenate([rows[int(o) : int(o) + 1] for o in opposite])


NEAR_HALVES = {4: [3, 2, 1, 0], 8: [6, 7, 4, 5, 2, 3, 0, 1]}


def butterfly_rounds(count, inner):
    rounds = []
    step = 1
    while step < inner:
        rounds.append([i ^ step for i in range(count)])
        step *= 2
    ring_size = count // inner
    step = 1
    while step < ring_size:
        if 2 * step == ring_size and ring_size in NEAR_HALVES:
            mirror = NEAR_HALVES[ring_size]
        else:
            mirror = [j ^ step for j in range(ring_size)]
        rounds.append([mirror[i // inner] * inner + i % inner for i in range(count)])
        step *= 2
    return rounds


def butterfly_sum(values, axes, deferred):
    round_index = 0
    for axis, inner in axes:
        for targets in butterfly_rounds(lax.axis_size(axis), inner):
            values = values + lax.ppermute(values, axis, list(enumerate(targets)))
            if round_index < len(deferred):
                values = deferred[round_index](values)
            round_index += 1
    return values


def per_device(populations, solid_mask, flow_rates, species_rates, cotangents):
    velocity, weights, opposite, ortho = lattice_tables()
    highest = lax.Precision.HIGHEST
    rows = populations.shape[0]
    groups = rows // 7
    is_flow = lax.axis_index("sec") == 0
    fluid = (solid_mask == 0)[None]

    flow = populations[:19]
    vx, vy, vz = (column(velocity[:, d]) for d in range(3))
    density = jnp.sum(flow, 0)
    own_motion = jnp.stack(
        [jnp.sum(flow * vx, 0), jnp.sum(flow * vy, 0), jnp.sum(flow * vz, 0)]
    ) / density[None]
    sent_motion = lax.ppermute(own_motion, "sec", [(0, 1)])
    motion = jnp.where(is_flow, own_motion, sent_motion)

    small_weights = column([0.25] + [0.125] * 6)
    grouped = populations.reshape((groups, 7) + populations.shape[1:])
    species_r = species_rates.reshape((groups, 1, 1, 1, 1))
    concentration = jnp.sum(grouped, 1)
    sx, sy, sz = (column(velocity[:7, d])[None] for d in range(3))
    projected_small = motion[0][None] * sx[0] + motion[1][None] * sy[0] + motion[2][None] * sz[0]
    factor = small_weights * (1.0 + 4.0 * projected_small)
    species_eq = factor[None] * concentration[:, None]
    species_gap = grouped - species_eq
    species_relaxed = grouped - species_r * species_gap
    species_bounce = jnp.swapaxes(reverse_pairs(jnp.swapaxes(grouped, 0, 1), opposite[:7]), 0, 1)
    species_post = jnp.where(fluid[None], species_relaxed, species_bounce).reshape(populations.shape)

    q_table = jnp.asarray(ortho, jnp.float32)
    relax = jnp.concatenate([jnp.zeros((4,), flow_rates.dtype), flow_rates]).reshape(19, 1, 1, 1)
    w = column(weights)
    projected = vx * motion[0][None] + vy * motion[1][None] + vz * motion[2][None]
    squared = jnp.sum(motion * motion, 0)
    poly = w * (1.0 + 3.0 * projected + 4.5 * projected * projected - 1.5 * squared[None])
    equilibrium = density[None] * poly
    moments = jnp.einsum("ji,jxyz->ixyz", q_table, flow - equilibrium, precision=highest)
    flow_relaxed = flow - jnp.einsum("ij,jxyz->ixyz", q_table, relax * moments, precision=highest)
    flow_post = jnp.where(fluid, flow_relaxed, reverse_pairs(flow, opposite))
    filler = jnp.zeros((rows - 19,) + populations.shape[1:], jnp.float32)
    post = jnp.where(is_flow, jnp.concatenate([flow_post, filler]), species_post)

    flow_moves = np.concatenate([velocity, np.zeros((rows - 19, 3))])
    species_moves = np.tile(velocity[:7], (groups, 1))
    both_moves = []
    for d in range(3):
        table = jnp.where(is_flow, column(flow_moves[:, d]), column(species_moves[:, d]))
        both_moves.append(jnp.concatenate([table, -table]))
    both = shift_rows(jnp.concatenate([post, cotangents]), both_moves)
    moved = both[:rows]
    returned = both[rows:]
    moved = jnp.where(is_flow, jnp.concatenate([moved[:19], filler]), moved)

    back_species = returned.reshape(grouped.shape)
    back_flow = returned[:19]
    species_rate_grad = -jnp.sum(
        jnp.where(fluid[None], back_species * species_gap, 0.0), axis=(1, 2, 3, 4)
    )
    back_moments = jnp.einsum("ji,jxyz->ixyz", q_table, back_flow, precision=highest)
    flow_rate_grad = -jnp.sum(
        jnp.where(fluid, back_moments * moments, 0.0)[4:], axis=(1, 2, 3)
    )
    local_rates = jnp.where(
        is_flow,
        jnp.concatenate([flow_rate_grad, jnp.zeros((groups,), jnp.float32)]),
        jnp.concatenate([jnp.zeros((15,), jnp.float32), species_rate_grad]),
    )

    later = {}

    def flow_adjoint(values):
        values, (back_flow_, back_moments_) = lax.optimization_barrier(
            (values, (back_flow, back_moments))
        )
        through_eq = jnp.einsum("ij,jxyz->ixyz", q_table, relax * back_moments_, precision=highest)
        density_grad = jnp.sum(through_eq * poly, 0)
        hw = through_eq * w
        hw_sum = jnp.sum(hw, 0)
        hwp = hw * (3.0 + 9.0 * projected)
        later["motion_grad"] = density[None] * (
            jnp.stack([jnp.sum(hwp * vx, 0), jnp.sum(hwp * vy, 0), jnp.sum(hwp * vz, 0)])
            - 3.0 * motion * hw_sum[None]
        )
        later["flow_base"] = back_flow_ - through_eq + density_grad[None]
        return values

    def species_adjoint(values):
        values, back = lax.optimization_barrier((values, back_species))
        weighted_back = back * small_weights[None]
        species_motion_grad = 4.0 * jnp.sum(
            species_r * concentration[:, None] * jnp.stack(
                [jnp.sum(weighted_back * sx, 1), jnp.sum(weighted_back * sy, 1), jnp.sum(weighted_back * sz, 1)], 1
            ),
            0,
        )
        later["species_motion_grad"] = jnp.where(fluid, species_motion_grad, 0.0)
        species_t = jnp.sum(back * factor[None], 1)
        species_grad_fluid = (1.0 - species_r) * back + species_r * species_t[:, None]
        bounced = jnp.swapaxes(reverse_pairs(jnp.swapaxes(back, 0, 1), opposite[:7]), 0, 1)
        later["species_grad"] = jnp.where(fluid[None], species_grad_fluid, bounced).reshape(
            populations.shape
        )
        return values

    partial_rates = butterfly_sum(local_rates, (("gy", 4), ("gz", 1)), [flow_adjoint, species_adjoint])
    plane = populations.shape[1:]
    rate_plane = jnp.zeros(plane, jnp.float32).at[0, 0, : partial_rates.shape[0]].set(partial_rates)
    payload = jnp.concatenate([later["species_motion_grad"], rate_plane[None]])
    other = lax.ppermute(payload, "sec", [(0, 1), (1, 0)])
    rate_grad = partial_rates + other[3, 0, 0, : partial_rates.shape[0]]

    motion_grad = jnp.where(fluid, later["motion_grad"] + other[:3], 0.0)
    along = vx * motion_grad[0][None] + vy * motion_grad[1][None] + vz * motion_grad[2][None]
    extra = (along - jnp.sum(motion * motion_grad, 0)[None]) / density[None]
    flow_grad = jnp.where(
        fluid, later["flow_base"] + extra, reverse_pairs(back_flow, opposite)
    )
    grad_rows = jnp.where(is_flow, jnp.concatenate([flow_grad, filler]), later["species_grad"])
    return (moved, grad_rows, rate_grad)


def solution(mesh):
    placed = (P("sec", None, "gy", "gz"), P(None, "gy", "gz"), P(), P(), P("sec", None, "gy", "gz"))
    return jax.shard_map(
        per_device,
        mesh=mesh,
        in_specs=placed,
        out_specs=(P("sec", None, "gy", "gz"), P("sec", None, "gy", "gz"), P()),
        check_vma=False,
    )
```

```python
import jax
import jax.numpy as jnp
import numpy as np
from jax import lax
from jax.sharding import PartitionSpec as P


def orthonormal_columns(basis):
    result = []
    for column in range(basis.shape[1]):
        vector = basis[:, column] * 1.0
        for repeat in range(2):
            for earlier in result:
                vector = vector - np.sum(earlier * vector) * earlier
        vector = vector / np.sqrt(np.sum(vector * vector))
        result.append(vector)
    return np.stack(result, 1)


def lattice_tables():
    axis_moves = [(1, 0, 0), (-1, 0, 0), (0, 1, 0), (0, -1, 0), (0, 0, 1), (0, 0, -1)]
    edge_moves = []
    for first, second in ((0, 1), (0, 2), (1, 2)):
        for sign_first in (1, -1):
            for sign_second in (1, -1):
                move = [0, 0, 0]
                move[first] = sign_first
                move[second] = sign_second
                edge_moves.append(tuple(move))
    velocity = np.array([(0, 0, 0)] + axis_moves + edge_moves) * 1.0
    weights = np.array([1.0 / 3.0] + [1.0 / 18.0] * 6 + [1.0 / 36.0] * 12)
    opposite = np.array(
        [int(np.argmin(np.abs(velocity + velocity[channel]).sum(1))) for channel in range(19)]
    )
    along_x = velocity[:, 0]
    along_y = velocity[:, 1]
    along_z = velocity[:, 2]
    basis = np.stack(
        [
            np.ones(19),
            along_x,
            along_y,
            along_z,
            along_x**2,
            along_y**2,
            along_z**2,
            along_x * along_y,
            along_y * along_z,
            along_x * along_z,
            along_x * along_y**2,
            along_x * along_z**2,
            along_y * along_x**2,
            along_y * along_z**2,
            along_z * along_x**2,
            along_z * along_y**2,
            along_x**2 * along_y**2,
            along_x**2 * along_z**2,
            along_y**2 * along_z**2,
        ],
        1,
    )
    ortho = orthonormal_columns(basis)
    return (velocity, weights, opposite, ortho)


def column(values):
    return jnp.asarray(np.asarray(values, np.float32).reshape(-1, 1, 1, 1))


def ring(axis, step):
    count = lax.axis_size(axis)
    return [(i, (i + step) % count) for i in range(count)]


def shift_rows(field, moves):
    move_x, move_y, move_z = moves
    size_y, size_z = field.shape[2], field.shape[3]
    low = lax.ppermute(field[:, :, size_y - 1 :, :], "gy", ring("gy", 1))
    high = lax.ppermute(field[:, :, :1, :], "gy", ring("gy", -1))
    from_low = jnp.concatenate([low, field[:, :, : size_y - 1, :]], axis=2)
    from_high = jnp.concatenate([field[:, :, 1:, :], high], axis=2)
    field = jnp.where(move_y > 0, from_low, jnp.where(move_y < 0, from_high, field))
    low = lax.ppermute(field[:, :, :, size_z - 1], "gz", ring("gz", 1))
    high = lax.ppermute(field[:, :, :, 0], "gz", ring("gz", -1))
    lane = lax.broadcasted_iota(jnp.int32, field.shape, 3)
    from_low = jnp.where(lane == 0, low[..., None], jnp.roll(field, 1, axis=3))
    from_high = jnp.where(lane == size_z - 1, high[..., None], jnp.roll(field, -1, axis=3))
    field = jnp.where(move_z > 0, from_low, jnp.where(move_z < 0, from_high, field))
    from_low = jnp.roll(field, 1, axis=1)
    from_high = jnp.roll(field, -1, axis=1)
    return jnp.where(move_x > 0, from_low, jnp.where(move_x < 0, from_high, field))


def reverse_pairs(rows, opposite):
    return jnp.concatenate([rows[int(o) : int(o) + 1] for o in opposite])


NEAR_HALVES = {4: [3, 2, 1, 0], 8: [6, 7, 4, 5, 2, 3, 0, 1]}


def butterfly_rounds(count, inner):
    rounds = []
    step = 1
    while step < inner:
        rounds.append([i ^ step for i in range(count)])
        step *= 2
    ring_size = count // inner
    step = 1
    while step < ring_size:
        if 2 * step == ring_size and ring_size in NEAR_HALVES:
            mirror = NEAR_HALVES[ring_size]
        else:
            mirror = [j ^ step for j in range(ring_size)]
        rounds.append([mirror[i // inner] * inner + i % inner for i in range(count)])
        step *= 2
    return rounds


def butterfly_sum(values, axes, deferred):
    round_index = 0
    for axis, inner in axes:
        for targets in butterfly_rounds(lax.axis_size(axis), inner):
            values = values + lax.ppermute(values, axis, list(enumerate(targets)))
            if round_index < len(deferred):
                values = deferred[round_index](values)
            round_index += 1
    return values


def per_device(populations, solid_mask, flow_rates, species_rates, cotangents):
    velocity, weights, opposite, ortho = lattice_tables()
    highest = lax.Precision.HIGHEST
    rows = populations.shape[0]
    groups = rows // 7
    is_flow = lax.axis_index("sec") == 0
    fluid = (solid_mask == 0)[None]

    flow = populations[:19]
    vx, vy, vz = (column(velocity[:, d]) for d in range(3))
    density = jnp.sum(flow, 0)
    own_motion = jnp.stack(
        [jnp.sum(flow * vx, 0), jnp.sum(flow * vy, 0), jnp.sum(flow * vz, 0)]
    ) / density[None]
    sent_motion = lax.ppermute(own_motion, "sec", [(0, 1)])

    small_weights = column([0.25] + [0.125] * 6)
    grouped = populations.reshape((groups, 7) + populations.shape[1:])
    species_r = species_rates.reshape((groups, 1, 1, 1, 1))
    concentration = jnp.sum(grouped, 1)
    sx, sy, sz = (column(velocity[:7, d])[None] for d in range(3))
    projected_small = (
        sent_motion[0][None] * sx[0] + sent_motion[1][None] * sy[0] + sent_motion[2][None] * sz[0]
    )
    factor = small_weights * (1.0 + 4.0 * projected_small)
    species_eq = factor[None] * concentration[:, None]
    species_gap = grouped - species_eq
    species_relaxed = grouped - species_r * species_gap
    species_bounce = jnp.swapaxes(reverse_pairs(jnp.swapaxes(grouped, 0, 1), opposite[:7]), 0, 1)
    species_post = jnp.where(fluid[None], species_relaxed, species_bounce).reshape(populations.shape)

    q_table = jnp.asarray(ortho, jnp.float32)
    relax = jnp.concatenate([jnp.zeros((4,), flow_rates.dtype), flow_rates]).reshape(19, 1, 1, 1)
    w = column(weights)
    projected = vx * own_motion[0][None] + vy * own_motion[1][None] + vz * own_motion[2][None]
    squared = jnp.sum(own_motion * own_motion, 0)
    poly = w * (1.0 + 3.0 * projected + 4.5 * projected * projected - 1.5 * squared[None])
    equilibrium = density[None] * poly
    moments = jnp.einsum("ji,jxyz->ixyz", q_table, flow - equilibrium, precision=highest)
    flow_relaxed = flow - jnp.einsum("ij,jxyz->ixyz", q_table, relax * moments, precision=highest)
    flow_post = jnp.where(fluid, flow_relaxed, reverse_pairs(flow, opposite))
    filler = jnp.zeros((rows - 19,) + populations.shape[1:], jnp.float32)

    flow_moves = np.concatenate([velocity, np.zeros((rows - 19, 3))])
    species_moves = np.tile(velocity[:7], (groups, 1))
    both_moves = []
    species_post_moves = []
    for d in range(3):
        table = jnp.where(is_flow, column(flow_moves[:, d]), column(species_moves[:, d]))
        both_moves.append(jnp.concatenate([column(flow_moves[:, d]), -table]))
        species_post_moves.append(column(species_moves[:, d]))
    first = jnp.concatenate([jnp.concatenate([flow_post, filler]), cotangents])
    both = shift_rows(first, both_moves)
    returned = both[rows:]
    back_species = returned.reshape(grouped.shape)
    back_flow = returned[:19]
    species_rate_grad = -jnp.sum(
        jnp.where(fluid[None], back_species * species_gap, 0.0), axis=(1, 2, 3, 4)
    )
    back_moments = jnp.einsum("ji,jxyz->ixyz", q_table, back_flow, precision=highest)
    flow_rate_grad = -jnp.sum(
        jnp.where(fluid, back_moments * moments, 0.0)[4:], axis=(1, 2, 3)
    )
    local_rates = jnp.where(
        is_flow,
        jnp.concatenate([flow_rate_grad, jnp.zeros((groups,), jnp.float32)]),
        jnp.concatenate([jnp.zeros((15,), jnp.float32), species_rate_grad]),
    )

    later = {}

    def flow_adjoint(values):
        values, (back_flow_, back_moments_) = lax.optimization_barrier(
            (values, (back_flow, back_moments))
        )
        through_eq = jnp.einsum("ij,jxyz->ixyz", q_table, relax * back_moments_, precision=highest)
        density_grad = jnp.sum(through_eq * poly, 0)
        hw = through_eq * w
        hw_sum = jnp.sum(hw, 0)
        hwp = hw * (3.0 + 9.0 * projected)
        later["motion_grad"] = density[None] * (
            jnp.stack([jnp.sum(hwp * vx, 0), jnp.sum(hwp * vy, 0), jnp.sum(hwp * vz, 0)])
            - 3.0 * own_motion * hw_sum[None]
        )
        later["flow_base"] = back_flow_ - through_eq + density_grad[None]
        return values

    def species_adjoint(values):
        values, back = lax.optimization_barrier((values, back_species))
        weighted_back = back * small_weights[None]
        species_motion_grad = 4.0 * jnp.sum(
            species_r * concentration[:, None] * jnp.stack(
                [jnp.sum(weighted_back * sx, 1), jnp.sum(weighted_back * sy, 1), jnp.sum(weighted_back * sz, 1)], 1
            ),
            0,
        )
        later["species_motion_grad"] = jnp.where(fluid, species_motion_grad, 0.0)
        species_t = jnp.sum(back * factor[None], 1)
        species_grad_fluid = (1.0 - species_r) * back + species_r * species_t[:, None]
        bounced = jnp.swapaxes(reverse_pairs(jnp.swapaxes(back, 0, 1), opposite[:7]), 0, 1)
        later["species_grad"] = jnp.where(fluid[None], species_grad_fluid, bounced).reshape(
            populations.shape
        )
        return values

    def species_passing(values):
        values, species_post_ = lax.optimization_barrier((values, species_post))
        later["species_moved"] = shift_rows(species_post_, species_post_moves)
        return values

    partial_rates = butterfly_sum(
        local_rates, (("gy", 4), ("gz", 1)), [species_passing, flow_adjoint, species_adjoint]
    )
    moved = jnp.where(is_flow, both[:rows], later["species_moved"])
    plane = populations.shape[1:]
    rate_plane = jnp.zeros(plane, jnp.float32).at[0, 0, : partial_rates.shape[0]].set(partial_rates)
    payload = jnp.concatenate([later["species_motion_grad"], rate_plane[None]])
    other = lax.ppermute(payload, "sec", [(0, 1), (1, 0)])
    rate_grad = partial_rates + other[3, 0, 0, : partial_rates.shape[0]]

    motion_grad = jnp.where(fluid, later["motion_grad"] + other[:3], 0.0)
    along = vx * motion_grad[0][None] + vy * motion_grad[1][None] + vz * motion_grad[2][None]
    extra = (along - jnp.sum(own_motion * motion_grad, 0)[None]) / density[None]
    flow_grad = jnp.where(
        fluid, later["flow_base"] + extra, reverse_pairs(back_flow, opposite)
    )
    grad_rows = jnp.where(is_flow, jnp.concatenate([flow_grad, filler]), later["species_grad"])
    return (moved, grad_rows, rate_grad)


def solution(mesh):
    placed = (P("sec", None, "gy", "gz"), P(None, "gy", "gz"), P(), P(), P("sec", None, "gy", "gz"))
    return jax.shard_map(
        per_device,
        mesh=mesh,
        in_specs=placed,
        out_specs=(P("sec", None, "gy", "gz"), P("sec", None, "gy", "gz"), P()),
        check_vma=False,
    )
```

```python
import jax
import jax.numpy as jnp
import numpy as np
from jax import lax
from jax.sharding import PartitionSpec as P


def orthonormal_columns(basis):
    result = []
    for column in range(basis.shape[1]):
        vector = basis[:, column] * 1.0
        for repeat in range(2):
            for earlier in result:
                vector = vector - np.sum(earlier * vector) * earlier
        vector = vector / np.sqrt(np.sum(vector * vector))
        result.append(vector)
    return np.stack(result, 1)


def lattice_tables():
    axis_moves = [(1, 0, 0), (-1, 0, 0), (0, 1, 0), (0, -1, 0), (0, 0, 1), (0, 0, -1)]
    edge_moves = []
    for first, second in ((0, 1), (0, 2), (1, 2)):
        for sign_first in (1, -1):
            for sign_second in (1, -1):
                move = [0, 0, 0]
                move[first] = sign_first
                move[second] = sign_second
                edge_moves.append(tuple(move))
    velocity = np.array([(0, 0, 0)] + axis_moves + edge_moves) * 1.0
    weights = np.array([1.0 / 3.0] + [1.0 / 18.0] * 6 + [1.0 / 36.0] * 12)
    opposite = np.array(
        [int(np.argmin(np.abs(velocity + velocity[channel]).sum(1))) for channel in range(19)]
    )
    along_x = velocity[:, 0]
    along_y = velocity[:, 1]
    along_z = velocity[:, 2]
    basis = np.stack(
        [
            np.ones(19),
            along_x,
            along_y,
            along_z,
            along_x**2,
            along_y**2,
            along_z**2,
            along_x * along_y,
            along_y * along_z,
            along_x * along_z,
            along_x * along_y**2,
            along_x * along_z**2,
            along_y * along_x**2,
            along_y * along_z**2,
            along_z * along_x**2,
            along_z * along_y**2,
            along_x**2 * along_y**2,
            along_x**2 * along_z**2,
            along_y**2 * along_z**2,
        ],
        1,
    )
    ortho = orthonormal_columns(basis)
    return (velocity, weights, opposite, ortho)


def column(values):
    return jnp.asarray(np.asarray(values, np.float32).reshape(-1, 1, 1, 1))


def ring(axis, step):
    count = lax.axis_size(axis)
    return [(i, (i + step) % count) for i in range(count)]


def shift_y(field, move_y):
    size_y = field.shape[2]
    low = lax.ppermute(field[:, :, size_y - 1 :, :], "gy", ring("gy", 1))
    high = lax.ppermute(field[:, :, :1, :], "gy", ring("gy", -1))
    from_low = jnp.concatenate([low, field[:, :, : size_y - 1, :]], axis=2)
    from_high = jnp.concatenate([field[:, :, 1:, :], high], axis=2)
    return jnp.where(move_y > 0, from_low, jnp.where(move_y < 0, from_high, field))


def shift_zx(field, move_z, move_x):
    size_z = field.shape[3]
    low = lax.ppermute(field[:, :, :, size_z - 1], "gz", ring("gz", 1))
    high = lax.ppermute(field[:, :, :, 0], "gz", ring("gz", -1))
    lane = lax.broadcasted_iota(jnp.int32, field.shape, 3)
    from_low = jnp.where(lane == 0, low[..., None], jnp.roll(field, 1, axis=3))
    from_high = jnp.where(lane == size_z - 1, high[..., None], jnp.roll(field, -1, axis=3))
    field = jnp.where(move_z > 0, from_low, jnp.where(move_z < 0, from_high, field))
    from_low = jnp.roll(field, 1, axis=1)
    from_high = jnp.roll(field, -1, axis=1)
    return jnp.where(move_x > 0, from_low, jnp.where(move_x < 0, from_high, field))


def shift_rows(field, moves):
    return shift_zx(shift_y(field, moves[1]), moves[2], moves[0])


def reverse_pairs(rows, opposite):
    return jnp.concatenate([rows[int(o) : int(o) + 1] for o in opposite])


NEAR_HALVES = {4: [3, 2, 1, 0], 8: [6, 7, 4, 5, 2, 3, 0, 1]}


def butterfly_rounds(count, inner):
    rounds = []
    step = 1
    while step < inner:
        rounds.append([i ^ step for i in range(count)])
        step *= 2
    ring_size = count // inner
    step = 1
    while step < ring_size:
        if 2 * step == ring_size and ring_size in NEAR_HALVES:
            mirror = NEAR_HALVES[ring_size]
        else:
            mirror = [j ^ step for j in range(ring_size)]
        rounds.append([mirror[i // inner] * inner + i % inner for i in range(count)])
        step *= 2
    return rounds


def butterfly_sum(values, axes, deferred):
    round_index = 0
    for axis, inner in axes:
        for targets in butterfly_rounds(lax.axis_size(axis), inner):
            values = values + lax.ppermute(values, axis, list(enumerate(targets)))
            if round_index < len(deferred):
                values = deferred[round_index](values)
            round_index += 1
    return values


def per_device(populations, solid_mask, flow_rates, species_rates, cotangents):
    velocity, weights, opposite, ortho = lattice_tables()
    highest = lax.Precision.HIGHEST
    rows = populations.shape[0]
    groups = rows // 7
    is_flow = lax.axis_index("sec") == 0
    fluid = (solid_mask == 0)[None]

    flow = populations[:19]
    vx, vy, vz = (column(velocity[:, d]) for d in range(3))
    density = jnp.sum(flow, 0)
    own_motion = jnp.stack(
        [jnp.sum(flow * vx, 0), jnp.sum(flow * vy, 0), jnp.sum(flow * vz, 0)]
    ) / density[None]
    sent_motion = lax.ppermute(own_motion, "sec", [(0, 1)])

    small_weights = column([0.25] + [0.125] * 6)
    grouped = populations.reshape((groups, 7) + populations.shape[1:])
    species_r = species_rates.reshape((groups, 1, 1, 1, 1))
    concentration = jnp.sum(grouped, 1)
    sx, sy, sz = (column(velocity[:7, d])[None] for d in range(3))
    projected_small = (
        sent_motion[0][None] * sx[0] + sent_motion[1][None] * sy[0] + sent_motion[2][None] * sz[0]
    )
    factor = small_weights * (1.0 + 4.0 * projected_small)
    species_eq = factor[None] * concentration[:, None]
    species_gap = grouped - species_eq
    species_relaxed = grouped - species_r * species_gap
    species_bounce = jnp.swapaxes(reverse_pairs(jnp.swapaxes(grouped, 0, 1), opposite[:7]), 0, 1)
    species_post = jnp.where(fluid[None], species_relaxed, species_bounce).reshape(populations.shape)

    q_table = jnp.asarray(ortho, jnp.float32)
    relax = jnp.concatenate([jnp.zeros((4,), flow_rates.dtype), flow_rates]).reshape(19, 1, 1, 1)
    w = column(weights)
    projected = vx * own_motion[0][None] + vy * own_motion[1][None] + vz * own_motion[2][None]
    squared = jnp.sum(own_motion * own_motion, 0)
    poly = w * (1.0 + 3.0 * projected + 4.5 * projected * projected - 1.5 * squared[None])
    equilibrium = density[None] * poly
    moments = jnp.einsum("ji,jxyz->ixyz", q_table, flow - equilibrium, precision=highest)
    flow_relaxed = flow - jnp.einsum("ij,jxyz->ixyz", q_table, relax * moments, precision=highest)
    flow_post = jnp.where(fluid, flow_relaxed, reverse_pairs(flow, opposite))
    filler = jnp.zeros((rows - 19,) + populations.shape[1:], jnp.float32)

    flow_moves = np.concatenate([velocity, np.zeros((rows - 19, 3))])
    species_moves = np.tile(velocity[:7], (groups, 1))
    post_moves = [
        jnp.where(is_flow, column(flow_moves[:, d]), column(species_moves[:, d])) for d in range(3)
    ]
    returned = shift_rows(cotangents, [-m for m in post_moves])
    back_species = returned.reshape(grouped.shape)
    back_flow = returned[:19]
    species_rate_grad = -jnp.sum(
        jnp.where(fluid[None], back_species * species_gap, 0.0), axis=(1, 2, 3, 4)
    )
    back_moments = jnp.einsum("ji,jxyz->ixyz", q_table, back_flow, precision=highest)
    flow_rate_grad = -jnp.sum(
        jnp.where(fluid, back_moments * moments, 0.0)[4:], axis=(1, 2, 3)
    )
    local_rates = jnp.where(
        is_flow,
        jnp.concatenate([flow_rate_grad, jnp.zeros((groups,), jnp.float32)]),
        jnp.concatenate([jnp.zeros((15,), jnp.float32), species_rate_grad]),
    )

    later = {}

    def flow_adjoint(values):
        values, (back_flow_, back_moments_) = lax.optimization_barrier(
            (values, (back_flow, back_moments))
        )
        through_eq = jnp.einsum("ij,jxyz->ixyz", q_table, relax * back_moments_, precision=highest)
        density_grad = jnp.sum(through_eq * poly, 0)
        hw = through_eq * w
        hw_sum = jnp.sum(hw, 0)
        hwp = hw * (3.0 + 9.0 * projected)
        later["motion_grad"] = density[None] * (
            jnp.stack([jnp.sum(hwp * vx, 0), jnp.sum(hwp * vy, 0), jnp.sum(hwp * vz, 0)])
            - 3.0 * own_motion * hw_sum[None]
        )
        later["flow_base"] = back_flow_ - through_eq + density_grad[None]
        return values

    def species_adjoint(values):
        values, back = lax.optimization_barrier((values, back_species))
        weighted_back = back * small_weights[None]
        species_motion_grad = 4.0 * jnp.sum(
            species_r * concentration[:, None] * jnp.stack(
                [jnp.sum(weighted_back * sx, 1), jnp.sum(weighted_back * sy, 1), jnp.sum(weighted_back * sz, 1)], 1
            ),
            0,
        )
        later["species_motion_grad"] = jnp.where(fluid, species_motion_grad, 0.0)
        species_t = jnp.sum(back * factor[None], 1)
        species_grad_fluid = (1.0 - species_r) * back + species_r * species_t[:, None]
        bounced = jnp.swapaxes(reverse_pairs(jnp.swapaxes(back, 0, 1), opposite[:7]), 0, 1)
        later["species_grad"] = jnp.where(fluid[None], species_grad_fluid, bounced).reshape(
            populations.shape
        )
        return values

    def post_passing_y(values):
        values, post_ = lax.optimization_barrier(
            (values, jnp.where(is_flow, jnp.concatenate([flow_post, filler]), species_post))
        )
        later["post_y"] = shift_y(post_, post_moves[1])
        return values

    def post_passing_zx(values):
        values, post_y = lax.optimization_barrier((values, later["post_y"]))
        later["moved"] = shift_zx(post_y, post_moves[2], post_moves[0])
        return values

    partial_rates = butterfly_sum(
        local_rates, (("gy", 4), ("gz", 1)), [post_passing_y, flow_adjoint, species_adjoint, post_passing_zx]
    )
    moved = jnp.where(is_flow, jnp.concatenate([later["moved"][:19], filler]), later["moved"])
    plane = populations.shape[1:]
    rate_plane = jnp.zeros(plane, jnp.float32).at[0, 0, : partial_rates.shape[0]].set(partial_rates)
    payload = jnp.concatenate([later["species_motion_grad"], rate_plane[None]])
    other = lax.ppermute(payload, "sec", [(0, 1), (1, 0)])
    rate_grad = partial_rates + other[3, 0, 0, : partial_rates.shape[0]]

    motion_grad = jnp.where(fluid, later["motion_grad"] + other[:3], 0.0)
    along = vx * motion_grad[0][None] + vy * motion_grad[1][None] + vz * motion_grad[2][None]
    extra = (along - jnp.sum(own_motion * motion_grad, 0)[None]) / density[None]
    flow_grad = jnp.where(
        fluid, later["flow_base"] + extra, reverse_pairs(back_flow, opposite)
    )
    grad_rows = jnp.where(is_flow, jnp.concatenate([flow_grad, filler]), later["species_grad"])
    return (moved, grad_rows, rate_grad)


def solution(mesh):
    placed = (P("sec", None, "gy", "gz"), P(None, "gy", "gz"), P(), P(), P("sec", None, "gy", "gz"))
    return jax.shard_map(
        per_device,
        mesh=mesh,
        in_specs=placed,
        out_specs=(P("sec", None, "gy", "gz"), P("sec", None, "gy", "gz"), P()),
        check_vma=False,
    )
```

```python
import jax
import jax.numpy as jnp
import numpy as np
from jax import lax
from jax.sharding import PartitionSpec as P


def orthonormal_columns(basis):
    result = []
    for column in range(basis.shape[1]):
        vector = basis[:, column] * 1.0
        for repeat in range(2):
            for earlier in result:
                vector = vector - np.sum(earlier * vector) * earlier
        vector = vector / np.sqrt(np.sum(vector * vector))
        result.append(vector)
    return np.stack(result, 1)


def lattice_tables():
    axis_moves = [(1, 0, 0), (-1, 0, 0), (0, 1, 0), (0, -1, 0), (0, 0, 1), (0, 0, -1)]
    edge_moves = []
    for first, second in ((0, 1), (0, 2), (1, 2)):
        for sign_first in (1, -1):
            for sign_second in (1, -1):
                move = [0, 0, 0]
                move[first] = sign_first
                move[second] = sign_second
                edge_moves.append(tuple(move))
    velocity = np.array([(0, 0, 0)] + axis_moves + edge_moves) * 1.0
    weights = np.array([1.0 / 3.0] + [1.0 / 18.0] * 6 + [1.0 / 36.0] * 12)
    opposite = np.array(
        [int(np.argmin(np.abs(velocity + velocity[channel]).sum(1))) for channel in range(19)]
    )
    along_x = velocity[:, 0]
    along_y = velocity[:, 1]
    along_z = velocity[:, 2]
    basis = np.stack(
        [
            np.ones(19),
            along_x,
            along_y,
            along_z,
            along_x**2,
            along_y**2,
            along_z**2,
            along_x * along_y,
            along_y * along_z,
            along_x * along_z,
            along_x * along_y**2,
            along_x * along_z**2,
            along_y * along_x**2,
            along_y * along_z**2,
            along_z * along_x**2,
            along_z * along_y**2,
            along_x**2 * along_y**2,
            along_x**2 * along_z**2,
            along_y**2 * along_z**2,
        ],
        1,
    )
    ortho = orthonormal_columns(basis)
    return (velocity, weights, opposite, ortho)


def column(values):
    return jnp.asarray(np.asarray(values, np.float32).reshape(-1, 1, 1, 1))


def ring(axis, step):
    count = lax.axis_size(axis)
    return [(i, (i + step) % count) for i in range(count)]


def shift_y(field, move_y):
    size_y = field.shape[2]
    low = lax.ppermute(field[:, :, size_y - 1 :, :], "gy", ring("gy", 1))
    high = lax.ppermute(field[:, :, :1, :], "gy", ring("gy", -1))
    from_low = jnp.concatenate([low, field[:, :, : size_y - 1, :]], axis=2)
    from_high = jnp.concatenate([field[:, :, 1:, :], high], axis=2)
    return jnp.where(move_y > 0, from_low, jnp.where(move_y < 0, from_high, field))


def shift_zx(field, move_z, move_x):
    size_z = field.shape[3]
    low = lax.ppermute(field[:, :, :, size_z - 1], "gz", ring("gz", 1))
    high = lax.ppermute(field[:, :, :, 0], "gz", ring("gz", -1))
    lane = lax.broadcasted_iota(jnp.int32, field.shape, 3)
    from_low = jnp.where(lane == 0, low[..., None], jnp.roll(field, 1, axis=3))
    from_high = jnp.where(lane == size_z - 1, high[..., None], jnp.roll(field, -1, axis=3))
    field = jnp.where(move_z > 0, from_low, jnp.where(move_z < 0, from_high, field))
    from_low = jnp.roll(field, 1, axis=1)
    from_high = jnp.roll(field, -1, axis=1)
    return jnp.where(move_x > 0, from_low, jnp.where(move_x < 0, from_high, field))


def shift_rows(field, moves):
    return shift_zx(shift_y(field, moves[1]), moves[2], moves[0])


def reverse_pairs(rows, opposite):
    return jnp.concatenate([rows[int(o) : int(o) + 1] for o in opposite])


NEAR_HALVES = {4: [3, 2, 1, 0], 8: [6, 7, 4, 5, 2, 3, 0, 1]}


def butterfly_rounds(count, inner):
    rounds = []
    step = 1
    while step < inner:
        rounds.append([i ^ step for i in range(count)])
        step *= 2
    ring_size = count // inner
    step = 1
    while step < ring_size:
        if 2 * step == ring_size and ring_size in NEAR_HALVES:
            mirror = NEAR_HALVES[ring_size]
        else:
            mirror = [j ^ step for j in range(ring_size)]
        rounds.append([mirror[i // inner] * inner + i % inner for i in range(count)])
        step *= 2
    return rounds


def butterfly_sum(values, axes, deferred):
    round_index = 0
    for axis, inner in axes:
        for targets in butterfly_rounds(lax.axis_size(axis), inner):
            values = values + lax.ppermute(values, axis, list(enumerate(targets)))
            if round_index < len(deferred):
                values = deferred[round_index](values)
            round_index += 1
    return values


def per_device(populations, solid_mask, flow_rates, species_rates, cotangents):
    velocity, weights, opposite, ortho = lattice_tables()
    highest = lax.Precision.HIGHEST
    rows = populations.shape[0]
    groups = rows // 7
    is_flow = lax.axis_index("sec") == 0
    fluid = (solid_mask == 0)[None]

    flow = populations[:19]
    vx, vy, vz = (column(velocity[:, d]) for d in range(3))
    density = jnp.sum(flow, 0)
    own_motion = jnp.stack(
        [jnp.sum(flow * vx, 0), jnp.sum(flow * vy, 0), jnp.sum(flow * vz, 0)]
    ) / density[None]
    sent_motion = lax.ppermute(own_motion, "sec", [(0, 1)])

    small_weights = column([0.25] + [0.125] * 6)
    grouped = populations.reshape((groups, 7) + populations.shape[1:])
    species_r = species_rates.reshape((groups, 1, 1, 1, 1))
    concentration = jnp.sum(grouped, 1)
    sx, sy, sz = (column(velocity[:7, d])[None] for d in range(3))
    projected_small = (
        sent_motion[0][None] * sx[0] + sent_motion[1][None] * sy[0] + sent_motion[2][None] * sz[0]
    )
    factor = small_weights * (1.0 + 4.0 * projected_small)
    species_eq = factor[None] * concentration[:, None]
    species_gap = grouped - species_eq

    q_table = jnp.asarray(ortho, jnp.float32)
    relax = jnp.concatenate([jnp.zeros((4,), flow_rates.dtype), flow_rates]).reshape(19, 1, 1, 1)
    w = column(weights)
    projected = vx * own_motion[0][None] + vy * own_motion[1][None] + vz * own_motion[2][None]
    squared = jnp.sum(own_motion * own_motion, 0)
    poly = w * (1.0 + 3.0 * projected + 4.5 * projected * projected - 1.5 * squared[None])
    equilibrium = density[None] * poly
    moments = jnp.einsum("ji,jxyz->ixyz", q_table, flow - equilibrium, precision=highest)
    filler = jnp.zeros((rows - 19,) + populations.shape[1:], jnp.float32)

    flow_moves = np.concatenate([velocity, np.zeros((rows - 19, 3))])
    species_moves = np.tile(velocity[:7], (groups, 1))
    post_moves = [
        jnp.where(is_flow, column(flow_moves[:, d]), column(species_moves[:, d])) for d in range(3)
    ]
    returned = shift_rows(cotangents, [-m for m in post_moves])
    back_species = returned.reshape(grouped.shape)
    back_flow = returned[:19]
    species_rate_grad = -jnp.sum(
        jnp.where(fluid[None], back_species * species_gap, 0.0), axis=(1, 2, 3, 4)
    )
    back_moments = jnp.einsum("ji,jxyz->ixyz", q_table, back_flow, precision=highest)
    flow_rate_grad = -jnp.sum(
        jnp.where(fluid, back_moments * moments, 0.0)[4:], axis=(1, 2, 3)
    )
    local_rates = jnp.where(
        is_flow,
        jnp.concatenate([flow_rate_grad, jnp.zeros((groups,), jnp.float32)]),
        jnp.concatenate([jnp.zeros((15,), jnp.float32), species_rate_grad]),
    )

    later = {}

    def flow_adjoint(values):
        values, (back_flow_, back_moments_) = lax.optimization_barrier(
            (values, (back_flow, back_moments))
        )
        through_eq = jnp.einsum("ij,jxyz->ixyz", q_table, relax * back_moments_, precision=highest)
        density_grad = jnp.sum(through_eq * poly, 0)
        hw = through_eq * w
        hw_sum = jnp.sum(hw, 0)
        hwp = hw * (3.0 + 9.0 * projected)
        later["motion_grad"] = density[None] * (
            jnp.stack([jnp.sum(hwp * vx, 0), jnp.sum(hwp * vy, 0), jnp.sum(hwp * vz, 0)])
            - 3.0 * own_motion * hw_sum[None]
        )
        later["flow_base"] = back_flow_ - through_eq + density_grad[None]
        return values

    def species_adjoint(values):
        values, back = lax.optimization_barrier((values, back_species))
        weighted_back = back * small_weights[None]
        species_motion_grad = 4.0 * jnp.sum(
            species_r * concentration[:, None] * jnp.stack(
                [jnp.sum(weighted_back * sx, 1), jnp.sum(weighted_back * sy, 1), jnp.sum(weighted_back * sz, 1)], 1
            ),
            0,
        )
        later["species_motion_grad"] = jnp.where(fluid, species_motion_grad, 0.0)
        species_t = jnp.sum(back * factor[None], 1)
        species_grad_fluid = (1.0 - species_r) * back + species_r * species_t[:, None]
        bounced = jnp.swapaxes(reverse_pairs(jnp.swapaxes(back, 0, 1), opposite[:7]), 0, 1)
        later["species_grad"] = jnp.where(fluid[None], species_grad_fluid, bounced).reshape(
            populations.shape
        )
        return values

    def post_passing_y(values):
        values, (flow_, grouped_, moments_, species_gap_) = lax.optimization_barrier(
            (values, (flow, grouped, moments, species_gap))
        )
        species_relaxed = grouped_ - species_r * species_gap_
        species_bounce = jnp.swapaxes(reverse_pairs(jnp.swapaxes(grouped_, 0, 1), opposite[:7]), 0, 1)
        species_post = jnp.where(fluid[None], species_relaxed, species_bounce).reshape(populations.shape)
        flow_relaxed = flow_ - jnp.einsum("ij,jxyz->ixyz", q_table, relax * moments_, precision=highest)
        flow_post = jnp.where(fluid, flow_relaxed, reverse_pairs(flow_, opposite))
        post_ = jnp.where(is_flow, jnp.concatenate([flow_post, filler]), species_post)
        later["post_y"] = shift_y(post_, post_moves[1])
        return values

    def post_passing_zx(values):
        values, post_y = lax.optimization_barrier((values, later["post_y"]))
        later["moved"] = shift_zx(post_y, post_moves[2], post_moves[0])
        return values

    partial_rates = butterfly_sum(
        local_rates, (("gy", 4), ("gz", 1)), [post_passing_y, flow_adjoint, species_adjoint, post_passing_zx]
    )
    moved = jnp.where(is_flow, jnp.concatenate([later["moved"][:19], filler]), later["moved"])
    plane = populations.shape[1:]
    rate_plane = jnp.zeros(plane, jnp.float32).at[0, 0, : partial_rates.shape[0]].set(partial_rates)
    payload = jnp.concatenate([later["species_motion_grad"], rate_plane[None]])
    other = lax.ppermute(payload, "sec", [(0, 1), (1, 0)])
    rate_grad = partial_rates + other[3, 0, 0, : partial_rates.shape[0]]

    motion_grad = jnp.where(fluid, later["motion_grad"] + other[:3], 0.0)
    along = vx * motion_grad[0][None] + vy * motion_grad[1][None] + vz * motion_grad[2][None]
    extra = (along - jnp.sum(own_motion * motion_grad, 0)[None]) / density[None]
    flow_grad = jnp.where(
        fluid, later["flow_base"] + extra, reverse_pairs(back_flow, opposite)
    )
    grad_rows = jnp.where(is_flow, jnp.concatenate([flow_grad, filler]), later["species_grad"])
    return (moved, grad_rows, rate_grad)


def solution(mesh):
    placed = (P("sec", None, "gy", "gz"), P(None, "gy", "gz"), P(), P(), P("sec", None, "gy", "gz"))
    return jax.shard_map(
        per_device,
        mesh=mesh,
        in_specs=placed,
        out_specs=(P("sec", None, "gy", "gz"), P("sec", None, "gy", "gz"), P()),
        check_vma=False,
    )
```

```python
import jax
import jax.numpy as jnp
import numpy as np
from jax import lax
from jax.sharding import PartitionSpec as P


def orthonormal_columns(basis):
    result = []
    for column in range(basis.shape[1]):
        vector = basis[:, column] * 1.0
        for repeat in range(2):
            for earlier in result:
                vector = vector - np.sum(earlier * vector) * earlier
        vector = vector / np.sqrt(np.sum(vector * vector))
        result.append(vector)
    return np.stack(result, 1)


def lattice_tables():
    axis_moves = [(1, 0, 0), (-1, 0, 0), (0, 1, 0), (0, -1, 0), (0, 0, 1), (0, 0, -1)]
    edge_moves = []
    for first, second in ((0, 1), (0, 2), (1, 2)):
        for sign_first in (1, -1):
            for sign_second in (1, -1):
                move = [0, 0, 0]
                move[first] = sign_first
                move[second] = sign_second
                edge_moves.append(tuple(move))
    velocity = np.array([(0, 0, 0)] + axis_moves + edge_moves) * 1.0
    weights = np.array([1.0 / 3.0] + [1.0 / 18.0] * 6 + [1.0 / 36.0] * 12)
    opposite = np.array(
        [int(np.argmin(np.abs(velocity + velocity[channel]).sum(1))) for channel in range(19)]
    )
    along_x = velocity[:, 0]
    along_y = velocity[:, 1]
    along_z = velocity[:, 2]
    basis = np.stack(
        [
            np.ones(19),
            along_x,
            along_y,
            along_z,
            along_x**2,
            along_y**2,
            along_z**2,
            along_x * along_y,
            along_y * along_z,
            along_x * along_z,
            along_x * along_y**2,
            along_x * along_z**2,
            along_y * along_x**2,
            along_y * along_z**2,
            along_z * along_x**2,
            along_z * along_y**2,
            along_x**2 * along_y**2,
            along_x**2 * along_z**2,
            along_y**2 * along_z**2,
        ],
        1,
    )
    ortho = orthonormal_columns(basis)
    return (velocity, weights, opposite, ortho)


def column(values):
    return jnp.asarray(np.asarray(values, np.float32).reshape(-1, 1, 1, 1))


def ring(axis, step):
    count = lax.axis_size(axis)
    return [(i, (i + step) % count) for i in range(count)]


def shift_rows(field, moves):
    move_x, move_y, move_z = moves
    size_y, size_z = field.shape[2], field.shape[3]
    low = lax.ppermute(field[:, :, size_y - 1 :, :], "gy", ring("gy", 1))
    high = lax.ppermute(field[:, :, :1, :], "gy", ring("gy", -1))
    from_low = jnp.concatenate([low, field[:, :, : size_y - 1, :]], axis=2)
    from_high = jnp.concatenate([field[:, :, 1:, :], high], axis=2)
    field = jnp.where(move_y > 0, from_low, jnp.where(move_y < 0, from_high, field))
    low = lax.ppermute(field[:, :, :, size_z - 1], "gz", ring("gz", 1))
    high = lax.ppermute(field[:, :, :, 0], "gz", ring("gz", -1))
    lane = lax.broadcasted_iota(jnp.int32, field.shape, 3)
    from_low = jnp.where(lane == 0, low[..., None], jnp.roll(field, 1, axis=3))
    from_high = jnp.where(lane == size_z - 1, high[..., None], jnp.roll(field, -1, axis=3))
    field = jnp.where(move_z > 0, from_low, jnp.where(move_z < 0, from_high, field))
    from_low = jnp.roll(field, 1, axis=1)
    from_high = jnp.roll(field, -1, axis=1)
    return jnp.where(move_x > 0, from_low, jnp.where(move_x < 0, from_high, field))


def reverse_pairs(rows, opposite):
    return jnp.concatenate([rows[int(o) : int(o) + 1] for o in opposite])


NEAR_HALVES = {4: [3, 2, 1, 0], 8: [6, 7, 4, 5, 2, 3, 0, 1]}


def butterfly_rounds(count, inner):
    rounds = []
    step = 1
    while step < inner:
        rounds.append([i ^ step for i in range(count)])
        step *= 2
    ring_size = count // inner
    step = 1
    while step < ring_size:
        if 2 * step == ring_size and ring_size in NEAR_HALVES:
            mirror = NEAR_HALVES[ring_size]
        else:
            mirror = [j ^ step for j in range(ring_size)]
        rounds.append([mirror[i // inner] * inner + i % inner for i in range(count)])
        step *= 2
    return rounds


def butterfly_sum(values, axes, deferred):
    round_index = 0
    for axis, inner in axes:
        for targets in butterfly_rounds(lax.axis_size(axis), inner):
            values = values + lax.ppermute(values, axis, list(enumerate(targets)))
            if round_index < len(deferred):
                values = deferred[round_index](values)
            round_index += 1
    return values


def mix(table, field):
    weights = jnp.asarray(np.asarray(table, np.float32)).reshape(table.shape + (1,) * (field.ndim - 1))
    return jnp.sum(weights * field[:, None], axis=0)


def per_device(populations, solid_mask, flow_rates, species_rates, cotangents):
    velocity, weights, opposite, ortho = lattice_tables()
    rows = populations.shape[0]
    groups = rows // 7
    is_flow = lax.axis_index("sec") == 0
    fluid = (solid_mask == 0)[None]

    flow = populations[:19]
    vx, vy, vz = (column(velocity[:, d]) for d in range(3))
    density = jnp.sum(flow, 0)
    own_motion = jnp.stack(
        [jnp.sum(flow * vx, 0), jnp.sum(flow * vy, 0), jnp.sum(flow * vz, 0)]
    ) / density[None]
    sent_motion = lax.ppermute(own_motion, "sec", [(0, 1)])
    motion = jnp.where(is_flow, own_motion, sent_motion)

    small_weights = column([0.25] + [0.125] * 6)
    grouped = populations.reshape((groups, 7) + populations.shape[1:])
    species_r = species_rates.reshape((groups, 1, 1, 1, 1))
    concentration = jnp.sum(grouped, 1)
    sx, sy, sz = (column(velocity[:7, d])[None] for d in range(3))
    projected_small = motion[0][None] * sx[0] + motion[1][None] * sy[0] + motion[2][None] * sz[0]
    factor = small_weights * (1.0 + 4.0 * projected_small)
    species_eq = factor[None] * concentration[:, None]
    species_gap = grouped - species_eq
    species_relaxed = grouped - species_r * species_gap
    species_bounce = jnp.swapaxes(reverse_pairs(jnp.swapaxes(grouped, 0, 1), opposite[:7]), 0, 1)
    species_post = jnp.where(fluid[None], species_relaxed, species_bounce).reshape(populations.shape)

    relax = jnp.concatenate([jnp.zeros((4,), flow_rates.dtype), flow_rates]).reshape(19, 1, 1, 1)
    w = column(weights)
    projected = vx * motion[0][None] + vy * motion[1][None] + vz * motion[2][None]
    squared = jnp.sum(motion * motion, 0)
    poly = w * (1.0 + 3.0 * projected + 4.5 * projected * projected - 1.5 * squared[None])
    equilibrium = density[None] * poly
    moments = mix(ortho, flow - equilibrium)
    flow_relaxed = flow - mix(ortho.T, relax * moments)
    flow_post = jnp.where(fluid, flow_relaxed, reverse_pairs(flow, opposite))
    filler = jnp.zeros((rows - 19,) + populations.shape[1:], jnp.float32)
    post = jnp.where(is_flow, jnp.concatenate([flow_post, filler]), species_post)

    flow_moves = np.concatenate([velocity, np.zeros((rows - 19, 3))])
    species_moves = np.tile(velocity[:7], (groups, 1))
    both_moves = []
    for d in range(3):
        table = jnp.where(is_flow, column(flow_moves[:, d]), column(species_moves[:, d]))
        both_moves.append(jnp.concatenate([table, -table]))
    both = shift_rows(jnp.concatenate([post, cotangents]), both_moves)
    moved = both[:rows]
    returned = both[rows:]
    moved = jnp.where(is_flow, jnp.concatenate([moved[:19], filler]), moved)

    back_species = returned.reshape(grouped.shape)
    back_flow = returned[:19]
    species_rate_grad = -jnp.sum(
        jnp.where(fluid[None], back_species * species_gap, 0.0), axis=(1, 2, 3, 4)
    )
    back_moments = mix(ortho, back_flow)
    flow_rate_grad = -jnp.sum(
        jnp.where(fluid, back_moments * moments, 0.0)[4:], axis=(1, 2, 3)
    )
    local_rates = jnp.where(
        is_flow,
        jnp.concatenate([flow_rate_grad, jnp.zeros((groups,), jnp.float32)]),
        jnp.concatenate([jnp.zeros((15,), jnp.float32), species_rate_grad]),
    )

    later = {}

    def flow_adjoint(values):
        values, (back_flow_, back_moments_) = lax.optimization_barrier(
            (values, (back_flow, back_moments))
        )
        through_eq = mix(ortho.T, relax * back_moments_)
        density_grad = jnp.sum(through_eq * poly, 0)
        hw = through_eq * w
        hw_sum = jnp.sum(hw, 0)
        hwp = hw * (3.0 + 9.0 * projected)
        later["motion_grad"] = density[None] * (
            jnp.stack([jnp.sum(hwp * vx, 0), jnp.sum(hwp * vy, 0), jnp.sum(hwp * vz, 0)])
            - 3.0 * motion * hw_sum[None]
        )
        later["flow_base"] = back_flow_ - through_eq + density_grad[None]
        return values

    def species_adjoint(values):
        values, back = lax.optimization_barrier((values, back_species))
        weighted_back = back * small_weights[None]
        species_motion_grad = 4.0 * jnp.sum(
            species_r * concentration[:, None] * jnp.stack(
                [jnp.sum(weighted_back * sx, 1), jnp.sum(weighted_back * sy, 1), jnp.sum(weighted_back * sz, 1)], 1
            ),
            0,
        )
        later["species_motion_grad"] = jnp.where(fluid, species_motion_grad, 0.0)
        species_t = jnp.sum(back * factor[None], 1)
        species_grad_fluid = (1.0 - species_r) * back + species_r * species_t[:, None]
        bounced = jnp.swapaxes(reverse_pairs(jnp.swapaxes(back, 0, 1), opposite[:7]), 0, 1)
        later["species_grad"] = jnp.where(fluid[None], species_grad_fluid, bounced).reshape(
            populations.shape
        )
        return values

    partial_rates = butterfly_sum(local_rates, (("gy", 4), ("gz", 1)), [flow_adjoint, species_adjoint])
    plane = populations.shape[1:]
    rate_plane = jnp.zeros(plane, jnp.float32).at[0, 0, : partial_rates.shape[0]].set(partial_rates)
    payload = jnp.concatenate([later["species_motion_grad"], rate_plane[None]])
    other = lax.ppermute(payload, "sec", [(0, 1), (1, 0)])
    rate_grad = partial_rates + other[3, 0, 0, : partial_rates.shape[0]]

    motion_grad = jnp.where(fluid, later["motion_grad"] + other[:3], 0.0)
    along = vx * motion_grad[0][None] + vy * motion_grad[1][None] + vz * motion_grad[2][None]
    extra = (along - jnp.sum(motion * motion_grad, 0)[None]) / density[None]
    flow_grad = jnp.where(
        fluid, later["flow_base"] + extra, reverse_pairs(back_flow, opposite)
    )
    grad_rows = jnp.where(is_flow, jnp.concatenate([flow_grad, filler]), later["species_grad"])
    return (moved, grad_rows, rate_grad)


def solution(mesh):
    placed = (P("sec", None, "gy", "gz"), P(None, "gy", "gz"), P(), P(), P("sec", None, "gy", "gz"))
    return jax.shard_map(
        per_device,
        mesh=mesh,
        in_specs=placed,
        out_specs=(P("sec", None, "gy", "gz"), P("sec", None, "gy", "gz"), P()),
        check_vma=False,
    )
```

```python
import jax
import jax.numpy as jnp
import numpy as np
from jax import lax
from jax.sharding import PartitionSpec as P


def orthonormal_columns(basis):
    result = []
    for column in range(basis.shape[1]):
        vector = basis[:, column] * 1.0
        for repeat in range(2):
            for earlier in result:
                vector = vector - np.sum(earlier * vector) * earlier
        vector = vector / np.sqrt(np.sum(vector * vector))
        result.append(vector)
    return np.stack(result, 1)


def lattice_tables():
    axis_moves = [(1, 0, 0), (-1, 0, 0), (0, 1, 0), (0, -1, 0), (0, 0, 1), (0, 0, -1)]
    edge_moves = []
    for first, second in ((0, 1), (0, 2), (1, 2)):
        for sign_first in (1, -1):
            for sign_second in (1, -1):
                move = [0, 0, 0]
                move[first] = sign_first
                move[second] = sign_second
                edge_moves.append(tuple(move))
    velocity = np.array([(0, 0, 0)] + axis_moves + edge_moves) * 1.0
    weights = np.array([1.0 / 3.0] + [1.0 / 18.0] * 6 + [1.0 / 36.0] * 12)
    opposite = np.array(
        [int(np.argmin(np.abs(velocity + velocity[channel]).sum(1))) for channel in range(19)]
    )
    along_x = velocity[:, 0]
    along_y = velocity[:, 1]
    along_z = velocity[:, 2]
    basis = np.stack(
        [
            np.ones(19),
            along_x,
            along_y,
            along_z,
            along_x**2,
            along_y**2,
            along_z**2,
            along_x * along_y,
            along_y * along_z,
            along_x * along_z,
            along_x * along_y**2,
            along_x * along_z**2,
            along_y * along_x**2,
            along_y * along_z**2,
            along_z * along_x**2,
            along_z * along_y**2,
            along_x**2 * along_y**2,
            along_x**2 * along_z**2,
            along_y**2 * along_z**2,
        ],
        1,
    )
    ortho = orthonormal_columns(basis)
    return (velocity, weights, opposite, ortho)


def column(values):
    return jnp.asarray(np.asarray(values, np.float32).reshape(-1, 1, 1, 1))


def ring(axis, step):
    count = lax.axis_size(axis)
    return [(i, (i + step) % count) for i in range(count)]


def shift_rows(field, moves):
    move_x, move_y, move_z = moves
    size_y, size_z = field.shape[2], field.shape[3]
    low = lax.ppermute(field[:, :, size_y - 1 :, :], "gy", ring("gy", 1))
    high = lax.ppermute(field[:, :, :1, :], "gy", ring("gy", -1))
    from_low = jnp.concatenate([low, field[:, :, : size_y - 1, :]], axis=2)
    from_high = jnp.concatenate([field[:, :, 1:, :], high], axis=2)
    field = jnp.where(move_y > 0, from_low, jnp.where(move_y < 0, from_high, field))
    low = lax.ppermute(field[:, :, :, size_z - 1], "gz", ring("gz", 1))
    high = lax.ppermute(field[:, :, :, 0], "gz", ring("gz", -1))
    lane = lax.broadcasted_iota(jnp.int32, field.shape, 3)
    from_low = jnp.where(lane == 0, low[..., None], jnp.roll(field, 1, axis=3))
    from_high = jnp.where(lane == size_z - 1, high[..., None], jnp.roll(field, -1, axis=3))
    field = jnp.where(move_z > 0, from_low, jnp.where(move_z < 0, from_high, field))
    from_low = jnp.roll(field, 1, axis=1)
    from_high = jnp.roll(field, -1, axis=1)
    return jnp.where(move_x > 0, from_low, jnp.where(move_x < 0, from_high, field))


def reverse_pairs(rows, opposite):
    return jnp.concatenate([rows[int(o) : int(o) + 1] for o in opposite])


NEAR_HALVES = {4: [3, 2, 1, 0], 8: [6, 7, 4, 5, 2, 3, 0, 1]}


def butterfly_rounds(count, inner):
    rounds = []
    step = 1
    while step < inner:
        rounds.append([i ^ step for i in range(count)])
        step *= 2
    ring_size = count // inner
    step = 1
    while step < ring_size:
        if 2 * step == ring_size and ring_size in NEAR_HALVES:
            mirror = NEAR_HALVES[ring_size]
        else:
            mirror = [j ^ step for j in range(ring_size)]
        rounds.append([mirror[i // inner] * inner + i % inner for i in range(count)])
        step *= 2
    return rounds


def butterfly_sum(values, axes, deferred):
    round_index = 0
    for axis, inner in axes:
        for targets in butterfly_rounds(lax.axis_size(axis), inner):
            values = values + lax.ppermute(values, axis, list(enumerate(targets)))
            if round_index < len(deferred):
                values = deferred[round_index](values)
            round_index += 1
    return values


def per_device(populations, solid_mask, flow_rates, species_rates, cotangents):
    velocity, weights, opposite, ortho = lattice_tables()
    highest = lax.Precision.HIGHEST
    rows = populations.shape[0]
    groups = rows // 7
    is_flow = lax.axis_index("sec") == 0
    fluid = (solid_mask == 0)[None]

    flow = populations[:19]
    vx, vy, vz = (column(velocity[:, d]) for d in range(3))
    density = jnp.sum(flow, 0)
    own_motion = jnp.stack(
        [jnp.sum(flow * vx, 0), jnp.sum(flow * vy, 0), jnp.sum(flow * vz, 0)]
    ) / density[None]
    sent_motion = lax.ppermute(own_motion, "sec", [(0, 1)])
    motion = jnp.where(is_flow, own_motion, sent_motion)
    populations, motion = lax.optimization_barrier((populations, motion))
    flow = populations[:19]

    small_weights = column([0.25] + [0.125] * 6)
    grouped = populations.reshape((groups, 7) + populations.shape[1:])
    species_r = species_rates.reshape((groups, 1, 1, 1, 1))
    concentration = jnp.sum(grouped, 1)
    sx, sy, sz = (column(velocity[:7, d])[None] for d in range(3))
    projected_small = motion[0][None] * sx[0] + motion[1][None] * sy[0] + motion[2][None] * sz[0]
    factor = small_weights * (1.0 + 4.0 * projected_small)
    species_eq = factor[None] * concentration[:, None]
    species_gap = grouped - species_eq
    species_relaxed = grouped - species_r * species_gap
    species_bounce = jnp.swapaxes(reverse_pairs(jnp.swapaxes(grouped, 0, 1), opposite[:7]), 0, 1)
    species_post = jnp.where(fluid[None], species_relaxed, species_bounce).reshape(populations.shape)

    q_table = jnp.asarray(ortho, jnp.float32)
    relax = jnp.concatenate([jnp.zeros((4,), flow_rates.dtype), flow_rates]).reshape(19, 1, 1, 1)
    w = column(weights)
    projected = vx * motion[0][None] + vy * motion[1][None] + vz * motion[2][None]
    squared = jnp.sum(motion * motion, 0)
    poly = w * (1.0 + 3.0 * projected + 4.5 * projected * projected - 1.5 * squared[None])
    equilibrium = density[None] * poly
    moments = jnp.einsum("ji,jxyz->ixyz", q_table, flow - equilibrium, precision=highest)
    flow_relaxed = flow - jnp.einsum("ij,jxyz->ixyz", q_table, relax * moments, precision=highest)
    flow_post = jnp.where(fluid, flow_relaxed, reverse_pairs(flow, opposite))
    filler = jnp.zeros((rows - 19,) + populations.shape[1:], jnp.float32)
    post = jnp.where(is_flow, jnp.concatenate([flow_post, filler]), species_post)

    flow_moves = np.concatenate([velocity, np.zeros((rows - 19, 3))])
    species_moves = np.tile(velocity[:7], (groups, 1))
    both_moves = []
    for d in range(3):
        table = jnp.where(is_flow, column(flow_moves[:, d]), column(species_moves[:, d]))
        both_moves.append(jnp.concatenate([table, -table]))
    both = shift_rows(jnp.concatenate([post, cotangents]), both_moves)
    moved = both[:rows]
    returned = both[rows:]
    moved = jnp.where(is_flow, jnp.concatenate([moved[:19], filler]), moved)

    back_species = returned.reshape(grouped.shape)
    back_flow = returned[:19]
    species_rate_grad = -jnp.sum(
        jnp.where(fluid[None], back_species * species_gap, 0.0), axis=(1, 2, 3, 4)
    )
    back_moments = jnp.einsum("ji,jxyz->ixyz", q_table, back_flow, precision=highest)
    flow_rate_grad = -jnp.sum(
        jnp.where(fluid, back_moments * moments, 0.0)[4:], axis=(1, 2, 3)
    )
    local_rates = jnp.where(
        is_flow,
        jnp.concatenate([flow_rate_grad, jnp.zeros((groups,), jnp.float32)]),
        jnp.concatenate([jnp.zeros((15,), jnp.float32), species_rate_grad]),
    )

    later = {}

    def flow_adjoint(values):
        values, (back_flow_, back_moments_) = lax.optimization_barrier(
            (values, (back_flow, back_moments))
        )
        through_eq = jnp.einsum("ij,jxyz->ixyz", q_table, relax * back_moments_, precision=highest)
        density_grad = jnp.sum(through_eq * poly, 0)
        hw = through_eq * w
        hw_sum = jnp.sum(hw, 0)
        hwp = hw * (3.0 + 9.0 * projected)
        later["motion_grad"] = density[None] * (
            jnp.stack([jnp.sum(hwp * vx, 0), jnp.sum(hwp * vy, 0), jnp.sum(hwp * vz, 0)])
            - 3.0 * motion * hw_sum[None]
        )
        later["flow_base"] = back_flow_ - through_eq + density_grad[None]
        return values

    def species_adjoint(values):
        values, back = lax.optimization_barrier((values, back_species))
        weighted_back = back * small_weights[None]
        species_motion_grad = 4.0 * jnp.sum(
            species_r * concentration[:, None] * jnp.stack(
                [jnp.sum(weighted_back * sx, 1), jnp.sum(weighted_back * sy, 1), jnp.sum(weighted_back * sz, 1)], 1
            ),
            0,
        )
        later["species_motion_grad"] = jnp.where(fluid, species_motion_grad, 0.0)
        species_t = jnp.sum(back * factor[None], 1)
        species_grad_fluid = (1.0 - species_r) * back + species_r * species_t[:, None]
        bounced = jnp.swapaxes(reverse_pairs(jnp.swapaxes(back, 0, 1), opposite[:7]), 0, 1)
        later["species_grad"] = jnp.where(fluid[None], species_grad_fluid, bounced).reshape(
            populations.shape
        )
        return values

    partial_rates = butterfly_sum(local_rates, (("gy", 4), ("gz", 1)), [flow_adjoint, species_adjoint])
    plane = populations.shape[1:]
    rate_plane = jnp.zeros(plane, jnp.float32).at[0, 0, : partial_rates.shape[0]].set(partial_rates)
    payload = jnp.concatenate([later["species_motion_grad"], rate_plane[None]])
    other = lax.ppermute(payload, "sec", [(0, 1), (1, 0)])
    rate_grad = partial_rates + other[3, 0, 0, : partial_rates.shape[0]]

    motion_grad = jnp.where(fluid, later["motion_grad"] + other[:3], 0.0)
    along = vx * motion_grad[0][None] + vy * motion_grad[1][None] + vz * motion_grad[2][None]
    extra = (along - jnp.sum(motion * motion_grad, 0)[None]) / density[None]
    flow_grad = jnp.where(
        fluid, later["flow_base"] + extra, reverse_pairs(back_flow, opposite)
    )
    grad_rows = jnp.where(is_flow, jnp.concatenate([flow_grad, filler]), later["species_grad"])
    return (moved, grad_rows, rate_grad)


def solution(mesh):
    placed = (P("sec", None, "gy", "gz"), P(None, "gy", "gz"), P(), P(), P("sec", None, "gy", "gz"))
    return jax.shard_map(
        per_device,
        mesh=mesh,
        in_specs=placed,
        out_specs=(P("sec", None, "gy", "gz"), P("sec", None, "gy", "gz"), P()),
        check_vma=False,
    )
```

```python
import jax
import jax.numpy as jnp
import numpy as np
from jax import lax
from jax.sharding import PartitionSpec as P


def orthonormal_columns(basis):
    result = []
    for column in range(basis.shape[1]):
        vector = basis[:, column] * 1.0
        for repeat in range(2):
            for earlier in result:
                vector = vector - np.sum(earlier * vector) * earlier
        vector = vector / np.sqrt(np.sum(vector * vector))
        result.append(vector)
    return np.stack(result, 1)


def lattice_tables():
    axis_moves = [(1, 0, 0), (-1, 0, 0), (0, 1, 0), (0, -1, 0), (0, 0, 1), (0, 0, -1)]
    edge_moves = []
    for first, second in ((0, 1), (0, 2), (1, 2)):
        for sign_first in (1, -1):
            for sign_second in (1, -1):
                move = [0, 0, 0]
                move[first] = sign_first
                move[second] = sign_second
                edge_moves.append(tuple(move))
    velocity = np.array([(0, 0, 0)] + axis_moves + edge_moves) * 1.0
    weights = np.array([1.0 / 3.0] + [1.0 / 18.0] * 6 + [1.0 / 36.0] * 12)
    opposite = np.array(
        [int(np.argmin(np.abs(velocity + velocity[channel]).sum(1))) for channel in range(19)]
    )
    along_x = velocity[:, 0]
    along_y = velocity[:, 1]
    along_z = velocity[:, 2]
    basis = np.stack(
        [
            np.ones(19),
            along_x,
            along_y,
            along_z,
            along_x**2,
            along_y**2,
            along_z**2,
            along_x * along_y,
            along_y * along_z,
            along_x * along_z,
            along_x * along_y**2,
            along_x * along_z**2,
            along_y * along_x**2,
            along_y * along_z**2,
            along_z * along_x**2,
            along_z * along_y**2,
            along_x**2 * along_y**2,
            along_x**2 * along_z**2,
            along_y**2 * along_z**2,
        ],
        1,
    )
    ortho = orthonormal_columns(basis)
    return (velocity, weights, opposite, ortho)


def column(values):
    return jnp.asarray(np.asarray(values, np.float32).reshape(-1, 1, 1, 1))


def ring(axis, step):
    count = lax.axis_size(axis)
    return [(i, (i + step) % count) for i in range(count)]


def shift_rows(field, moves):
    move_x, move_y, move_z = moves
    size_y, size_z = field.shape[2], field.shape[3]
    low = lax.ppermute(field[:, :, size_y - 1 :, :], "gy", ring("gy", 1))
    high = lax.ppermute(field[:, :, :1, :], "gy", ring("gy", -1))
    from_low = jnp.concatenate([low, field[:, :, : size_y - 1, :]], axis=2)
    from_high = jnp.concatenate([field[:, :, 1:, :], high], axis=2)
    field = jnp.where(move_y > 0, from_low, jnp.where(move_y < 0, from_high, field))
    low = lax.ppermute(field[:, :, :, size_z - 1], "gz", ring("gz", 1))
    high = lax.ppermute(field[:, :, :, 0], "gz", ring("gz", -1))
    lane = lax.broadcasted_iota(jnp.int32, field.shape, 3)
    from_low = jnp.where(lane == 0, low[..., None], jnp.roll(field, 1, axis=3))
    from_high = jnp.where(lane == size_z - 1, high[..., None], jnp.roll(field, -1, axis=3))
    field = jnp.where(move_z > 0, from_low, jnp.where(move_z < 0, from_high, field))
    from_low = jnp.roll(field, 1, axis=1)
    from_high = jnp.roll(field, -1, axis=1)
    return jnp.where(move_x > 0, from_low, jnp.where(move_x < 0, from_high, field))


def reverse_pairs(rows, opposite):
    return jnp.concatenate([rows[int(o) : int(o) + 1] for o in opposite])


NEAR_HALVES = {4: [3, 2, 1, 0], 8: [6, 7, 4, 5, 2, 3, 0, 1]}


def butterfly_rounds(count, inner):
    rounds = []
    step = 1
    while step < inner:
        rounds.append([i ^ step for i in range(count)])
        step *= 2
    ring_size = count // inner
    step = 1
    while step < ring_size:
        if 2 * step == ring_size and ring_size in NEAR_HALVES:
            mirror = NEAR_HALVES[ring_size]
        else:
            mirror = [j ^ step for j in range(ring_size)]
        rounds.append([mirror[i // inner] * inner + i % inner for i in range(count)])
        step *= 2
    return rounds


def butterfly_sum(values, axes, deferred):
    round_index = 0
    for axis, inner in axes:
        for targets in butterfly_rounds(lax.axis_size(axis), inner):
            values = values + lax.ppermute(values, axis, list(enumerate(targets)))
            if round_index < len(deferred):
                values = deferred[round_index](values)
            round_index += 1
    return values


def per_device(populations, solid_mask, flow_rates, species_rates, cotangents):
    velocity, weights, opposite, ortho = lattice_tables()
    highest = lax.Precision.HIGHEST
    rows = populations.shape[0]
    groups = rows // 7
    is_flow = lax.axis_index("sec") == 0
    fluid = (solid_mask == 0)[None]

    flow = populations[:19]
    vx, vy, vz = (column(velocity[:, d]) for d in range(3))
    density = jnp.sum(flow, 0)
    own_motion = jnp.stack(
        [jnp.sum(flow * vx, 0), jnp.sum(flow * vy, 0), jnp.sum(flow * vz, 0)]
    ) / density[None]
    sent_motion = lax.ppermute(own_motion, "sec", [(0, 1)])
    motion = jnp.where(is_flow, own_motion, sent_motion)

    small_weights = column([0.25] + [0.125] * 6)
    grouped = populations.reshape((groups, 7) + populations.shape[1:])
    species_r = species_rates.reshape((groups, 1, 1, 1, 1))
    concentration = jnp.sum(grouped, 1)
    sx, sy, sz = (column(velocity[:7, d])[None] for d in range(3))
    projected_small = motion[0][None] * sx[0] + motion[1][None] * sy[0] + motion[2][None] * sz[0]
    factor = small_weights * (1.0 + 4.0 * projected_small)
    species_eq = factor[None] * concentration[:, None]
    species_gap = grouped - species_eq
    species_relaxed = grouped - species_r * species_gap
    species_bounce = jnp.swapaxes(reverse_pairs(jnp.swapaxes(grouped, 0, 1), opposite[:7]), 0, 1)
    species_post = jnp.where(fluid[None], species_relaxed, species_bounce).reshape(populations.shape)

    q_table = jnp.asarray(ortho, jnp.float32)
    relax = jnp.concatenate([jnp.zeros((4,), flow_rates.dtype), flow_rates]).reshape(19, 1, 1, 1)
    w = column(weights)
    projected = vx * motion[0][None] + vy * motion[1][None] + vz * motion[2][None]
    squared = jnp.sum(motion * motion, 0)
    poly = w * (1.0 + 3.0 * projected + 4.5 * projected * projected - 1.5 * squared[None])
    equilibrium = density[None] * poly
    moments = jnp.einsum("ji,jxyz->ixyz", q_table, flow - equilibrium, precision=highest)
    flow_relaxed = flow - jnp.einsum("ij,jxyz->ixyz", q_table, relax * moments, precision=highest)
    flow_post = jnp.where(fluid, flow_relaxed, reverse_pairs(flow, opposite))
    filler = jnp.zeros((rows - 19,) + populations.shape[1:], jnp.float32)
    post = jnp.where(is_flow, jnp.concatenate([flow_post, filler]), species_post)

    flow_moves = np.concatenate([velocity, np.zeros((rows - 19, 3))])
    species_moves = np.tile(velocity[:7], (groups, 1))
    both_moves = []
    for d in range(3):
        table = jnp.where(is_flow, column(flow_moves[:, d]), column(species_moves[:, d]))
        both_moves.append(jnp.concatenate([table, -table]))
    both = shift_rows(jnp.concatenate([post, cotangents]), both_moves)
    moved = both[:rows]
    returned = both[rows:]
    moved = jnp.where(is_flow, jnp.concatenate([moved[:19], filler]), moved)

    back_species = returned.reshape(grouped.shape)
    back_flow = returned[:19]
    species_rate_grad = -jnp.sum(
        jnp.where(fluid[None], back_species * species_gap, 0.0), axis=(1, 2, 3, 4)
    )
    back_moments = jnp.einsum("ji,jxyz->ixyz", q_table, back_flow, precision=highest)
    flow_rate_grad = -jnp.sum(
        jnp.where(fluid, back_moments * moments, 0.0)[4:], axis=(1, 2, 3)
    )
    local_rates = jnp.where(
        is_flow,
        jnp.concatenate([flow_rate_grad, jnp.zeros((groups,), jnp.float32)]),
        jnp.concatenate([jnp.zeros((15,), jnp.float32), species_rate_grad]),
    )

    later = {}

    def flow_adjoint(values):
        values, (back_flow_, back_moments_) = lax.optimization_barrier(
            (values, (back_flow, back_moments))
        )
        through_eq = jnp.einsum("ij,jxyz->ixyz", q_table, relax * back_moments_, precision=highest)
        density_grad = jnp.sum(through_eq * poly, 0)
        hw = through_eq * w
        hw_sum = jnp.sum(hw, 0)
        hwp = hw * (3.0 + 9.0 * projected)
        later["motion_grad"] = density[None] * (
            jnp.stack([jnp.sum(hwp * vx, 0), jnp.sum(hwp * vy, 0), jnp.sum(hwp * vz, 0)])
            - 3.0 * motion * hw_sum[None]
        )
        later["flow_base"] = back_flow_ - through_eq + density_grad[None]
        return values

    def species_adjoint(values):
        values, back = lax.optimization_barrier((values, back_species))
        weighted_back = back * small_weights[None]
        species_motion_grad = 4.0 * jnp.sum(
            species_r * concentration[:, None] * jnp.stack(
                [jnp.sum(weighted_back * sx, 1), jnp.sum(weighted_back * sy, 1), jnp.sum(weighted_back * sz, 1)], 1
            ),
            0,
        )
        later["species_motion_grad"] = jnp.where(fluid, species_motion_grad, 0.0)
        species_t = jnp.sum(back * factor[None], 1)
        species_grad_fluid = (1.0 - species_r) * back + species_r * species_t[:, None]
        bounced = jnp.swapaxes(reverse_pairs(jnp.swapaxes(back, 0, 1), opposite[:7]), 0, 1)
        later["species_grad"] = jnp.where(fluid[None], species_grad_fluid, bounced).reshape(
            populations.shape
        )
        return values

    partial_rates = butterfly_sum(local_rates, (("gy", 4),), [flow_adjoint, species_adjoint])
    plane = populations.shape[1:]
    rate_plane = jnp.zeros(plane, jnp.float32).at[0, 0, : partial_rates.shape[0]].set(partial_rates)
    payload = jnp.concatenate([later["species_motion_grad"], rate_plane[None]])
    other = lax.ppermute(payload, "sec", [(0, 1), (1, 0)])
    partial_rates = partial_rates + other[3, 0, 0, : partial_rates.shape[0]]

    def flow_gradient(values):
        values, received = lax.optimization_barrier((values, other[:3]))
        motion_grad = jnp.where(fluid, later["motion_grad"] + received, 0.0)
        along = vx * motion_grad[0][None] + vy * motion_grad[1][None] + vz * motion_grad[2][None]
        extra = (along - jnp.sum(motion * motion_grad, 0)[None]) / density[None]
        flow_grad = jnp.where(
            fluid, later["flow_base"] + extra, reverse_pairs(back_flow, opposite)
        )
        later["grad_rows"] = jnp.where(
            is_flow, jnp.concatenate([flow_grad, filler]), later["species_grad"]
        )
        return values

    rate_grad = butterfly_sum(partial_rates, (("gz", 1),), [flow_gradient])
    grad_rows = later["grad_rows"]
    return (moved, grad_rows, rate_grad)


def solution(mesh):
    placed = (P("sec", None, "gy", "gz"), P(None, "gy", "gz"), P(), P(), P("sec", None, "gy", "gz"))
    return jax.shard_map(
        per_device,
        mesh=mesh,
        in_specs=placed,
        out_specs=(P("sec", None, "gy", "gz"), P("sec", None, "gy", "gz"), P()),
        check_vma=False,
    )
```

```python
import jax
import jax.numpy as jnp
import numpy as np
from jax import lax
from jax.sharding import PartitionSpec as P


def orthonormal_columns(basis):
    result = []
    for column in range(basis.shape[1]):
        vector = basis[:, column] * 1.0
        for repeat in range(2):
            for earlier in result:
                vector = vector - np.sum(earlier * vector) * earlier
        vector = vector / np.sqrt(np.sum(vector * vector))
        result.append(vector)
    return np.stack(result, 1)


def lattice_tables():
    axis_moves = [(1, 0, 0), (-1, 0, 0), (0, 1, 0), (0, -1, 0), (0, 0, 1), (0, 0, -1)]
    edge_moves = []
    for first, second in ((0, 1), (0, 2), (1, 2)):
        for sign_first in (1, -1):
            for sign_second in (1, -1):
                move = [0, 0, 0]
                move[first] = sign_first
                move[second] = sign_second
                edge_moves.append(tuple(move))
    velocity = np.array([(0, 0, 0)] + axis_moves + edge_moves) * 1.0
    weights = np.array([1.0 / 3.0] + [1.0 / 18.0] * 6 + [1.0 / 36.0] * 12)
    opposite = np.array(
        [int(np.argmin(np.abs(velocity + velocity[channel]).sum(1))) for channel in range(19)]
    )
    along_x = velocity[:, 0]
    along_y = velocity[:, 1]
    along_z = velocity[:, 2]
    basis = np.stack(
        [
            np.ones(19),
            along_x,
            along_y,
            along_z,
            along_x**2,
            along_y**2,
            along_z**2,
            along_x * along_y,
            along_y * along_z,
            along_x * along_z,
            along_x * along_y**2,
            along_x * along_z**2,
            along_y * along_x**2,
            along_y * along_z**2,
            along_z * along_x**2,
            along_z * along_y**2,
            along_x**2 * along_y**2,
            along_x**2 * along_z**2,
            along_y**2 * along_z**2,
        ],
        1,
    )
    ortho = orthonormal_columns(basis)
    return (velocity, weights, opposite, ortho)


def column(values):
    return jnp.asarray(np.asarray(values, np.float32).reshape(-1, 1, 1, 1))


def ring(axis, step):
    count = lax.axis_size(axis)
    return [(i, (i + step) % count) for i in range(count)]


def shift_rows(field, moves):
    move_x, move_y, move_z = moves
    size_y, size_z = field.shape[2], field.shape[3]
    low = lax.ppermute(field[:, :, size_y - 1 :, :], "gy", ring("gy", 1))
    high = lax.ppermute(field[:, :, :1, :], "gy", ring("gy", -1))
    from_low = jnp.concatenate([low, field[:, :, : size_y - 1, :]], axis=2)
    from_high = jnp.concatenate([field[:, :, 1:, :], high], axis=2)
    field = jnp.where(move_y > 0, from_low, jnp.where(move_y < 0, from_high, field))
    low = lax.ppermute(field[:, :, :, size_z - 1], "gz", ring("gz", 1))
    high = lax.ppermute(field[:, :, :, 0], "gz", ring("gz", -1))
    lane = lax.broadcasted_iota(jnp.int32, field.shape, 3)
    from_low = jnp.where(lane == 0, low[..., None], jnp.roll(field, 1, axis=3))
    from_high = jnp.where(lane == size_z - 1, high[..., None], jnp.roll(field, -1, axis=3))
    field = jnp.where(move_z > 0, from_low, jnp.where(move_z < 0, from_high, field))
    from_low = jnp.roll(field, 1, axis=1)
    from_high = jnp.roll(field, -1, axis=1)
    return jnp.where(move_x > 0, from_low, jnp.where(move_x < 0, from_high, field))


def reverse_pairs(rows, opposite):
    return jnp.concatenate([rows[int(o) : int(o) + 1] for o in opposite])


NEAR_HALVES = {4: [3, 2, 1, 0], 8: [6, 7, 4, 5, 2, 3, 0, 1]}


def butterfly_rounds(count, inner):
    rounds = []
    step = 1
    while step < inner:
        rounds.append([i ^ step for i in range(count)])
        step *= 2
    ring_size = count // inner
    step = 1
    while step < ring_size:
        if 2 * step == ring_size and ring_size in NEAR_HALVES:
            mirror = NEAR_HALVES[ring_size]
        else:
            mirror = [j ^ step for j in range(ring_size)]
        rounds.append([mirror[i // inner] * inner + i % inner for i in range(count)])
        step *= 2
    return rounds


def butterfly_sum(values, axes, deferred):
    round_index = 0
    for axis, inner in axes:
        for targets in butterfly_rounds(lax.axis_size(axis), inner):
            values = values + lax.ppermute(values, axis, list(enumerate(targets)))
            if round_index < len(deferred):
                values = deferred[round_index](values)
            round_index += 1
    return values


def per_device(populations, solid_mask, flow_rates, species_rates, cotangents):
    velocity, weights, opposite, ortho = lattice_tables()
    highest = lax.Precision.HIGHEST
    rows = populations.shape[0]
    groups = rows // 7
    is_flow = lax.axis_index("sec") == 0
    fluid = (solid_mask == 0)[None]

    flow = populations[:19]
    vx, vy, vz = (column(velocity[:, d]) for d in range(3))
    density = jnp.sum(flow, 0)
    own_motion = jnp.stack(
        [jnp.sum(flow * vx, 0), jnp.sum(flow * vy, 0), jnp.sum(flow * vz, 0)]
    ) / density[None]
    sent_motion = lax.ppermute(own_motion, "sec", [(0, 1)])
    motion = jnp.where(is_flow, own_motion, sent_motion)

    small_weights = column([0.25] + [0.125] * 6)
    grouped = populations.reshape((groups, 7) + populations.shape[1:])
    species_r = species_rates.reshape((groups, 1, 1, 1, 1))
    concentration = jnp.sum(grouped, 1)
    sx, sy, sz = (column(velocity[:7, d])[None] for d in range(3))
    projected_small = motion[0][None] * sx[0] + motion[1][None] * sy[0] + motion[2][None] * sz[0]
    factor = small_weights * (1.0 + 4.0 * projected_small)
    species_eq = factor[None] * concentration[:, None]
    species_gap = grouped - species_eq
    species_relaxed = grouped - species_r * species_gap
    species_bounce = jnp.swapaxes(reverse_pairs(jnp.swapaxes(grouped, 0, 1), opposite[:7]), 0, 1)
    species_post = jnp.where(fluid[None], species_relaxed, species_bounce).reshape(populations.shape)

    q_table = jnp.asarray(ortho, jnp.float32)
    relax = jnp.concatenate([jnp.zeros((4,), flow_rates.dtype), flow_rates]).reshape(19, 1, 1, 1)
    w = column(weights)
    projected = vx * motion[0][None] + vy * motion[1][None] + vz * motion[2][None]
    squared = jnp.sum(motion * motion, 0)
    poly = w * (1.0 + 3.0 * projected + 4.5 * projected * projected - 1.5 * squared[None])
    equilibrium = density[None] * poly
    moments = jnp.einsum("ji,jxyz->ixyz", q_table, flow - equilibrium, precision=highest)
    fluid_moments = jnp.where(fluid, moments, 0.0)
    flow_relaxed = flow - jnp.einsum("ij,jxyz->ixyz", q_table, relax * moments, precision=highest)
    flow_post = jnp.where(fluid, flow_relaxed, reverse_pairs(flow, opposite))
    filler = jnp.zeros((rows - 19,) + populations.shape[1:], jnp.float32)
    post = jnp.where(is_flow, jnp.concatenate([flow_post, filler]), species_post)

    flow_moves = np.concatenate([velocity, np.zeros((rows - 19, 3))])
    species_moves = np.tile(velocity[:7], (groups, 1))
    both_moves = []
    for d in range(3):
        table = jnp.where(is_flow, column(flow_moves[:, d]), column(species_moves[:, d]))
        both_moves.append(jnp.concatenate([table, -table]))
    both = shift_rows(jnp.concatenate([post, cotangents]), both_moves)
    moved = both[:rows]
    returned = both[rows:]
    moved = jnp.where(is_flow, jnp.concatenate([moved[:19], filler]), moved)

    back_species = returned.reshape(grouped.shape)
    back_flow = returned[:19]
    species_rate_grad = -jnp.sum(
        jnp.where(fluid[None], back_species * species_gap, 0.0), axis=(1, 2, 3, 4)
    )
    pairs = jnp.einsum("ixyz,kxyz->ik", back_flow, fluid_moments, precision=highest)
    flow_rate_grad = -jnp.sum(q_table * pairs, axis=0)[4:]
    local_rates = jnp.where(
        is_flow,
        jnp.concatenate([flow_rate_grad, jnp.zeros((groups,), jnp.float32)]),
        jnp.concatenate([jnp.zeros((15,), jnp.float32), species_rate_grad]),
    )

    later = {}

    def flow_adjoint(values):
        values, back_flow_ = lax.optimization_barrier((values, back_flow))
        back_moments_ = jnp.einsum("ji,jxyz->ixyz", q_table, back_flow_, precision=highest)
        through_eq = jnp.einsum("ij,jxyz->ixyz", q_table, relax * back_moments_, precision=highest)
        density_grad = jnp.sum(through_eq * poly, 0)
        hw = through_eq * w
        hw_sum = jnp.sum(hw, 0)
        hwp = hw * (3.0 + 9.0 * projected)
        later["motion_grad"] = density[None] * (
            jnp.stack([jnp.sum(hwp * vx, 0), jnp.sum(hwp * vy, 0), jnp.sum(hwp * vz, 0)])
            - 3.0 * motion * hw_sum[None]
        )
        later["flow_base"] = back_flow_ - through_eq + density_grad[None]
        return values

    def species_adjoint(values):
        values, back = lax.optimization_barrier((values, back_species))
        weighted_back = back * small_weights[None]
        species_motion_grad = 4.0 * jnp.sum(
            species_r * concentration[:, None] * jnp.stack(
                [jnp.sum(weighted_back * sx, 1), jnp.sum(weighted_back * sy, 1), jnp.sum(weighted_back * sz, 1)], 1
            ),
            0,
        )
        later["species_motion_grad"] = jnp.where(fluid, species_motion_grad, 0.0)
        species_t = jnp.sum(back * factor[None], 1)
        species_grad_fluid = (1.0 - species_r) * back + species_r * species_t[:, None]
        bounced = jnp.swapaxes(reverse_pairs(jnp.swapaxes(back, 0, 1), opposite[:7]), 0, 1)
        later["species_grad"] = jnp.where(fluid[None], species_grad_fluid, bounced).reshape(
            populations.shape
        )
        return values

    partial_rates = butterfly_sum(local_rates, (("gy", 4),), [flow_adjoint, species_adjoint])
    plane = populations.shape[1:]
    rate_plane = jnp.zeros(plane, jnp.float32).at[0, 0, : partial_rates.shape[0]].set(partial_rates)
    payload = jnp.concatenate([later["species_motion_grad"], rate_plane[None]])
    other = lax.ppermute(payload, "sec", [(0, 1), (1, 0)])
    partial_rates = partial_rates + other[3, 0, 0, : partial_rates.shape[0]]

    def flow_gradient(values):
        values, received = lax.optimization_barrier((values, other[:3]))
        motion_grad = jnp.where(fluid, later["motion_grad"] + received, 0.0)
        along = vx * motion_grad[0][None] + vy * motion_grad[1][None] + vz * motion_grad[2][None]
        extra = (along - jnp.sum(motion * motion_grad, 0)[None]) / density[None]
        flow_grad = jnp.where(
            fluid, later["flow_base"] + extra, reverse_pairs(back_flow, opposite)
        )
        later["grad_rows"] = jnp.where(
            is_flow, jnp.concatenate([flow_grad, filler]), later["species_grad"]
        )
        return values

    rate_grad = butterfly_sum(partial_rates, (("gz", 1),), [flow_gradient])
    grad_rows = later["grad_rows"]
    return (moved, grad_rows, rate_grad)


def solution(mesh):
    placed = (P("sec", None, "gy", "gz"), P(None, "gy", "gz"), P(), P(), P("sec", None, "gy", "gz"))
    return jax.shard_map(
        per_device,
        mesh=mesh,
        in_specs=placed,
        out_specs=(P("sec", None, "gy", "gz"), P("sec", None, "gy", "gz"), P()),
        check_vma=False,
    )
```

```python
import jax
import jax.numpy as jnp
import numpy as np
from jax import lax
from jax.sharding import PartitionSpec as P


def orthonormal_columns(basis):
    result = []
    for column in range(basis.shape[1]):
        vector = basis[:, column] * 1.0
        for repeat in range(2):
            for earlier in result:
                vector = vector - np.sum(earlier * vector) * earlier
        vector = vector / np.sqrt(np.sum(vector * vector))
        result.append(vector)
    return np.stack(result, 1)


def lattice_tables():
    axis_moves = [(1, 0, 0), (-1, 0, 0), (0, 1, 0), (0, -1, 0), (0, 0, 1), (0, 0, -1)]
    edge_moves = []
    for first, second in ((0, 1), (0, 2), (1, 2)):
        for sign_first in (1, -1):
            for sign_second in (1, -1):
                move = [0, 0, 0]
                move[first] = sign_first
                move[second] = sign_second
                edge_moves.append(tuple(move))
    velocity = np.array([(0, 0, 0)] + axis_moves + edge_moves) * 1.0
    weights = np.array([1.0 / 3.0] + [1.0 / 18.0] * 6 + [1.0 / 36.0] * 12)
    opposite = np.array(
        [int(np.argmin(np.abs(velocity + velocity[channel]).sum(1))) for channel in range(19)]
    )
    along_x = velocity[:, 0]
    along_y = velocity[:, 1]
    along_z = velocity[:, 2]
    basis = np.stack(
        [
            np.ones(19),
            along_x,
            along_y,
            along_z,
            along_x**2,
            along_y**2,
            along_z**2,
            along_x * along_y,
            along_y * along_z,
            along_x * along_z,
            along_x * along_y**2,
            along_x * along_z**2,
            along_y * along_x**2,
            along_y * along_z**2,
            along_z * along_x**2,
            along_z * along_y**2,
            along_x**2 * along_y**2,
            along_x**2 * along_z**2,
            along_y**2 * along_z**2,
        ],
        1,
    )
    ortho = orthonormal_columns(basis)
    return (velocity, weights, opposite, ortho)


def column(values):
    return jnp.asarray(np.asarray(values, np.float32).reshape(-1, 1, 1, 1))


def ring(axis, step):
    count = lax.axis_size(axis)
    return [(i, (i + step) % count) for i in range(count)]


def exchange_rows(field, moves):
    move_x, move_y, move_z = moves
    size_y, size_z = field.shape[2], field.shape[3]
    low = lax.ppermute(field[:, :, size_y - 1 :, :], "gy", ring("gy", 1))
    high = lax.ppermute(field[:, :, :1, :], "gy", ring("gy", -1))
    from_low = jnp.concatenate([low, field[:, :, : size_y - 1, :]], axis=2)
    from_high = jnp.concatenate([field[:, :, 1:, :], high], axis=2)
    field = jnp.where(move_y > 0, from_low, jnp.where(move_y < 0, from_high, field))
    low = lax.ppermute(field[:, :, :, size_z - 1], "gz", ring("gz", 1))
    high = lax.ppermute(field[:, :, :, 0], "gz", ring("gz", -1))
    return field, low, high


def finish_rows(field, low, high, move_z, move_x):
    size_z = field.shape[3]
    lane = lax.broadcasted_iota(jnp.int32, field.shape, 3)
    from_low = jnp.where(lane == 0, low[..., None], jnp.roll(field, 1, axis=3))
    from_high = jnp.where(lane == size_z - 1, high[..., None], jnp.roll(field, -1, axis=3))
    field = jnp.where(move_z > 0, from_low, jnp.where(move_z < 0, from_high, field))
    from_low = jnp.roll(field, 1, axis=1)
    from_high = jnp.roll(field, -1, axis=1)
    return jnp.where(move_x > 0, from_low, jnp.where(move_x < 0, from_high, field))


def reverse_pairs(rows, opposite):
    return jnp.concatenate([rows[int(o) : int(o) + 1] for o in opposite])


NEAR_HALVES = {4: [3, 2, 1, 0], 8: [6, 7, 4, 5, 2, 3, 0, 1]}


def butterfly_rounds(count, inner):
    rounds = []
    step = 1
    while step < inner:
        rounds.append([i ^ step for i in range(count)])
        step *= 2
    ring_size = count // inner
    step = 1
    while step < ring_size:
        if 2 * step == ring_size and ring_size in NEAR_HALVES:
            mirror = NEAR_HALVES[ring_size]
        else:
            mirror = [j ^ step for j in range(ring_size)]
        rounds.append([mirror[i // inner] * inner + i % inner for i in range(count)])
        step *= 2
    return rounds


def butterfly_sum(values, axes, deferred):
    round_index = 0
    for axis, inner in axes:
        for targets in butterfly_rounds(lax.axis_size(axis), inner):
            values = values + lax.ppermute(values, axis, list(enumerate(targets)))
            if round_index < len(deferred):
                values = deferred[round_index](values)
            round_index += 1
    return values


def per_device(populations, solid_mask, flow_rates, species_rates, cotangents):
    velocity, weights, opposite, ortho = lattice_tables()
    highest = lax.Precision.HIGHEST
    rows = populations.shape[0]
    groups = rows // 7
    is_flow = lax.axis_index("sec") == 0
    fluid = (solid_mask == 0)[None]

    flow = populations[:19]
    vx, vy, vz = (column(velocity[:, d]) for d in range(3))
    density = jnp.sum(flow, 0)
    own_motion = jnp.stack(
        [jnp.sum(flow * vx, 0), jnp.sum(flow * vy, 0), jnp.sum(flow * vz, 0)]
    ) / density[None]
    sent_motion = lax.ppermute(own_motion, "sec", [(0, 1)])
    motion = jnp.where(is_flow, own_motion, sent_motion)

    small_weights = column([0.25] + [0.125] * 6)
    grouped = populations.reshape((groups, 7) + populations.shape[1:])
    species_r = species_rates.reshape((groups, 1, 1, 1, 1))
    concentration = jnp.sum(grouped, 1)
    sx, sy, sz = (column(velocity[:7, d])[None] for d in range(3))
    projected_small = motion[0][None] * sx[0] + motion[1][None] * sy[0] + motion[2][None] * sz[0]
    factor = small_weights * (1.0 + 4.0 * projected_small)
    species_eq = factor[None] * concentration[:, None]
    species_gap = grouped - species_eq
    species_relaxed = grouped - species_r * species_gap
    species_bounce = jnp.swapaxes(reverse_pairs(jnp.swapaxes(grouped, 0, 1), opposite[:7]), 0, 1)
    species_post = jnp.where(fluid[None], species_relaxed, species_bounce).reshape(populations.shape)

    q_table = jnp.asarray(ortho, jnp.float32)
    relax = jnp.concatenate([jnp.zeros((4,), flow_rates.dtype), flow_rates]).reshape(19, 1, 1, 1)
    w = column(weights)
    projected = vx * motion[0][None] + vy * motion[1][None] + vz * motion[2][None]
    squared = jnp.sum(motion * motion, 0)
    poly = w * (1.0 + 3.0 * projected + 4.5 * projected * projected - 1.5 * squared[None])
    equilibrium = density[None] * poly
    moments = jnp.einsum("ji,jxyz->ixyz", q_table, flow - equilibrium, precision=highest)
    flow_relaxed = flow - jnp.einsum("ij,jxyz->ixyz", q_table, relax * moments, precision=highest)
    flow_post = jnp.where(fluid, flow_relaxed, reverse_pairs(flow, opposite))
    filler = jnp.zeros((rows - 19,) + populations.shape[1:], jnp.float32)
    post = jnp.where(is_flow, jnp.concatenate([flow_post, filler]), species_post)

    flow_moves = np.concatenate([velocity, np.zeros((rows - 19, 3))])
    species_moves = np.tile(velocity[:7], (groups, 1))
    both_moves = []
    for d in range(3):
        table = jnp.where(is_flow, column(flow_moves[:, d]), column(species_moves[:, d]))
        both_moves.append(jnp.concatenate([table, -table]))
    both, low_z, high_z = exchange_rows(jnp.concatenate([post, cotangents]), both_moves)
    returned = finish_rows(
        both[rows:], low_z[rows:], high_z[rows:], both_moves[2][rows:], both_moves[0][rows:]
    )

    back_species = returned.reshape(grouped.shape)
    back_flow = returned[:19]
    species_rate_grad = -jnp.sum(
        jnp.where(fluid[None], back_species * species_gap, 0.0), axis=(1, 2, 3, 4)
    )
    back_moments = jnp.einsum("ji,jxyz->ixyz", q_table, back_flow, precision=highest)
    flow_rate_grad = -jnp.sum(
        jnp.where(fluid, back_moments * moments, 0.0)[4:], axis=(1, 2, 3)
    )
    local_rates = jnp.where(
        is_flow,
        jnp.concatenate([flow_rate_grad, jnp.zeros((groups,), jnp.float32)]),
        jnp.concatenate([jnp.zeros((15,), jnp.float32), species_rate_grad]),
    )

    later = {}

    def post_passing(values):
        values, (field_, low_, high_) = lax.optimization_barrier(
            (values, (both[:rows], low_z[:rows], high_z[:rows]))
        )
        moved_ = finish_rows(field_, low_, high_, both_moves[2][:rows], both_moves[0][:rows])
        later["moved"] = jnp.where(is_flow, jnp.concatenate([moved_[:19], filler]), moved_)
        return values

    def flow_adjoint(values):
        values, (back_flow_, back_moments_) = lax.optimization_barrier(
            (values, (back_flow, back_moments))
        )
        through_eq = jnp.einsum("ij,jxyz->ixyz", q_table, relax * back_moments_, precision=highest)
        density_grad = jnp.sum(through_eq * poly, 0)
        hw = through_eq * w
        hw_sum = jnp.sum(hw, 0)
        hwp = hw * (3.0 + 9.0 * projected)
        later["motion_grad"] = density[None] * (
            jnp.stack([jnp.sum(hwp * vx, 0), jnp.sum(hwp * vy, 0), jnp.sum(hwp * vz, 0)])
            - 3.0 * motion * hw_sum[None]
        )
        later["flow_base"] = back_flow_ - through_eq + density_grad[None]
        return values

    def species_adjoint(values):
        values, back = lax.optimization_barrier((values, back_species))
        weighted_back = back * small_weights[None]
        species_motion_grad = 4.0 * jnp.sum(
            species_r * concentration[:, None] * jnp.stack(
                [jnp.sum(weighted_back * sx, 1), jnp.sum(weighted_back * sy, 1), jnp.sum(weighted_back * sz, 1)], 1
            ),
            0,
        )
        later["species_motion_grad"] = jnp.where(fluid, species_motion_grad, 0.0)
        species_t = jnp.sum(back * factor[None], 1)
        species_grad_fluid = (1.0 - species_r) * back + species_r * species_t[:, None]
        bounced = jnp.swapaxes(reverse_pairs(jnp.swapaxes(back, 0, 1), opposite[:7]), 0, 1)
        later["species_grad"] = jnp.where(fluid[None], species_grad_fluid, bounced).reshape(
            populations.shape
        )
        return values

    partial_rates = butterfly_sum(local_rates, (("gy", 4),), [flow_adjoint, species_adjoint, post_passing])
    plane = populations.shape[1:]
    rate_plane = jnp.zeros(plane, jnp.float32).at[0, 0, : partial_rates.shape[0]].set(partial_rates)
    payload = jnp.concatenate([later["species_motion_grad"], rate_plane[None]])
    other = lax.ppermute(payload, "sec", [(0, 1), (1, 0)])
    partial_rates = partial_rates + other[3, 0, 0, : partial_rates.shape[0]]

    def flow_gradient(values):
        values, received = lax.optimization_barrier((values, other[:3]))
        motion_grad = jnp.where(fluid, later["motion_grad"] + received, 0.0)
        along = vx * motion_grad[0][None] + vy * motion_grad[1][None] + vz * motion_grad[2][None]
        extra = (along - jnp.sum(motion * motion_grad, 0)[None]) / density[None]
        flow_grad = jnp.where(
            fluid, later["flow_base"] + extra, reverse_pairs(back_flow, opposite)
        )
        later["grad_rows"] = jnp.where(
            is_flow, jnp.concatenate([flow_grad, filler]), later["species_grad"]
        )
        return values

    rate_grad = butterfly_sum(partial_rates, (("gz", 1),), [flow_gradient])
    grad_rows = later["grad_rows"]
    return (later["moved"], grad_rows, rate_grad)


def solution(mesh):
    placed = (P("sec", None, "gy", "gz"), P(None, "gy", "gz"), P(), P(), P("sec", None, "gy", "gz"))
    return jax.shard_map(
        per_device,
        mesh=mesh,
        in_specs=placed,
        out_specs=(P("sec", None, "gy", "gz"), P("sec", None, "gy", "gz"), P()),
        check_vma=False,
    )
```

```python
import jax
import jax.numpy as jnp
import numpy as np
from jax import lax
from jax.sharding import PartitionSpec as P


def orthonormal_columns(basis):
    result = []
    for column in range(basis.shape[1]):
        vector = basis[:, column] * 1.0
        for repeat in range(2):
            for earlier in result:
                vector = vector - np.sum(earlier * vector) * earlier
        vector = vector / np.sqrt(np.sum(vector * vector))
        result.append(vector)
    return np.stack(result, 1)


def lattice_tables():
    axis_moves = [(1, 0, 0), (-1, 0, 0), (0, 1, 0), (0, -1, 0), (0, 0, 1), (0, 0, -1)]
    edge_moves = []
    for first, second in ((0, 1), (0, 2), (1, 2)):
        for sign_first in (1, -1):
            for sign_second in (1, -1):
                move = [0, 0, 0]
                move[first] = sign_first
                move[second] = sign_second
                edge_moves.append(tuple(move))
    velocity = np.array([(0, 0, 0)] + axis_moves + edge_moves) * 1.0
    weights = np.array([1.0 / 3.0] + [1.0 / 18.0] * 6 + [1.0 / 36.0] * 12)
    opposite = np.array(
        [int(np.argmin(np.abs(velocity + velocity[channel]).sum(1))) for channel in range(19)]
    )
    along_x = velocity[:, 0]
    along_y = velocity[:, 1]
    along_z = velocity[:, 2]
    basis = np.stack(
        [
            np.ones(19),
            along_x,
            along_y,
            along_z,
            along_x**2,
            along_y**2,
            along_z**2,
            along_x * along_y,
            along_y * along_z,
            along_x * along_z,
            along_x * along_y**2,
            along_x * along_z**2,
            along_y * along_x**2,
            along_y * along_z**2,
            along_z * along_x**2,
            along_z * along_y**2,
            along_x**2 * along_y**2,
            along_x**2 * along_z**2,
            along_y**2 * along_z**2,
        ],
        1,
    )
    ortho = orthonormal_columns(basis)
    return (velocity, weights, opposite, ortho)


def column(values):
    return jnp.asarray(np.asarray(values, np.float32).reshape(-1, 1, 1, 1))


def ring(axis, step):
    count = lax.axis_size(axis)
    return [(i, (i + step) % count) for i in range(count)]


def shift_rows(field, moves):
    move_x, move_y, move_z = moves
    size_y, size_z = field.shape[2], field.shape[3]
    low = lax.ppermute(field[:, :, size_y - 1 :, :], "gy", ring("gy", 1))
    high = lax.ppermute(field[:, :, :1, :], "gy", ring("gy", -1))
    from_low = jnp.concatenate([low, field[:, :, : size_y - 1, :]], axis=2)
    from_high = jnp.concatenate([field[:, :, 1:, :], high], axis=2)
    field = jnp.where(move_y > 0, from_low, jnp.where(move_y < 0, from_high, field))
    low = lax.ppermute(field[:, :, :, size_z - 1], "gz", ring("gz", 1))
    high = lax.ppermute(field[:, :, :, 0], "gz", ring("gz", -1))
    lane = lax.broadcasted_iota(jnp.int32, field.shape, 3)
    from_low = jnp.where(lane == 0, low[..., None], jnp.roll(field, 1, axis=3))
    from_high = jnp.where(lane == size_z - 1, high[..., None], jnp.roll(field, -1, axis=3))
    field = jnp.where(move_z > 0, from_low, jnp.where(move_z < 0, from_high, field))
    from_low = jnp.roll(field, 1, axis=1)
    from_high = jnp.roll(field, -1, axis=1)
    return jnp.where(move_x > 0, from_low, jnp.where(move_x < 0, from_high, field))


def reverse_pairs(rows, opposite):
    return jnp.concatenate([rows[int(o) : int(o) + 1] for o in opposite])


NEAR_HALVES = {4: [3, 2, 1, 0], 8: [6, 7, 4, 5, 2, 3, 0, 1]}


def butterfly_rounds(count, inner):
    rounds = []
    step = 1
    while step < inner:
        rounds.append([i ^ step for i in range(count)])
        step *= 2
    ring_size = count // inner
    step = 1
    while step < ring_size:
        if 2 * step == ring_size and ring_size in NEAR_HALVES:
            mirror = NEAR_HALVES[ring_size]
        else:
            mirror = [j ^ step for j in range(ring_size)]
        rounds.append([mirror[i // inner] * inner + i % inner for i in range(count)])
        step *= 2
    return rounds


def butterfly_sum(values, axes, deferred):
    round_index = 0
    for axis, inner in axes:
        for targets in butterfly_rounds(lax.axis_size(axis), inner):
            values = values + lax.ppermute(values, axis, list(enumerate(targets)))
            if round_index < len(deferred):
                values = deferred[round_index](values)
            round_index += 1
    return values


def per_device(populations, solid_mask, flow_rates, species_rates, cotangents):
    velocity, weights, opposite, ortho = lattice_tables()
    highest = lax.Precision.HIGHEST
    rows = populations.shape[0]
    groups = rows // 7
    is_flow = lax.axis_index("sec") == 0
    fluid = (solid_mask == 0)[None]

    flow = populations[:19]
    vx, vy, vz = (column(velocity[:, d]) for d in range(3))
    density = jnp.sum(flow, 0)
    own_motion = jnp.stack(
        [jnp.sum(flow * vx, 0), jnp.sum(flow * vy, 0), jnp.sum(flow * vz, 0)]
    ) / density[None]
    sent_motion = lax.ppermute(own_motion, "sec", [(0, 1)])

    small_weights = column([0.25] + [0.125] * 6)
    grouped = populations.reshape((groups, 7) + populations.shape[1:])
    species_r = species_rates.reshape((groups, 1, 1, 1, 1))
    concentration = jnp.sum(grouped, 1)
    sx, sy, sz = (column(velocity[:7, d])[None] for d in range(3))
    projected_small = (
        sent_motion[0][None] * sx[0] + sent_motion[1][None] * sy[0] + sent_motion[2][None] * sz[0]
    )
    factor = small_weights * (1.0 + 4.0 * projected_small)
    species_eq = factor[None] * concentration[:, None]
    species_gap = grouped - species_eq
    species_relaxed = grouped - species_r * species_gap
    species_bounce = jnp.swapaxes(reverse_pairs(jnp.swapaxes(grouped, 0, 1), opposite[:7]), 0, 1)
    species_post = jnp.where(fluid[None], species_relaxed, species_bounce).reshape(populations.shape)

    q_table = jnp.asarray(ortho, jnp.float32)
    relax = jnp.concatenate([jnp.zeros((4,), flow_rates.dtype), flow_rates]).reshape(19, 1, 1, 1)
    w = column(weights)
    projected = vx * own_motion[0][None] + vy * own_motion[1][None] + vz * own_motion[2][None]
    squared = jnp.sum(own_motion * own_motion, 0)
    poly = w * (1.0 + 3.0 * projected + 4.5 * projected * projected - 1.5 * squared[None])
    equilibrium = density[None] * poly
    moments = jnp.einsum("ji,jxyz->ixyz", q_table, flow - equilibrium, precision=highest)
    flow_relaxed = flow - jnp.einsum("ij,jxyz->ixyz", q_table, relax * moments, precision=highest)
    flow_post = jnp.where(fluid, flow_relaxed, reverse_pairs(flow, opposite))
    filler = jnp.zeros((rows - 19,) + populations.shape[1:], jnp.float32)
    post = jnp.where(is_flow, jnp.concatenate([flow_post, filler]), species_post)

    flow_moves = np.concatenate([velocity, np.zeros((rows - 19, 3))])
    species_moves = np.tile(velocity[:7], (groups, 1))
    both_moves = []
    for d in range(3):
        table = jnp.where(is_flow, column(flow_moves[:, d]), column(species_moves[:, d]))
        both_moves.append(jnp.concatenate([table, -table]))
    both = shift_rows(jnp.concatenate([post, cotangents]), both_moves)
    moved = both[:rows]
    returned = both[rows:]
    moved = jnp.where(is_flow, jnp.concatenate([moved[:19], filler]), moved)

    back_species = returned.reshape(grouped.shape)
    back_flow = returned[:19]
    species_rate_grad = -jnp.sum(
        jnp.where(fluid[None], back_species * species_gap, 0.0), axis=(1, 2, 3, 4)
    )
    back_moments = jnp.einsum("ji,jxyz->ixyz", q_table, back_flow, precision=highest)
    flow_rate_grad = -jnp.sum(
        jnp.where(fluid, back_moments * moments, 0.0)[4:], axis=(1, 2, 3)
    )
    local_rates = jnp.where(
        is_flow,
        jnp.concatenate([flow_rate_grad, jnp.zeros((groups,), jnp.float32)]),
        jnp.concatenate([jnp.zeros((15,), jnp.float32), species_rate_grad]),
    )

    later = {}

    def flow_adjoint(values):
        values, (back_flow_, back_moments_) = lax.optimization_barrier(
            (values, (back_flow, back_moments))
        )
        through_eq = jnp.einsum("ij,jxyz->ixyz", q_table, relax * back_moments_, precision=highest)
        density_grad = jnp.sum(through_eq * poly, 0)
        hw = through_eq * w
        hw_sum = jnp.sum(hw, 0)
        hwp = hw * (3.0 + 9.0 * projected)
        later["motion_grad"] = density[None] * (
            jnp.stack([jnp.sum(hwp * vx, 0), jnp.sum(hwp * vy, 0), jnp.sum(hwp * vz, 0)])
            - 3.0 * own_motion * hw_sum[None]
        )
        later["flow_base"] = back_flow_ - through_eq + density_grad[None]
        return values

    def species_adjoint(values):
        values, back = lax.optimization_barrier((values, back_species))
        weighted_back = back * small_weights[None]
        species_motion_grad = 4.0 * jnp.sum(
            species_r * concentration[:, None] * jnp.stack(
                [jnp.sum(weighted_back * sx, 1), jnp.sum(weighted_back * sy, 1), jnp.sum(weighted_back * sz, 1)], 1
            ),
            0,
        )
        later["species_motion_grad"] = jnp.where(fluid, species_motion_grad, 0.0)
        species_t = jnp.sum(back * factor[None], 1)
        species_grad_fluid = (1.0 - species_r) * back + species_r * species_t[:, None]
        bounced = jnp.swapaxes(reverse_pairs(jnp.swapaxes(back, 0, 1), opposite[:7]), 0, 1)
        later["species_grad"] = jnp.where(fluid[None], species_grad_fluid, bounced).reshape(
            populations.shape
        )
        return values

    partial_rates = butterfly_sum(local_rates, (("gy", 4),), [flow_adjoint, species_adjoint])
    plane = populations.shape[1:]
    rate_plane = jnp.zeros(plane, jnp.float32).at[0, 0, : partial_rates.shape[0]].set(partial_rates)
    payload = jnp.concatenate([later["species_motion_grad"], rate_plane[None]])
    other = lax.ppermute(payload, "sec", [(0, 1), (1, 0)])
    partial_rates = partial_rates + other[3, 0, 0, : partial_rates.shape[0]]

    def flow_gradient(values):
        values, received = lax.optimization_barrier((values, other[:3]))
        motion_grad = jnp.where(fluid, later["motion_grad"] + received, 0.0)
        along = vx * motion_grad[0][None] + vy * motion_grad[1][None] + vz * motion_grad[2][None]
        extra = (along - jnp.sum(own_motion * motion_grad, 0)[None]) / density[None]
        flow_grad = jnp.where(
            fluid, later["flow_base"] + extra, reverse_pairs(back_flow, opposite)
        )
        later["grad_rows"] = jnp.where(
            is_flow, jnp.concatenate([flow_grad, filler]), later["species_grad"]
        )
        return values

    rate_grad = butterfly_sum(partial_rates, (("gz", 1),), [flow_gradient])
    grad_rows = later["grad_rows"]
    return (moved, grad_rows, rate_grad)


def solution(mesh):
    placed = (P("sec", None, "gy", "gz"), P(None, "gy", "gz"), P(), P(), P("sec", None, "gy", "gz"))
    return jax.shard_map(
        per_device,
        mesh=mesh,
        in_specs=placed,
        out_specs=(P("sec", None, "gy", "gz"), P("sec", None, "gy", "gz"), P()),
        check_vma=False,
    )
```

```python
import jax
import jax.numpy as jnp
import numpy as np
from jax import lax
from jax.sharding import PartitionSpec as P


def orthonormal_columns(basis):
    result = []
    for column in range(basis.shape[1]):
        vector = basis[:, column] * 1.0
        for repeat in range(2):
            for earlier in result:
                vector = vector - np.sum(earlier * vector) * earlier
        vector = vector / np.sqrt(np.sum(vector * vector))
        result.append(vector)
    return np.stack(result, 1)


def lattice_tables():
    axis_moves = [(1, 0, 0), (-1, 0, 0), (0, 1, 0), (0, -1, 0), (0, 0, 1), (0, 0, -1)]
    edge_moves = []
    for first, second in ((0, 1), (0, 2), (1, 2)):
        for sign_first in (1, -1):
            for sign_second in (1, -1):
                move = [0, 0, 0]
                move[first] = sign_first
                move[second] = sign_second
                edge_moves.append(tuple(move))
    velocity = np.array([(0, 0, 0)] + axis_moves + edge_moves) * 1.0
    weights = np.array([1.0 / 3.0] + [1.0 / 18.0] * 6 + [1.0 / 36.0] * 12)
    opposite = np.array(
        [int(np.argmin(np.abs(velocity + velocity[channel]).sum(1))) for channel in range(19)]
    )
    along_x = velocity[:, 0]
    along_y = velocity[:, 1]
    along_z = velocity[:, 2]
    basis = np.stack(
        [
            np.ones(19),
            along_x,
            along_y,
            along_z,
            along_x**2,
            along_y**2,
            along_z**2,
            along_x * along_y,
            along_y * along_z,
            along_x * along_z,
            along_x * along_y**2,
            along_x * along_z**2,
            along_y * along_x**2,
            along_y * along_z**2,
            along_z * along_x**2,
            along_z * along_y**2,
            along_x**2 * along_y**2,
            along_x**2 * along_z**2,
            along_y**2 * along_z**2,
        ],
        1,
    )
    ortho = orthonormal_columns(basis)
    return (velocity, weights, opposite, ortho)


def column(values):
    return jnp.asarray(np.asarray(values, np.float32).reshape(-1, 1, 1, 1))


def ring(axis, step):
    count = lax.axis_size(axis)
    return [(i, (i + step) % count) for i in range(count)]


def shift_rows(field, moves):
    move_x, move_y, move_z = moves
    size_y, size_z = field.shape[2], field.shape[3]
    low = lax.ppermute(field[:, :, size_y - 1 :, :], "gy", ring("gy", 1))
    high = lax.ppermute(field[:, :, :1, :], "gy", ring("gy", -1))
    from_low = jnp.concatenate([low, field[:, :, : size_y - 1, :]], axis=2)
    from_high = jnp.concatenate([field[:, :, 1:, :], high], axis=2)
    field = jnp.where(move_y > 0, from_low, jnp.where(move_y < 0, from_high, field))
    low = lax.ppermute(field[:, :, :, size_z - 1], "gz", ring("gz", 1))
    high = lax.ppermute(field[:, :, :, 0], "gz", ring("gz", -1))
    lane = lax.broadcasted_iota(jnp.int32, field.shape, 3)
    from_low = jnp.where(lane == 0, low[..., None], jnp.roll(field, 1, axis=3))
    from_high = jnp.where(lane == size_z - 1, high[..., None], jnp.roll(field, -1, axis=3))
    field = jnp.where(move_z > 0, from_low, jnp.where(move_z < 0, from_high, field))
    from_low = jnp.roll(field, 1, axis=1)
    from_high = jnp.roll(field, -1, axis=1)
    return jnp.where(move_x > 0, from_low, jnp.where(move_x < 0, from_high, field))


def reverse_pairs(rows, opposite):
    return jnp.concatenate([rows[int(o) : int(o) + 1] for o in opposite])


NEAR_HALVES = {4: [3, 2, 1, 0], 8: [6, 7, 4, 5, 2, 3, 0, 1]}


def butterfly_rounds(count, inner):
    rounds = []
    step = 1
    while step < inner:
        rounds.append([i ^ step for i in range(count)])
        step *= 2
    ring_size = count // inner
    step = 1
    while step < ring_size:
        if 2 * step == ring_size and ring_size in NEAR_HALVES:
            mirror = NEAR_HALVES[ring_size]
        else:
            mirror = [j ^ step for j in range(ring_size)]
        rounds.append([mirror[i // inner] * inner + i % inner for i in range(count)])
        step *= 2
    return rounds


def butterfly_sum(values, axes, deferred):
    round_index = 0
    for axis, inner in axes:
        for targets in butterfly_rounds(lax.axis_size(axis), inner):
            values = values + lax.ppermute(values, axis, list(enumerate(targets)))
            if round_index < len(deferred):
                values = deferred[round_index](values)
            round_index += 1
    return values


def per_device(populations, solid_mask, flow_rates, species_rates, cotangents):
    velocity, weights, opposite, ortho = lattice_tables()
    highest = lax.Precision.HIGHEST
    rows = populations.shape[0]
    groups = rows // 7
    is_flow = lax.axis_index("sec") == 0
    fluid = (solid_mask == 0)[None]

    flow = populations[:19]
    vx, vy, vz = (column(velocity[:, d]) for d in range(3))
    density = jnp.sum(flow, 0)
    own_motion = jnp.stack(
        [jnp.sum(flow * vx, 0), jnp.sum(flow * vy, 0), jnp.sum(flow * vz, 0)]
    ) / density[None]
    sent_motion = lax.ppermute(own_motion, "sec", [(0, 1)])
    motion = jnp.where(is_flow, own_motion, sent_motion)

    small_weights = column([0.25] + [0.125] * 6)
    grouped = populations.reshape((groups, 7) + populations.shape[1:])
    species_r = species_rates.reshape((groups, 1, 1, 1, 1))
    concentration = jnp.sum(grouped, 1)
    sx, sy, sz = (column(velocity[:7, d])[None] for d in range(3))
    projected_small = motion[0][None] * sx[0] + motion[1][None] * sy[0] + motion[2][None] * sz[0]
    factor = small_weights * (1.0 + 4.0 * projected_small)
    species_eq = factor[None] * concentration[:, None]
    species_gap = grouped - species_eq
    species_relaxed = grouped - species_r * species_gap
    species_bounce = jnp.swapaxes(reverse_pairs(jnp.swapaxes(grouped, 0, 1), opposite[:7]), 0, 1)
    species_post = jnp.where(fluid[None], species_relaxed, species_bounce).reshape(populations.shape)

    q_table = jnp.asarray(ortho, jnp.float32)
    relax = jnp.concatenate([jnp.zeros((4,), flow_rates.dtype), flow_rates]).reshape(19, 1, 1, 1)
    w = column(weights)
    projected = vx * motion[0][None] + vy * motion[1][None] + vz * motion[2][None]
    squared = jnp.sum(motion * motion, 0)
    poly = w * (1.0 + 3.0 * projected + 4.5 * projected * projected - 1.5 * squared[None])
    equilibrium = density[None] * poly
    moments = jnp.einsum("ji,jxyz->ixyz", q_table, flow - equilibrium, precision=highest)
    flow_relaxed = flow - jnp.einsum("ij,jxyz->ixyz", q_table, relax * moments, precision=highest)
    flow_post = jnp.where(fluid, flow_relaxed, reverse_pairs(flow, opposite))
    filler = jnp.zeros((rows - 19,) + populations.shape[1:], jnp.float32)
    post = jnp.where(is_flow, jnp.concatenate([flow_post, filler]), species_post)

    flow_moves = np.concatenate([velocity, np.zeros((rows - 19, 3))])
    species_moves = np.tile(velocity[:7], (groups, 1))
    both_moves = []
    for d in range(3):
        table = jnp.where(is_flow, column(flow_moves[:, d]), column(species_moves[:, d]))
        both_moves.append(jnp.concatenate([table, -table]))
    both = shift_rows(jnp.concatenate([post, cotangents]), both_moves)
    moved = both[:rows]
    returned = both[rows:]
    moved = jnp.where(is_flow, jnp.concatenate([moved[:19], filler]), moved)

    back_species = returned.reshape(grouped.shape)
    back_flow = returned[:19]
    species_rate_grad = -jnp.sum(
        jnp.where(fluid[None], back_species * species_gap, 0.0), axis=(1, 2, 3, 4)
    )
    back_moments = jnp.einsum("ji,jxyz->ixyz", q_table, back_flow, precision=highest)
    flow_rate_grad = -jnp.sum(
        jnp.where(fluid, back_moments * moments, 0.0)[4:], axis=(1, 2, 3)
    )
    local_rates = jnp.where(
        is_flow,
        jnp.concatenate([flow_rate_grad, jnp.zeros((groups,), jnp.float32)]),
        jnp.concatenate([jnp.zeros((15,), jnp.float32), species_rate_grad]),
    )

    later = {}

    def flow_adjoint(values):
        values, (back_flow_, back_moments_) = lax.optimization_barrier(
            (values, (back_flow, back_moments))
        )
        through_eq = jnp.einsum("ij,jxyz->ixyz", q_table, relax * back_moments_, precision=highest)
        density_grad = jnp.sum(through_eq * poly, 0)
        hw = through_eq * w
        hw_sum = jnp.sum(hw, 0)
        hwp = hw * (3.0 + 9.0 * projected)
        later["motion_grad"] = density[None] * (
            jnp.stack([jnp.sum(hwp * vx, 0), jnp.sum(hwp * vy, 0), jnp.sum(hwp * vz, 0)])
            - 3.0 * motion * hw_sum[None]
        )
        later["flow_base"] = back_flow_ - through_eq + density_grad[None]
        return values

    def species_adjoint(values):
        values, back = lax.optimization_barrier((values, back_species))
        weighted_back = back * small_weights[None]
        species_motion_grad = 4.0 * jnp.sum(
            species_r * concentration[:, None] * jnp.stack(
                [jnp.sum(weighted_back * sx, 1), jnp.sum(weighted_back * sy, 1), jnp.sum(weighted_back * sz, 1)], 1
            ),
            0,
        )
        later["species_motion_grad"] = jnp.where(fluid, species_motion_grad, 0.0)
        species_t = jnp.sum(back * factor[None], 1)
        species_grad_fluid = (1.0 - species_r) * back + species_r * species_t[:, None]
        bounced = jnp.swapaxes(reverse_pairs(jnp.swapaxes(back, 0, 1), opposite[:7]), 0, 1)
        later["species_grad"] = jnp.where(fluid[None], species_grad_fluid, bounced).reshape(
            populations.shape
        )
        return values

    gy_rounds = butterfly_rounds(lax.axis_size("gy"), 4)
    partial_rates = local_rates
    for index, targets in enumerate(gy_rounds[:-1]):
        partial_rates = partial_rates + lax.ppermute(partial_rates, "gy", list(enumerate(targets)))
        partial_rates = [flow_adjoint, species_adjoint][index](partial_rates) if index < 2 else partial_rates
    mirror = gy_rounds[-1]
    count = lax.axis_size("gy")
    plane = populations.shape[1:]
    rate_plane = jnp.zeros(plane, jnp.float32).at[0, 0, : partial_rates.shape[0]].set(partial_rates)
    payload = jnp.concatenate([later["species_motion_grad"], rate_plane[None]])
    other = lax.ppermute(payload, "sec", [(0, 1), (1, 0)])
    across_y = lax.ppermute(partial_rates, "gy", list(enumerate(mirror)))
    diagonal = lax.ppermute(
        partial_rates,
        ("sec", "gy"),
        [(sec * count + i, (1 - sec) * count + mirror[i]) for sec in range(2) for i in range(count)],
    )
    partial_rates = partial_rates + other[3, 0, 0, : partial_rates.shape[0]] + across_y + diagonal

    def flow_gradient(values):
        values, received = lax.optimization_barrier((values, other[:3]))
        motion_grad = jnp.where(fluid, later["motion_grad"] + received, 0.0)
        along = vx * motion_grad[0][None] + vy * motion_grad[1][None] + vz * motion_grad[2][None]
        extra = (along - jnp.sum(motion * motion_grad, 0)[None]) / density[None]
        flow_grad = jnp.where(
            fluid, later["flow_base"] + extra, reverse_pairs(back_flow, opposite)
        )
        later["grad_rows"] = jnp.where(
            is_flow, jnp.concatenate([flow_grad, filler]), later["species_grad"]
        )
        return values

    rate_grad = butterfly_sum(partial_rates, (("gz", 1),), [flow_gradient])
    grad_rows = later["grad_rows"]
    return (moved, grad_rows, rate_grad)


def solution(mesh):
    placed = (P("sec", None, "gy", "gz"), P(None, "gy", "gz"), P(), P(), P("sec", None, "gy", "gz"))
    return jax.shard_map(
        per_device,
        mesh=mesh,
        in_specs=placed,
        out_specs=(P("sec", None, "gy", "gz"), P("sec", None, "gy", "gz"), P()),
        check_vma=False,
    )
```

```python
import jax
import jax.numpy as jnp
import numpy as np
from jax import lax
from jax.sharding import PartitionSpec as P


def orthonormal_columns(basis):
    result = []
    for column in range(basis.shape[1]):
        vector = basis[:, column] * 1.0
        for repeat in range(2):
            for earlier in result:
                vector = vector - np.sum(earlier * vector) * earlier
        vector = vector / np.sqrt(np.sum(vector * vector))
        result.append(vector)
    return np.stack(result, 1)


def lattice_tables():
    axis_moves = [(1, 0, 0), (-1, 0, 0), (0, 1, 0), (0, -1, 0), (0, 0, 1), (0, 0, -1)]
    edge_moves = []
    for first, second in ((0, 1), (0, 2), (1, 2)):
        for sign_first in (1, -1):
            for sign_second in (1, -1):
                move = [0, 0, 0]
                move[first] = sign_first
                move[second] = sign_second
                edge_moves.append(tuple(move))
    velocity = np.array([(0, 0, 0)] + axis_moves + edge_moves) * 1.0
    weights = np.array([1.0 / 3.0] + [1.0 / 18.0] * 6 + [1.0 / 36.0] * 12)
    opposite = np.array(
        [int(np.argmin(np.abs(velocity + velocity[channel]).sum(1))) for channel in range(19)]
    )
    along_x = velocity[:, 0]
    along_y = velocity[:, 1]
    along_z = velocity[:, 2]
    basis = np.stack(
        [
            np.ones(19),
            along_x,
            along_y,
            along_z,
            along_x**2,
            along_y**2,
            along_z**2,
            along_x * along_y,
            along_y * along_z,
            along_x * along_z,
            along_x * along_y**2,
            along_x * along_z**2,
            along_y * along_x**2,
            along_y * along_z**2,
            along_z * along_x**2,
            along_z * along_y**2,
            along_x**2 * along_y**2,
            along_x**2 * along_z**2,
            along_y**2 * along_z**2,
        ],
        1,
    )
    ortho = orthonormal_columns(basis)
    return (velocity, weights, opposite, ortho)


def column(values):
    return jnp.asarray(np.asarray(values, np.float32).reshape(-1, 1, 1, 1))


def ring(axis, step):
    count = lax.axis_size(axis)
    return [(i, (i + step) % count) for i in range(count)]


def shift_rows(field, moves):
    move_x, move_y, move_z = moves
    size_y, size_z = field.shape[2], field.shape[3]
    low = lax.ppermute(field[:, :, size_y - 1 :, :], "gy", ring("gy", 1))
    high = lax.ppermute(field[:, :, :1, :], "gy", ring("gy", -1))
    from_low = jnp.concatenate([low, field[:, :, : size_y - 1, :]], axis=2)
    from_high = jnp.concatenate([field[:, :, 1:, :], high], axis=2)
    field = jnp.where(move_y > 0, from_low, jnp.where(move_y < 0, from_high, field))
    lane = lax.broadcasted_iota(jnp.int32, field.shape, 3)
    last = jnp.sum(jnp.where(lane == size_z - 1, field, 0.0), axis=3)
    first = jnp.sum(jnp.where(lane == 0, field, 0.0), axis=3)
    low = lax.ppermute(last, "gz", ring("gz", 1))
    high = lax.ppermute(first, "gz", ring("gz", -1))
    from_low = jnp.where(lane == 0, low[..., None], jnp.roll(field, 1, axis=3))
    from_high = jnp.where(lane == size_z - 1, high[..., None], jnp.roll(field, -1, axis=3))
    field = jnp.where(move_z > 0, from_low, jnp.where(move_z < 0, from_high, field))
    from_low = jnp.roll(field, 1, axis=1)
    from_high = jnp.roll(field, -1, axis=1)
    return jnp.where(move_x > 0, from_low, jnp.where(move_x < 0, from_high, field))


def reverse_pairs(rows, opposite):
    return jnp.concatenate([rows[int(o) : int(o) + 1] for o in opposite])


NEAR_HALVES = {4: [3, 2, 1, 0], 8: [6, 7, 4, 5, 2, 3, 0, 1]}


def butterfly_rounds(count, inner):
    rounds = []
    step = 1
    while step < inner:
        rounds.append([i ^ step for i in range(count)])
        step *= 2
    ring_size = count // inner
    step = 1
    while step < ring_size:
        if 2 * step == ring_size and ring_size in NEAR_HALVES:
            mirror = NEAR_HALVES[ring_size]
        else:
            mirror = [j ^ step for j in range(ring_size)]
        rounds.append([mirror[i // inner] * inner + i % inner for i in range(count)])
        step *= 2
    return rounds


def butterfly_sum(values, axes, deferred):
    round_index = 0
    for axis, inner in axes:
        for targets in butterfly_rounds(lax.axis_size(axis), inner):
            values = values + lax.ppermute(values, axis, list(enumerate(targets)))
            if round_index < len(deferred):
                values = deferred[round_index](values)
            round_index += 1
    return values


def per_device(populations, solid_mask, flow_rates, species_rates, cotangents):
    velocity, weights, opposite, ortho = lattice_tables()
    highest = lax.Precision.HIGHEST
    rows = populations.shape[0]
    groups = rows // 7
    is_flow = lax.axis_index("sec") == 0
    fluid = (solid_mask == 0)[None]

    flow = populations[:19]
    vx, vy, vz = (column(velocity[:, d]) for d in range(3))
    density = jnp.sum(flow, 0)
    own_motion = jnp.stack(
        [jnp.sum(flow * vx, 0), jnp.sum(flow * vy, 0), jnp.sum(flow * vz, 0)]
    ) / density[None]
    sent_motion = lax.ppermute(own_motion, "sec", [(0, 1)])
    motion = jnp.where(is_flow, own_motion, sent_motion)

    small_weights = column([0.25] + [0.125] * 6)
    grouped = populations.reshape((groups, 7) + populations.shape[1:])
    species_r = species_rates.reshape((groups, 1, 1, 1, 1))
    concentration = jnp.sum(grouped, 1)
    sx, sy, sz = (column(velocity[:7, d])[None] for d in range(3))
    projected_small = motion[0][None] * sx[0] + motion[1][None] * sy[0] + motion[2][None] * sz[0]
    factor = small_weights * (1.0 + 4.0 * projected_small)
    species_eq = factor[None] * concentration[:, None]
    species_gap = grouped - species_eq
    species_relaxed = grouped - species_r * species_gap
    species_bounce = jnp.swapaxes(reverse_pairs(jnp.swapaxes(grouped, 0, 1), opposite[:7]), 0, 1)
    species_post = jnp.where(fluid[None], species_relaxed, species_bounce).reshape(populations.shape)

    q_table = jnp.asarray(ortho, jnp.float32)
    relax = jnp.concatenate([jnp.zeros((4,), flow_rates.dtype), flow_rates]).reshape(19, 1, 1, 1)
    w = column(weights)
    projected = vx * motion[0][None] + vy * motion[1][None] + vz * motion[2][None]
    squared = jnp.sum(motion * motion, 0)
    poly = w * (1.0 + 3.0 * projected + 4.5 * projected * projected - 1.5 * squared[None])
    equilibrium = density[None] * poly
    moments = jnp.einsum("ji,jxyz->ixyz", q_table, flow - equilibrium, precision=highest)
    flow_relaxed = flow - jnp.einsum("ij,jxyz->ixyz", q_table, relax * moments, precision=highest)
    flow_post = jnp.where(fluid, flow_relaxed, reverse_pairs(flow, opposite))
    filler = jnp.zeros((rows - 19,) + populations.shape[1:], jnp.float32)
    post = jnp.where(is_flow, jnp.concatenate([flow_post, filler]), species_post)

    flow_moves = np.concatenate([velocity, np.zeros((rows - 19, 3))])
    species_moves = np.tile(velocity[:7], (groups, 1))
    both_moves = []
    for d in range(3):
        table = jnp.where(is_flow, column(flow_moves[:, d]), column(species_moves[:, d]))
        both_moves.append(jnp.concatenate([table, -table]))
    both = shift_rows(jnp.concatenate([post, cotangents]), both_moves)
    moved = both[:rows]
    returned = both[rows:]
    moved = jnp.where(is_flow, jnp.concatenate([moved[:19], filler]), moved)

    back_species = returned.reshape(grouped.shape)
    back_flow = returned[:19]
    species_rate_grad = -jnp.sum(
        jnp.where(fluid[None], back_species * species_gap, 0.0), axis=(1, 2, 3, 4)
    )
    back_moments = jnp.einsum("ji,jxyz->ixyz", q_table, back_flow, precision=highest)
    flow_rate_grad = -jnp.sum(
        jnp.where(fluid, back_moments * moments, 0.0)[4:], axis=(1, 2, 3)
    )
    local_rates = jnp.where(
        is_flow,
        jnp.concatenate([flow_rate_grad, jnp.zeros((groups,), jnp.float32)]),
        jnp.concatenate([jnp.zeros((15,), jnp.float32), species_rate_grad]),
    )

    later = {}

    def flow_adjoint(values):
        values, (back_flow_, back_moments_) = lax.optimization_barrier(
            (values, (back_flow, back_moments))
        )
        through_eq = jnp.einsum("ij,jxyz->ixyz", q_table, relax * back_moments_, precision=highest)
        density_grad = jnp.sum(through_eq * poly, 0)
        hw = through_eq * w
        hw_sum = jnp.sum(hw, 0)
        hwp = hw * (3.0 + 9.0 * projected)
        later["motion_grad"] = density[None] * (
            jnp.stack([jnp.sum(hwp * vx, 0), jnp.sum(hwp * vy, 0), jnp.sum(hwp * vz, 0)])
            - 3.0 * motion * hw_sum[None]
        )
        later["flow_base"] = back_flow_ - through_eq + density_grad[None]
        return values

    def species_adjoint(values):
        values, back = lax.optimization_barrier((values, back_species))
        weighted_back = back * small_weights[None]
        species_motion_grad = 4.0 * jnp.sum(
            species_r * concentration[:, None] * jnp.stack(
                [jnp.sum(weighted_back * sx, 1), jnp.sum(weighted_back * sy, 1), jnp.sum(weighted_back * sz, 1)], 1
            ),
            0,
        )
        later["species_motion_grad"] = jnp.where(fluid, species_motion_grad, 0.0)
        species_t = jnp.sum(back * factor[None], 1)
        species_grad_fluid = (1.0 - species_r) * back + species_r * species_t[:, None]
        bounced = jnp.swapaxes(reverse_pairs(jnp.swapaxes(back, 0, 1), opposite[:7]), 0, 1)
        later["species_grad"] = jnp.where(fluid[None], species_grad_fluid, bounced).reshape(
            populations.shape
        )
        return values

    partial_rates = butterfly_sum(local_rates, (("gy", 4),), [flow_adjoint, species_adjoint])
    plane = populations.shape[1:]
    rate_plane = jnp.zeros(plane, jnp.float32).at[0, 0, : partial_rates.shape[0]].set(partial_rates)
    payload = jnp.concatenate([later["species_motion_grad"], rate_plane[None]])
    other = lax.ppermute(payload, "sec", [(0, 1), (1, 0)])
    partial_rates = partial_rates + other[3, 0, 0, : partial_rates.shape[0]]

    def flow_gradient(values):
        values, received = lax.optimization_barrier((values, other[:3]))
        motion_grad = jnp.where(fluid, later["motion_grad"] + received, 0.0)
        along = vx * motion_grad[0][None] + vy * motion_grad[1][None] + vz * motion_grad[2][None]
        extra = (along - jnp.sum(motion * motion_grad, 0)[None]) / density[None]
        flow_grad = jnp.where(
            fluid, later["flow_base"] + extra, reverse_pairs(back_flow, opposite)
        )
        later["grad_rows"] = jnp.where(
            is_flow, jnp.concatenate([flow_grad, filler]), later["species_grad"]
        )
        return values

    rate_grad = butterfly_sum(partial_rates, (("gz", 1),), [flow_gradient])
    grad_rows = later["grad_rows"]
    return (moved, grad_rows, rate_grad)


def solution(mesh):
    placed = (P("sec", None, "gy", "gz"), P(None, "gy", "gz"), P(), P(), P("sec", None, "gy", "gz"))
    return jax.shard_map(
        per_device,
        mesh=mesh,
        in_specs=placed,
        out_specs=(P("sec", None, "gy", "gz"), P("sec", None, "gy", "gz"), P()),
        check_vma=False,
    )
```

```python
import jax
import jax.numpy as jnp
import numpy as np
from jax import lax
from jax.sharding import PartitionSpec as P


def orthonormal_columns(basis):
    result = []
    for column in range(basis.shape[1]):
        vector = basis[:, column] * 1.0
        for repeat in range(2):
            for earlier in result:
                vector = vector - np.sum(earlier * vector) * earlier
        vector = vector / np.sqrt(np.sum(vector * vector))
        result.append(vector)
    return np.stack(result, 1)


def lattice_tables():
    axis_moves = [(1, 0, 0), (-1, 0, 0), (0, 1, 0), (0, -1, 0), (0, 0, 1), (0, 0, -1)]
    edge_moves = []
    for first, second in ((0, 1), (0, 2), (1, 2)):
        for sign_first in (1, -1):
            for sign_second in (1, -1):
                move = [0, 0, 0]
                move[first] = sign_first
                move[second] = sign_second
                edge_moves.append(tuple(move))
    velocity = np.array([(0, 0, 0)] + axis_moves + edge_moves) * 1.0
    weights = np.array([1.0 / 3.0] + [1.0 / 18.0] * 6 + [1.0 / 36.0] * 12)
    opposite = np.array(
        [int(np.argmin(np.abs(velocity + velocity[channel]).sum(1))) for channel in range(19)]
    )
    along_x = velocity[:, 0]
    along_y = velocity[:, 1]
    along_z = velocity[:, 2]
    basis = np.stack(
        [
            np.ones(19),
            along_x,
            along_y,
            along_z,
            along_x**2,
            along_y**2,
            along_z**2,
            along_x * along_y,
            along_y * along_z,
            along_x * along_z,
            along_x * along_y**2,
            along_x * along_z**2,
            along_y * along_x**2,
            along_y * along_z**2,
            along_z * along_x**2,
            along_z * along_y**2,
            along_x**2 * along_y**2,
            along_x**2 * along_z**2,
            along_y**2 * along_z**2,
        ],
        1,
    )
    ortho = orthonormal_columns(basis)
    return (velocity, weights, opposite, ortho)


def column(values):
    return jnp.asarray(np.asarray(values, np.float32).reshape(-1, 1, 1, 1))


def ring(axis, step):
    count = lax.axis_size(axis)
    return [(i, (i + step) % count) for i in range(count)]


def shift_rows(field, moves):
    move_x, move_y, move_z = moves
    size_y, size_z = field.shape[2], field.shape[3]
    low = lax.ppermute(field[:, :, size_y - 1 :, :], "gy", ring("gy", 1))
    high = lax.ppermute(field[:, :, :1, :], "gy", ring("gy", -1))
    from_low = jnp.concatenate([low, field[:, :, : size_y - 1, :]], axis=2)
    from_high = jnp.concatenate([field[:, :, 1:, :], high], axis=2)
    field = jnp.where(move_y > 0, from_low, jnp.where(move_y < 0, from_high, field))
    lane = lax.broadcasted_iota(jnp.int32, field.shape, 3)
    last = jnp.sum(jnp.where(lane == size_z - 1, field, 0.0), axis=3)
    first = jnp.sum(jnp.where(lane == 0, field, 0.0), axis=3)
    low = lax.ppermute(last, "gz", ring("gz", 1))
    high = lax.ppermute(first, "gz", ring("gz", -1))
    from_low = jnp.where(lane == 0, low[..., None], jnp.roll(field, 1, axis=3))
    from_high = jnp.where(lane == size_z - 1, high[..., None], jnp.roll(field, -1, axis=3))
    field = jnp.where(move_z > 0, from_low, jnp.where(move_z < 0, from_high, field))
    from_low = jnp.roll(field, 1, axis=1)
    from_high = jnp.roll(field, -1, axis=1)
    return jnp.where(move_x > 0, from_low, jnp.where(move_x < 0, from_high, field))


def reverse_pairs(rows, opposite):
    return jnp.concatenate([rows[int(o) : int(o) + 1] for o in opposite])


NEAR_HALVES = {4: [3, 2, 1, 0], 8: [6, 7, 4, 5, 2, 3, 0, 1]}


def butterfly_rounds(count, inner):
    rounds = []
    step = 1
    while step < inner:
        rounds.append([i ^ step for i in range(count)])
        step *= 2
    ring_size = count // inner
    step = 1
    while step < ring_size:
        if 2 * step == ring_size and ring_size in NEAR_HALVES:
            mirror = NEAR_HALVES[ring_size]
        else:
            mirror = [j ^ step for j in range(ring_size)]
        rounds.append([mirror[i // inner] * inner + i % inner for i in range(count)])
        step *= 2
    return rounds


def butterfly_sum(values, axes, deferred):
    round_index = 0
    for axis, inner in axes:
        for targets in butterfly_rounds(lax.axis_size(axis), inner):
            values = values + lax.ppermute(values, axis, list(enumerate(targets)))
            if round_index < len(deferred):
                values = deferred[round_index](values)
            round_index += 1
    return values


def per_device(populations, solid_mask, flow_rates, species_rates, cotangents):
    velocity, weights, opposite, ortho = lattice_tables()
    highest = lax.Precision.HIGHEST
    rows = populations.shape[0]
    groups = rows // 7
    is_flow = lax.axis_index("sec") == 0
    fluid = (solid_mask == 0)[None]

    flow = populations[:19]
    vx, vy, vz = (column(velocity[:, d]) for d in range(3))
    density = jnp.sum(flow, 0)
    own_motion = jnp.stack(
        [jnp.sum(flow * vx, 0), jnp.sum(flow * vy, 0), jnp.sum(flow * vz, 0)]
    ) / density[None]
    sent_motion = lax.ppermute(own_motion, "sec", [(0, 1)])
    motion = jnp.where(is_flow, own_motion, sent_motion)

    small_weights = column([0.25] + [0.125] * 6)
    grouped = populations.reshape((groups, 7) + populations.shape[1:])
    species_r = species_rates.reshape((groups, 1, 1, 1, 1))
    concentration = jnp.sum(grouped, 1)
    sx, sy, sz = (column(velocity[:7, d])[None] for d in range(3))
    projected_small = motion[0][None] * sx[0] + motion[1][None] * sy[0] + motion[2][None] * sz[0]
    factor = small_weights * (1.0 + 4.0 * projected_small)
    species_eq = factor[None] * concentration[:, None]
    species_gap = grouped - species_eq
    species_relaxed = grouped - species_r * species_gap
    species_bounce = jnp.swapaxes(reverse_pairs(jnp.swapaxes(grouped, 0, 1), opposite[:7]), 0, 1)
    species_post = jnp.where(fluid[None], species_relaxed, species_bounce).reshape(populations.shape)

    q_table = jnp.asarray(ortho, jnp.float32)
    relax = jnp.concatenate([jnp.zeros((4,), flow_rates.dtype), flow_rates]).reshape(19, 1, 1, 1)
    w = column(weights)
    projected = vx * motion[0][None] + vy * motion[1][None] + vz * motion[2][None]
    squared = jnp.sum(motion * motion, 0)
    poly = w * (1.0 + 3.0 * projected + 4.5 * projected * projected - 1.5 * squared[None])
    equilibrium = density[None] * poly
    moments = jnp.einsum("ji,jxyz->ixyz", q_table, flow - equilibrium, precision=highest)
    flow_relaxed = flow - jnp.einsum("ij,jxyz->ixyz", q_table, relax * moments, precision=highest)
    flow_post = jnp.where(fluid, flow_relaxed, reverse_pairs(flow, opposite))
    filler = jnp.zeros((rows - 19,) + populations.shape[1:], jnp.float32)
    post = jnp.where(is_flow, jnp.concatenate([flow_post, filler]), species_post)

    flow_moves = np.concatenate([velocity, np.zeros((rows - 19, 3))])
    species_moves = np.tile(velocity[:7], (groups, 1))
    both_moves = []
    for d in range(3):
        table = jnp.where(is_flow, column(flow_moves[:, d]), column(species_moves[:, d]))
        both_moves.append(jnp.concatenate([table, -table]))
    both = shift_rows(jnp.concatenate([post, cotangents]), both_moves)
    moved = both[:rows]
    returned = both[rows:]
    moved = jnp.where(is_flow, jnp.concatenate([moved[:19], filler]), moved)

    back_species = returned.reshape(grouped.shape)
    back_flow = returned[:19]
    species_rate_grad = -jnp.sum(
        jnp.where(fluid[None], back_species * species_gap, 0.0), axis=(1, 2, 3, 4)
    )
    back_moments = jnp.einsum("ji,jxyz->ixyz", q_table, back_flow, precision=highest)
    flow_rate_grad = -jnp.sum(
        jnp.where(fluid, back_moments * moments, 0.0)[4:], axis=(1, 2, 3)
    )
    local_rates = jnp.where(
        is_flow,
        jnp.concatenate([flow_rate_grad, jnp.zeros((groups,), jnp.float32)]),
        jnp.concatenate([jnp.zeros((15,), jnp.float32), species_rate_grad]),
    )

    later = {}

    def flow_adjoint(values):
        values, (back_flow_, back_moments_) = lax.optimization_barrier(
            (values, (back_flow, back_moments))
        )
        through_eq = jnp.einsum("ij,jxyz->ixyz", q_table, relax * back_moments_, precision=highest)
        density_grad = jnp.sum(through_eq * poly, 0)
        hw = through_eq * w
        hw_sum = jnp.sum(hw, 0)
        hwp = hw * (3.0 + 9.0 * projected)
        later["motion_grad"] = density[None] * (
            jnp.stack([jnp.sum(hwp * vx, 0), jnp.sum(hwp * vy, 0), jnp.sum(hwp * vz, 0)])
            - 3.0 * motion * hw_sum[None]
        )
        later["flow_base"] = back_flow_ - through_eq + density_grad[None]
        return values

    def species_adjoint(values):
        values, back = lax.optimization_barrier((values, back_species))
        weighted_back = back * small_weights[None]
        species_motion_grad = 4.0 * jnp.sum(
            species_r * concentration[:, None] * jnp.stack(
                [jnp.sum(weighted_back * sx, 1), jnp.sum(weighted_back * sy, 1), jnp.sum(weighted_back * sz, 1)], 1
            ),
            0,
        )
        later["species_motion_grad"] = jnp.where(fluid, species_motion_grad, 0.0)
        species_t = jnp.sum(back * factor[None], 1)
        species_grad_fluid = (1.0 - species_r) * back + species_r * species_t[:, None]
        bounced = jnp.swapaxes(reverse_pairs(jnp.swapaxes(back, 0, 1), opposite[:7]), 0, 1)
        later["species_grad"] = jnp.where(fluid[None], species_grad_fluid, bounced).reshape(
            populations.shape
        )
        return values

    partial_rates = butterfly_sum(local_rates, (("gy", 4),), [flow_adjoint, species_adjoint])
    plane = populations.shape[1:]
    rate_plane = jnp.zeros(plane, jnp.float32).at[0, 0, : partial_rates.shape[0]].set(partial_rates)
    payload = jnp.concatenate([later["species_motion_grad"], rate_plane[None]])
    other = lax.ppermute(payload, "sec", [(0, 1), (1, 0)])
    partial_rates = partial_rates + other[3, 0, 0, : partial_rates.shape[0]]

    def flow_gradient(values):
        values, received = lax.optimization_barrier((values, other[:3]))
        motion_grad = jnp.where(fluid, later["motion_grad"] + received, 0.0)
        along = vx * motion_grad[0][None] + vy * motion_grad[1][None] + vz * motion_grad[2][None]
        extra = (along - jnp.sum(motion * motion_grad, 0)[None]) / density[None]
        flow_grad = jnp.where(
            fluid, later["flow_base"] + extra, reverse_pairs(back_flow, opposite)
        )
        later["grad_rows"] = jnp.where(
            is_flow, jnp.concatenate([flow_grad, filler]), later["species_grad"]
        )
        return values

    count_z = lax.axis_size("gz")
    rate_grad = partial_rates + lax.ppermute(partial_rates, "gz", [(i, i ^ 1) for i in range(count_z)])
    rate_grad = flow_gradient(rate_grad)
    rate_grad = rate_grad + sum(
        lax.ppermute(rate_grad, "gz", [(i, i ^ step) for i in range(count_z)]) for step in (2, 4, 6)
    )
    grad_rows = later["grad_rows"]
    return (moved, grad_rows, rate_grad)


def solution(mesh):
    placed = (P("sec", None, "gy", "gz"), P(None, "gy", "gz"), P(), P(), P("sec", None, "gy", "gz"))
    return jax.shard_map(
        per_device,
        mesh=mesh,
        in_specs=placed,
        out_specs=(P("sec", None, "gy", "gz"), P("sec", None, "gy", "gz"), P()),
        check_vma=False,
    )
```
